32 devices in a mesh: pulse: 8 (over z, x), rng: 4 (over y, core).
Axes of the slice: x: 2, y: 2, z: 4, core: 2. Of those that a mesh axis runs over, the one named last changes fastest.
Arguments:
- echoes: float32 [2, 192, 32768], P(None, 'pulse', 'rng'), may hold values from -6 to 6
- row_list: int32 [192], replicated, may hold values from 0 to 191, as said below
- wavenumber: float32 [4, 8192], P(None, ('pulse', 'rng')), may hold values from 1 to 1.5
- az_wavenumber: float32 [192], replicated, may hold values from -0.6 to 0.6
- stolt_offset: int32 [4, 8192], P(None, ('pulse', 'rng')), may hold values from -6 to 32765, as said below
- stolt_coef: float32 [8, 4, 8192], P(None, None, ('pulse', 'rng')), may hold values from -2 to 2
Outputs:
- image: float32 [2, 4, 8192, 192], P(None, None, ('pulse', 'rng'))
The draws below stay inside these ranges and needn't reach their ends.
Inputs may be any that keep to these rules, and one draw needn't show every extreme that they name: row_list[j] - j lies in -8 .. 8, and both ends are taken. stolt_offset[s, q] - (s * 8192 + q) lies in -6 .. -2, and both ends are taken.
All inputs are finite; a program needn't handle non-finite values.
Results may differ from the reference program's by a relative error of at most 0.00007.
Values sent between devices are 32-bit elements; how exact they have to be, the bound alone decides.
No kernel may reach another device: no remote copies, remote signals or barrier semaphores. Data moves between devices by JAX's collectives and lax.ppermute only.
A program may use at most 64 MiB of HBM per device.

```python
import math
import jax
import jax.numpy as jnp
from jax import lax

NR = 32768
LANES = 4
TAPS = 8
W = 8
NP = 192
SPAN = 8192


def draw_row_list(key, part):
    row_index = jnp.arange(NP, dtype=jnp.int32)
    offset_draw = jax.random.randint(key, (NP,), -W, W + 1, dtype=jnp.int32)
    offset_draw = offset_draw.at[NP // 2].set(-W).at[NP // 2 + 1].set(W)
    offset_draw = offset_draw.at[0].set(-W).at[NP - 1].set(W)
    return jnp.clip(row_index + offset_draw, 0, NP - 1).astype(jnp.int32)


def draw_stolt_offset(key, part):
    bin_index = jnp.arange(NR, dtype=jnp.int32)
    offset_draw = jax.random.randint(key, (NR,), -6, -1, dtype=jnp.int32)
    offset_draw = offset_draw.at[0].set(-6).at[NR - 1].set(-2)
    return (bin_index + offset_draw).reshape(LANES, SPAN).astype(jnp.int32)


def shard_levels(key, dims, cuts, least, top_value):
    loudness, own = 1.0, jax.random.fold_in(key, 6)
    for position, parts in cuts:
        draws = jnp.exp(jax.random.uniform(jax.random.fold_in(own, position), (parts,), jnp.float32, least / len(cuts), top_value / len(cuts)))
        loudness = loudness * jnp.repeat(draws, dims[position] // parts).reshape([-1 if axis == position else 1 for axis in range(len(dims))])
    return loudness


def bell_draw(key, extent, spread, most, shards=(), kind=jnp.bfloat16):
    entries = jax.random.normal(key, extent, jnp.float32) * spread
    if len(shards) > 0:
        entries = shard_levels(key, extent, shards, -0.22, 0.18) * entries
    return jnp.clip(entries, min=-most, max=most).astype(kind)


def setup_inputs(seed: int = 0) -> dict:
    key_of = jax.random.split(jax.random.key(seed), 7)
    return {
        "echoes": bell_draw(key_of[0], (2, NP, NR), 1.0, 6.0, ((1, 8), (2, 4)), jnp.float32),
        "row_list": draw_row_list(jax.random.fold_in(key_of[6], 71), 0),
        "wavenumber": jnp.clip(1.0 + 0.5 * jax.random.uniform(key_of[2], (LANES, SPAN), jnp.float32) ** shard_levels(key_of[2], (LANES, SPAN), ((1, 32),), -0.2, 0.2), 1.0, 1.5),
        "az_wavenumber": jnp.clip(jax.random.uniform(key_of[3], (NP,), jnp.float32, -0.6, 0.6), -0.6, 0.6),
        "stolt_offset": draw_stolt_offset(jax.random.fold_in(key_of[6], 71), 0),
        "stolt_coef": bell_draw(key_of[5], (TAPS, LANES, SPAN), 0.35, 2.0, ((2, 32),), jnp.float32),
    }


phase_scale = 24.0

def reference(echoes, row_list, wavenumber, az_wavenumber, stolt_offset, stolt_coef):
    chosen = jnp.take(echoes, row_list, axis=1)
    samples = chosen.reshape(2, NP, LANES, SPAN).transpose(0, 1, 3, 2).reshape(2, NP, NR)
    spectrum = lax.complex(samples[0], samples[1])
    spectrum = jnp.fft.fft(spectrum, axis=1) / math.sqrt(NR)
    spectrum = jnp.fft.fft(spectrum, axis=0) / math.sqrt(NP)
    spectrum = spectrum.T
    wave_flat = wavenumber.reshape(NR)
    phase_angle = phase_scale * jnp.sqrt(wave_flat[:, None] ** 2 - az_wavenumber[None, :] ** 2)
    spectrum = spectrum * lax.complex(jnp.cos(phase_angle), jnp.sin(phase_angle))
    real_part = jnp.real(spectrum)
    imag_part = jnp.imag(spectrum)
    offsets = stolt_offset.reshape(NR)
    weights = stolt_coef.reshape(TAPS, NR)
    total_real = jnp.zeros_like(real_part)
    total_imag = jnp.zeros_like(imag_part)
    for tap_index in range(TAPS):
        source = offsets + tap_index
        inside = (source >= 0) & (source < NR)
        tap_weight = jnp.where(inside, weights[tap_index], 0.0)[:, None]
        clipped = jnp.clip(source, 0, NR - 1).astype(jnp.int32)
        total_real = total_real + tap_weight * jnp.take(real_part, clipped, axis=0)
        total_imag = total_imag + tap_weight * jnp.take(imag_part, clipped, axis=0)
    return jnp.stack([total_real, total_imag]).reshape(2, LANES, SPAN, NP)
```

```python
import math

import jax
import jax.numpy as jnp
from jax import lax
from jax.sharding import PartitionSpec as P

phase_scale = 24.0
highest = lax.Precision.HIGHEST
RIM = 6


def split_factor(length):
    outer_len = 1
    while length % (outer_len * 2) == 0 and outer_len * 2 * (outer_len * 2) <= length:
        outer_len = outer_len * 2
    return outer_len


def dft_table(length, factor):
    index_range = jnp.arange(length, dtype=jnp.int32)
    product = index_range[:, None] * index_range[None, :] % length
    twist_angle = product.astype(jnp.float32) * (-2.0 * math.pi / length)
    return (jnp.cos(twist_angle) * factor, jnp.sin(twist_angle) * factor)


def complex_einsum(pattern, real_part, imag_part, table_real, table_imag):

    def contract(operand, matrix):
        return jnp.einsum(pattern, operand, matrix, precision=highest)

    return (
        contract(real_part, table_real) - contract(imag_part, table_imag),
        contract(real_part, table_imag) + contract(imag_part, table_real),
    )


def last_axis_dft(real_part, imag_part, length, factor):
    inner_len = split_factor(length)
    outer_len = length // inner_len
    leading = real_part.shape[:-1]
    real_part = real_part.reshape(leading + (outer_len, inner_len))
    imag_part = imag_part.reshape(leading + (outer_len, inner_len))
    outer_real, outer_imag = dft_table(outer_len, 1.0)
    real_part, imag_part = complex_einsum(
        "...ba,ub->...ua", real_part, imag_part, outer_real, outer_imag
    )
    col_index = jnp.arange(outer_len, dtype=jnp.int32)[:, None]
    row_index = jnp.arange(inner_len, dtype=jnp.int32)[None, :]
    twist_angle = (col_index * row_index % length).astype(jnp.float32) * (-2.0 * math.pi / length)
    twist_real = jnp.cos(twist_angle)
    twist_imag = jnp.sin(twist_angle)
    real_part, imag_part = (
        real_part * twist_real - imag_part * twist_imag,
        real_part * twist_imag + imag_part * twist_real,
    )
    inner_real, inner_imag = dft_table(inner_len, factor)
    real_part, imag_part = complex_einsum(
        "...ua,va->...vu", real_part, imag_part, inner_real, inner_imag
    )
    return (real_part.reshape(leading + (length,)), imag_part.reshape(leading + (length,)))


def azimuth_matrix(row_list, scale):
    total_rows = row_list.shape[0]
    pulse_index = jnp.arange(total_rows, dtype=jnp.int32)
    select = (row_list[:, None] == pulse_index[None, :]).astype(jnp.float32)
    dft_real, dft_imag = dft_table(total_rows, scale)
    fold_real = jnp.einsum("ji,ja->ai", select, dft_real, precision=highest)
    fold_imag = jnp.einsum("ji,ja->ai", select, dft_imag, precision=highest)
    top = jnp.concatenate([fold_real, -fold_imag], axis=1)
    bottom = jnp.concatenate([fold_imag, fold_real], axis=1)
    return jnp.concatenate([top, bottom], axis=0)


def on_device(echoes, row_list, wavenumber, az_wavenumber, stolt_offset, stolt_coef):
    rows_here = echoes.shape[1]
    span_len = echoes.shape[2]
    lane_count = lax.axis_size("rng")
    pulse_count = lax.axis_size("pulse")
    device_count = pulse_count * lane_count
    total_rows = row_list.shape[0]
    range_len = span_len * lane_count
    block_len = span_len // device_count
    position = lax.axis_index(("pulse", "rng"))

    real_part, imag_part = last_axis_dft(echoes[0], echoes[1], span_len, 1.0)
    spectrum = jnp.stack([real_part, imag_part])
    spectrum = spectrum.reshape(2, rows_here, device_count, block_len)
    spectrum = jnp.transpose(spectrum, (2, 0, 1, 3))
    spectrum = lax.all_to_all(
        spectrum, ("pulse", "rng"), split_axis=0, concat_axis=0, tiled=True
    )
    spectrum = spectrum.reshape(pulse_count, lane_count, 2, rows_here, block_len)

    q_global = position * block_len + jnp.arange(block_len, dtype=jnp.int32)
    bin_index = jnp.arange(lane_count, dtype=jnp.int32)[:, None] * span_len + q_global[None, :]
    lane_index = jnp.arange(lane_count, dtype=jnp.int32)
    turn = (lane_index[:, None, None] * bin_index[None, :, :]) % range_len
    turn_angle = turn.astype(jnp.float32) * (-2.0 * math.pi / range_len)
    turn_real = jnp.cos(turn_angle)
    turn_imag = jnp.sin(turn_angle)
    lane_real = spectrum[:, :, 0]
    lane_imag = spectrum[:, :, 1]
    combined_real = []
    combined_imag = []
    for s in range(lane_count):
        acc_real = 0.0
        acc_imag = 0.0
        for r in range(lane_count):
            wr = turn_real[r, s][None, None, :]
            wi = turn_imag[r, s][None, None, :]
            acc_real = acc_real + lane_real[:, r] * wr - lane_imag[:, r] * wi
            acc_imag = acc_imag + lane_real[:, r] * wi + lane_imag[:, r] * wr
        combined_real.append(acc_real)
        combined_imag.append(acc_imag)
    combined = jnp.stack([jnp.stack(combined_real), jnp.stack(combined_imag)], axis=1)
    combined = combined.reshape(lane_count, 2 * total_rows, block_len)

    fold = azimuth_matrix(row_list, 1.0 / math.sqrt(range_len * total_rows))
    azimuth = jnp.einsum("xy,syq->sxq", fold, combined, precision=highest)
    azimuth = azimuth.reshape(lane_count, 2, total_rows, block_len)

    phase_angle = phase_scale * jnp.sqrt(
        wavenumber[:, None, :] ** 2 - az_wavenumber[None, :, None] ** 2
    )
    phase_real = jnp.cos(phase_angle)
    phase_imag = jnp.sin(phase_angle)
    az_real = azimuth[:, 0]
    az_imag = azimuth[:, 1]
    focused = jnp.stack(
        [
            az_real * phase_real - az_imag * phase_imag,
            az_real * phase_imag + az_imag * phase_real,
        ],
        axis=1,
    )

    axes = ("pulse", "rng")
    up = [(i, (i + 1) % device_count) for i in range(device_count)]
    down = [(j, i) for i, j in up]
    right_edge = jnp.swapaxes(focused[..., block_len - RIM:], 2, 3)
    left_edge = jnp.swapaxes(focused[..., :RIM], 2, 3)
    left_rim = lax.ppermute(right_edge, axes, up)
    right_rim = lax.ppermute(left_edge, axes, down)
    left_rim = jnp.where(position == 0, jnp.roll(left_rim, 1, axis=0), left_rim)
    right_rim = jnp.where(
        position == device_count - 1, jnp.roll(right_rim, -1, axis=0), right_rim
    )

    tap_count = stolt_coef.shape[0]
    piece_index = jnp.arange(block_len, dtype=jnp.int32)
    relative = stolt_offset - bin_index + RIM
    tap_index = jnp.arange(tap_count, dtype=jnp.int32)
    source = stolt_offset[None, :, :] + tap_index[:, None, None]
    inside = (source >= 0) & (source < range_len)
    weights = jnp.where(inside, stolt_coef, 0.0)
    columns = jnp.arange(block_len + 2 * RIM, dtype=jnp.int32)
    target = piece_index[:, None] + relative[:, :, None]
    band = jnp.zeros((lane_count, block_len, block_len + 2 * RIM), jnp.float32)
    for t in range(tap_count):
        band = band + jnp.where(columns[None, None, :] == target + t, weights[t][:, :, None], 0.0)
    band_left = band[:, :, :RIM]
    band_main = band[:, :, RIM:RIM + block_len]
    band_right = band[:, :, RIM + block_len:]

    image = jnp.einsum("sij,scaj->csia", band_main, focused, precision=highest)
    image = image + jnp.einsum("sij,scja->csia", band_left, left_rim, precision=highest)
    image = image + jnp.einsum("sij,scja->csia", band_right, right_rim, precision=highest)
    return image


def solution(mesh):
    in_specs = (
        P(None, "pulse", "rng"),
        P(),
        P(None, ("pulse", "rng")),
        P(),
        P(None, ("pulse", "rng")),
        P(None, None, ("pulse", "rng")),
    )
    out_specs = P(None, None, ("pulse", "rng"), None)
    return jax.shard_map(
        on_device, mesh=mesh, in_specs=in_specs, out_specs=out_specs, check_vma=False
    )
```

```python
import math

import jax
import jax.numpy as jnp
from jax import lax
from jax.sharding import PartitionSpec as P

phase_scale = 24.0
highest = lax.Precision.HIGHEST
RIM = 6


def split_factor(length):
    outer_len = 1
    while length % (outer_len * 2) == 0 and outer_len * 2 * (outer_len * 2) <= length:
        outer_len = outer_len * 2
    return outer_len


def dft_table(length, factor):
    index_range = jnp.arange(length, dtype=jnp.int32)
    product = index_range[:, None] * index_range[None, :] % length
    twist_angle = product.astype(jnp.float32) * (-2.0 * math.pi / length)
    return (jnp.cos(twist_angle) * factor, jnp.sin(twist_angle) * factor)


def complex_einsum(pattern, real_part, imag_part, table_real, table_imag):

    def contract(operand, matrix):
        return jnp.einsum(pattern, operand, matrix, precision=highest)

    return (
        contract(real_part, table_real) - contract(imag_part, table_imag),
        contract(real_part, table_imag) + contract(imag_part, table_real),
    )


def last_axis_dft(real_part, imag_part, length, factor):
    inner_len = split_factor(length)
    outer_len = length // inner_len
    leading = real_part.shape[:-1]
    real_part = real_part.reshape(leading + (outer_len, inner_len))
    imag_part = imag_part.reshape(leading + (outer_len, inner_len))
    outer_real, outer_imag = dft_table(outer_len, 1.0)
    real_part, imag_part = complex_einsum(
        "...ba,ub->...ua", real_part, imag_part, outer_real, outer_imag
    )
    col_index = jnp.arange(outer_len, dtype=jnp.int32)[:, None]
    row_index = jnp.arange(inner_len, dtype=jnp.int32)[None, :]
    twist_angle = (col_index * row_index % length).astype(jnp.float32) * (-2.0 * math.pi / length)
    twist_real = jnp.cos(twist_angle)
    twist_imag = jnp.sin(twist_angle)
    real_part, imag_part = (
        real_part * twist_real - imag_part * twist_imag,
        real_part * twist_imag + imag_part * twist_real,
    )
    inner_real, inner_imag = dft_table(inner_len, factor)
    real_part, imag_part = complex_einsum(
        "...ua,va->...vu", real_part, imag_part, inner_real, inner_imag
    )
    return (real_part.reshape(leading + (length,)), imag_part.reshape(leading + (length,)))


def azimuth_matrix(row_list, scale):
    total_rows = row_list.shape[0]
    pulse_index = jnp.arange(total_rows, dtype=jnp.int32)
    select = (row_list[:, None] == pulse_index[None, :]).astype(jnp.float32)
    dft_real, dft_imag = dft_table(total_rows, scale)
    fold_real = jnp.einsum("ji,ja->ai", select, dft_real, precision=highest)
    fold_imag = jnp.einsum("ji,ja->ai", select, dft_imag, precision=highest)
    top = jnp.concatenate([fold_real, -fold_imag], axis=1)
    bottom = jnp.concatenate([fold_imag, fold_real], axis=1)
    return jnp.concatenate([top, bottom], axis=0)


def on_device(echoes, row_list, wavenumber, az_wavenumber, stolt_offset, stolt_coef):
    rows_here = echoes.shape[1]
    span_len = echoes.shape[2]
    lane_count = lax.axis_size("rng")
    pulse_count = lax.axis_size("pulse")
    device_count = pulse_count * lane_count
    total_rows = row_list.shape[0]
    range_len = span_len * lane_count
    block_len = span_len // device_count
    position = lax.axis_index(("pulse", "rng"))

    small_fold = total_rows <= 512
    chunk_rows = 8 if rows_here % 8 == 0 and small_fold else rows_here
    chunk_count = rows_here // chunk_rows

    q_global = position * block_len + jnp.arange(block_len, dtype=jnp.int32)
    bin_index = jnp.arange(lane_count, dtype=jnp.int32)[:, None] * span_len + q_global[None, :]
    lane_index = jnp.arange(lane_count, dtype=jnp.int32)
    turn = (lane_index[:, None, None] * bin_index[None, :, :]) % range_len
    turn_angle = turn.astype(jnp.float32) * (-2.0 * math.pi / range_len)
    turn_real = jnp.cos(turn_angle)
    turn_imag = jnp.sin(turn_angle)

    fold = azimuth_matrix(row_list, 1.0 / math.sqrt(range_len * total_rows))
    fold = fold.reshape(2 * total_rows, 2, pulse_count, chunk_count, chunk_rows)

    azimuth = None
    for chunk in range(chunk_count):
        rows = slice(chunk * chunk_rows, (chunk + 1) * chunk_rows)
        real_part, imag_part = last_axis_dft(echoes[0, rows], echoes[1, rows], span_len, 1.0)
        spectrum = jnp.stack([real_part, imag_part])
        spectrum = spectrum.reshape(2, chunk_rows, device_count, block_len)
        spectrum = jnp.transpose(spectrum, (2, 0, 1, 3))
        spectrum = lax.all_to_all(
            spectrum, ("pulse", "rng"), split_axis=0, concat_axis=0, tiled=True
        )
        spectrum = spectrum.reshape(pulse_count, lane_count, 2, chunk_rows, block_len)
        lane_real = spectrum[:, :, 0]
        lane_imag = spectrum[:, :, 1]
        combined_real = []
        combined_imag = []
        for s in range(lane_count):
            acc_real = 0.0
            acc_imag = 0.0
            for r in range(lane_count):
                wr = turn_real[r, s][None, None, :]
                wi = turn_imag[r, s][None, None, :]
                acc_real = acc_real + lane_real[:, r] * wr - lane_imag[:, r] * wi
                acc_imag = acc_imag + lane_real[:, r] * wi + lane_imag[:, r] * wr
            combined_real.append(acc_real)
            combined_imag.append(acc_imag)
        combined = jnp.stack([jnp.stack(combined_real), jnp.stack(combined_imag)], axis=1)
        combined = combined.reshape(lane_count, 2 * pulse_count * chunk_rows, block_len)
        part_fold = fold[:, :, :, chunk].reshape(2 * total_rows, 2 * pulse_count * chunk_rows)
        part = jnp.einsum("xy,syq->sxq", part_fold, combined, precision=highest)
        azimuth = part if azimuth is None else azimuth + part
    azimuth = azimuth.reshape(lane_count, 2, total_rows, block_len)

    phase_angle = phase_scale * jnp.sqrt(
        wavenumber[:, None, :] ** 2 - az_wavenumber[None, :, None] ** 2
    )
    phase_real, phase_imag = lax.optimization_barrier(
        (jnp.cos(phase_angle), jnp.sin(phase_angle))
    )
    az_real = azimuth[:, 0]
    az_imag = azimuth[:, 1]
    focused = jnp.stack(
        [
            az_real * phase_real - az_imag * phase_imag,
            az_real * phase_imag + az_imag * phase_real,
        ],
        axis=1,
    )

    axes = ("pulse", "rng")
    up = [(i, (i + 1) % device_count) for i in range(device_count)]
    down = [(j, i) for i, j in up]
    right_edge = jnp.swapaxes(focused[..., block_len - RIM:], 2, 3)
    left_edge = jnp.swapaxes(focused[..., :RIM], 2, 3)
    left_rim = lax.ppermute(right_edge, axes, up)
    right_rim = lax.ppermute(left_edge, axes, down)
    left_rim = jnp.where(position == 0, jnp.roll(left_rim, 1, axis=0), left_rim)
    right_rim = jnp.where(
        position == device_count - 1, jnp.roll(right_rim, -1, axis=0), right_rim
    )

    tap_count = stolt_coef.shape[0]
    piece_index = jnp.arange(block_len, dtype=jnp.int32)
    relative = stolt_offset - bin_index + RIM
    tap_index = jnp.arange(tap_count, dtype=jnp.int32)
    source = stolt_offset[None, :, :] + tap_index[:, None, None]
    inside = (source >= 0) & (source < range_len)
    weights = jnp.where(inside, stolt_coef, 0.0)
    columns = jnp.arange(block_len + 2 * RIM, dtype=jnp.int32)
    target = piece_index[:, None] + relative[:, :, None]
    band = jnp.zeros((lane_count, block_len, block_len + 2 * RIM), jnp.float32)
    for t in range(tap_count):
        band = band + jnp.where(columns[None, None, :] == target + t, weights[t][:, :, None], 0.0)
    band_left = band[:, :, :RIM]
    band_main = band[:, :, RIM:RIM + block_len]
    band_right = band[:, :, RIM + block_len:]

    image = jnp.einsum("sij,scaj->csia", band_main, focused, precision=highest)
    image = image + jnp.einsum("sij,scja->csia", band_left, left_rim, precision=highest)
    image = image + jnp.einsum("sij,scja->csia", band_right, right_rim, precision=highest)
    return image


def solution(mesh):
    in_specs = (
        P(None, "pulse", "rng"),
        P(),
        P(None, ("pulse", "rng")),
        P(),
        P(None, ("pulse", "rng")),
        P(None, None, ("pulse", "rng")),
    )
    out_specs = P(None, None, ("pulse", "rng"), None)
    return jax.shard_map(
        on_device, mesh=mesh, in_specs=in_specs, out_specs=out_specs, check_vma=False
    )
```

```python
import math

import jax
import jax.numpy as jnp
from jax import lax
from jax.sharding import PartitionSpec as P

phase_scale = 24.0
highest = lax.Precision.HIGHEST
RIM = 8


def split_factor(length):
    outer_len = 1
    while length % (outer_len * 2) == 0 and outer_len * 2 * (outer_len * 2) <= length:
        outer_len = outer_len * 2
    return outer_len


def dft_table(length, factor):
    index_range = jnp.arange(length, dtype=jnp.int32)
    product = index_range[:, None] * index_range[None, :] % length
    twist_angle = product.astype(jnp.float32) * (-2.0 * math.pi / length)
    return (jnp.cos(twist_angle) * factor, jnp.sin(twist_angle) * factor)


def complex_einsum(pattern, real_part, imag_part, table_real, table_imag):

    def contract(operand, matrix):
        return jnp.einsum(pattern, operand, matrix, precision=highest)

    return (
        contract(real_part, table_real) - contract(imag_part, table_imag),
        contract(real_part, table_imag) + contract(imag_part, table_real),
    )


def last_axis_dft(real_part, imag_part, length, factor):
    inner_len = split_factor(length)
    outer_len = length // inner_len
    leading = real_part.shape[:-1]
    real_part = real_part.reshape(leading + (outer_len, inner_len))
    imag_part = imag_part.reshape(leading + (outer_len, inner_len))
    outer_real, outer_imag = dft_table(outer_len, 1.0)
    real_part, imag_part = complex_einsum(
        "...ba,ub->...ua", real_part, imag_part, outer_real, outer_imag
    )
    col_index = jnp.arange(outer_len, dtype=jnp.int32)[:, None]
    row_index = jnp.arange(inner_len, dtype=jnp.int32)[None, :]
    twist_angle = (col_index * row_index % length).astype(jnp.float32) * (-2.0 * math.pi / length)
    twist_real = jnp.cos(twist_angle)
    twist_imag = jnp.sin(twist_angle)
    real_part, imag_part = (
        real_part * twist_real - imag_part * twist_imag,
        real_part * twist_imag + imag_part * twist_real,
    )
    inner_real, inner_imag = dft_table(inner_len, factor)
    real_part, imag_part = complex_einsum(
        "...ua,va->...vu", real_part, imag_part, inner_real, inner_imag
    )
    return (real_part.reshape(leading + (length,)), imag_part.reshape(leading + (length,)))


def azimuth_matrix(row_list, scale):
    total_rows = row_list.shape[0]
    pulse_index = jnp.arange(total_rows, dtype=jnp.int32)
    select = (row_list[:, None] == pulse_index[None, :]).astype(jnp.float32)
    dft_real, dft_imag = dft_table(total_rows, scale)
    fold_real = jnp.einsum("ji,ja->ai", select, dft_real, precision=highest)
    fold_imag = jnp.einsum("ji,ja->ai", select, dft_imag, precision=highest)
    top = jnp.concatenate([fold_real, -fold_imag], axis=1)
    bottom = jnp.concatenate([fold_imag, fold_real], axis=1)
    return jnp.concatenate([top, bottom], axis=0)


def on_device(echoes, row_list, wavenumber, az_wavenumber, stolt_offset, stolt_coef):
    rows_here = echoes.shape[1]
    span_len = echoes.shape[2]
    lane_count = lax.axis_size("rng")
    pulse_count = lax.axis_size("pulse")
    device_count = pulse_count * lane_count
    total_rows = row_list.shape[0]
    range_len = span_len * lane_count
    block_len = span_len // device_count
    position = lax.axis_index(("pulse", "rng"))
    lane_pos = lax.axis_index("rng")

    real_part, imag_part = last_axis_dft(echoes[0], echoes[1], span_len, 1.0)
    q_index = jnp.arange(span_len, dtype=jnp.int32)
    twist_angle = ((lane_pos * q_index) % range_len).astype(jnp.float32) * (
        -2.0 * math.pi / range_len
    )
    twist_real = jnp.cos(twist_angle)[None, :]
    twist_imag = jnp.sin(twist_angle)[None, :]
    spectrum = jnp.stack(
        [
            real_part * twist_real - imag_part * twist_imag,
            real_part * twist_imag + imag_part * twist_real,
        ]
    )
    spectrum = spectrum.reshape(2, rows_here, device_count, block_len)
    spectrum = jnp.transpose(spectrum, (2, 0, 1, 3))
    spectrum = lax.all_to_all(
        spectrum, ("pulse", "rng"), split_axis=0, concat_axis=0, tiled=True
    )
    spectrum = spectrum.reshape(pulse_count, lane_count, 2, rows_here, block_len)

    lane_real = spectrum[:, :, 0]
    lane_imag = spectrum[:, :, 1]
    combined_real = []
    combined_imag = []
    for s in range(lane_count):
        acc_real = 0.0
        acc_imag = 0.0
        for r in range(lane_count):
            turn = -2.0 * math.pi * ((r * s) % lane_count) / lane_count
            wr = round(math.cos(turn), 12)
            wi = round(math.sin(turn), 12)
            if wr != 0.0:
                acc_real = acc_real + wr * lane_real[:, r]
                acc_imag = acc_imag + wr * lane_imag[:, r]
            if wi != 0.0:
                acc_real = acc_real - wi * lane_imag[:, r]
                acc_imag = acc_imag + wi * lane_real[:, r]
        combined_real.append(acc_real)
        combined_imag.append(acc_imag)
    combined = jnp.stack([jnp.stack(combined_real), jnp.stack(combined_imag)], axis=1)
    combined = combined.reshape(lane_count, 2 * total_rows, block_len)

    fold = azimuth_matrix(row_list, 1.0 / math.sqrt(range_len * total_rows))
    az_real = jnp.einsum("ay,syq->sqa", fold[:total_rows], combined, precision=highest)
    az_imag = jnp.einsum("ay,syq->sqa", fold[total_rows:], combined, precision=highest)

    phase_angle = phase_scale * jnp.sqrt(
        wavenumber[:, :, None] ** 2 - az_wavenumber[None, None, :] ** 2
    )
    phase_real, phase_imag = lax.optimization_barrier(
        (jnp.cos(phase_angle), jnp.sin(phase_angle))
    )
    focused_real = az_real * phase_real - az_imag * phase_imag
    focused_imag = az_real * phase_imag + az_imag * phase_real
    focused = jnp.stack([focused_real, focused_imag])

    axes = ("pulse", "rng")
    up = [(i, (i + 1) % device_count) for i in range(device_count)]
    down = [(j, i) for i, j in up]
    left_rim = lax.ppermute(focused[:, :, block_len - RIM:], axes, up)
    right_rim = lax.ppermute(focused[:, :, :RIM], axes, down)
    left_rim = jnp.where(position == 0, jnp.roll(left_rim, 1, axis=1), left_rim)
    right_rim = jnp.where(
        position == device_count - 1, jnp.roll(right_rim, -1, axis=1), right_rim
    )
    widened = jnp.concatenate([left_rim, focused, right_rim], axis=2)

    tap_count = stolt_coef.shape[0]
    piece_index = jnp.arange(block_len, dtype=jnp.int32)
    q_global = position * block_len + piece_index
    bin_index = jnp.arange(lane_count, dtype=jnp.int32)[:, None] * span_len + q_global[None, :]
    relative = stolt_offset - bin_index + RIM
    tap_index = jnp.arange(tap_count, dtype=jnp.int32)
    source = stolt_offset[None, :, :] + tap_index[:, None, None]
    inside = (source >= 0) & (source < range_len)
    weights = jnp.where(inside, stolt_coef, 0.0)
    columns = jnp.arange(block_len + 2 * RIM, dtype=jnp.int32)
    target = piece_index[:, None] + relative[:, :, None]
    band = jnp.zeros((lane_count, block_len, block_len + 2 * RIM), jnp.float32)
    for t in range(tap_count):
        band = band + jnp.where(columns[None, None, :] == target + t, weights[t][:, :, None], 0.0)

    return jnp.einsum("sij,csja->csia", band, widened, precision=highest)


def solution(mesh):
    in_specs = (
        P(None, "pulse", "rng"),
        P(),
        P(None, ("pulse", "rng")),
        P(),
        P(None, ("pulse", "rng")),
        P(None, None, ("pulse", "rng")),
    )
    out_specs = P(None, None, ("pulse", "rng"), None)
    return jax.shard_map(
        on_device, mesh=mesh, in_specs=in_specs, out_specs=out_specs, check_vma=False
    )
```

```python
import math

import jax
import jax.numpy as jnp
from jax import lax
from jax.sharding import PartitionSpec as P

phase_scale = 24.0
highest = lax.Precision.HIGHEST
RIM = 8


def split_factor(length):
    outer_len = 1
    while length % (outer_len * 2) == 0 and outer_len * 2 * (outer_len * 2) <= length:
        outer_len = outer_len * 2
    return outer_len


def dft_table(length, factor):
    index_range = jnp.arange(length, dtype=jnp.int32)
    product = index_range[:, None] * index_range[None, :] % length
    twist_angle = product.astype(jnp.float32) * (-2.0 * math.pi / length)
    return (jnp.cos(twist_angle) * factor, jnp.sin(twist_angle) * factor)


def complex_einsum(pattern, real_part, imag_part, table_real, table_imag):

    def contract(operand, matrix):
        return jnp.einsum(pattern, operand, matrix, precision=highest)

    return (
        contract(real_part, table_real) - contract(imag_part, table_imag),
        contract(real_part, table_imag) + contract(imag_part, table_real),
    )


def last_axis_dft(real_part, imag_part, length, factor):
    inner_len = split_factor(length)
    outer_len = length // inner_len
    leading = real_part.shape[:-1]
    real_part = real_part.reshape(leading + (outer_len, inner_len))
    imag_part = imag_part.reshape(leading + (outer_len, inner_len))
    outer_real, outer_imag = dft_table(outer_len, 1.0)
    real_part, imag_part = complex_einsum(
        "...ba,ub->...ua", real_part, imag_part, outer_real, outer_imag
    )
    col_index = jnp.arange(outer_len, dtype=jnp.int32)[:, None]
    row_index = jnp.arange(inner_len, dtype=jnp.int32)[None, :]
    twist_angle = (col_index * row_index % length).astype(jnp.float32) * (-2.0 * math.pi / length)
    twist_real = jnp.cos(twist_angle)
    twist_imag = jnp.sin(twist_angle)
    real_part, imag_part = (
        real_part * twist_real - imag_part * twist_imag,
        real_part * twist_imag + imag_part * twist_real,
    )
    inner_real, inner_imag = dft_table(inner_len, factor)
    real_part, imag_part = complex_einsum(
        "...ua,va->...vu", real_part, imag_part, inner_real, inner_imag
    )
    return (real_part.reshape(leading + (length,)), imag_part.reshape(leading + (length,)))


def azimuth_matrix(row_list, scale):
    total_rows = row_list.shape[0]
    pulse_index = jnp.arange(total_rows, dtype=jnp.int32)
    select = (row_list[:, None] == pulse_index[None, :]).astype(jnp.float32)
    dft_real, dft_imag = dft_table(total_rows, scale)
    fold_real = jnp.einsum("ji,ja->ai", select, dft_real, precision=highest)
    fold_imag = jnp.einsum("ji,ja->ai", select, dft_imag, precision=highest)
    top = jnp.concatenate([fold_real, -fold_imag], axis=1)
    bottom = jnp.concatenate([fold_imag, fold_real], axis=1)
    return jnp.concatenate([top, bottom], axis=0)


def on_device(echoes, row_list, wavenumber, az_wavenumber, stolt_offset, stolt_coef):
    rows_here = echoes.shape[1]
    span_len = echoes.shape[2]
    lane_count = lax.axis_size("rng")
    pulse_count = lax.axis_size("pulse")
    device_count = pulse_count * lane_count
    total_rows = row_list.shape[0]
    range_len = span_len * lane_count
    block_len = span_len // device_count
    position = lax.axis_index(("pulse", "rng"))
    lane_pos = lax.axis_index("rng")

    real_part, imag_part = last_axis_dft(echoes[0], echoes[1], span_len, 1.0)
    q_index = jnp.arange(span_len, dtype=jnp.int32)
    twist_angle = ((lane_pos * q_index) % range_len).astype(jnp.float32) * (
        -2.0 * math.pi / range_len
    )
    twist_real = jnp.cos(twist_angle)[None, :]
    twist_imag = jnp.sin(twist_angle)[None, :]
    spectrum = jnp.stack(
        [
            real_part * twist_real - imag_part * twist_imag,
            real_part * twist_imag + imag_part * twist_real,
        ]
    )
    spectrum = spectrum.reshape(2, rows_here, device_count, block_len)
    spectrum = jnp.transpose(spectrum, (2, 0, 1, 3))
    spectrum = lax.all_to_all(
        spectrum, ("pulse", "rng"), split_axis=0, concat_axis=0, tiled=True
    )
    spectrum = spectrum.reshape(pulse_count, lane_count, 2, rows_here, block_len)

    lane_real = spectrum[:, :, 0]
    lane_imag = spectrum[:, :, 1]
    combined_real = []
    combined_imag = []
    for s in range(lane_count):
        acc_real = 0.0
        acc_imag = 0.0
        for r in range(lane_count):
            turn = -2.0 * math.pi * ((r * s) % lane_count) / lane_count
            wr = round(math.cos(turn), 12)
            wi = round(math.sin(turn), 12)
            if wr != 0.0:
                acc_real = acc_real + wr * lane_real[:, r]
                acc_imag = acc_imag + wr * lane_imag[:, r]
            if wi != 0.0:
                acc_real = acc_real - wi * lane_imag[:, r]
                acc_imag = acc_imag + wi * lane_real[:, r]
        combined_real.append(acc_real)
        combined_imag.append(acc_imag)
    combined = jnp.stack([jnp.stack(combined_real), jnp.stack(combined_imag)], axis=1)
    combined = combined.reshape(lane_count, 2 * total_rows, block_len)

    fold = azimuth_matrix(row_list, 1.0 / math.sqrt(range_len * total_rows))
    az_real = jnp.einsum("ay,syq->sqa", fold[:total_rows], combined, precision=highest)
    az_imag = jnp.einsum("ay,syq->sqa", fold[total_rows:], combined, precision=highest)

    phase_angle = phase_scale * jnp.sqrt(
        wavenumber[:, :, None] ** 2 - az_wavenumber[None, None, :] ** 2
    )
    phase_real, phase_imag = lax.optimization_barrier(
        (jnp.cos(phase_angle), jnp.sin(phase_angle))
    )
    focused_real = az_real * phase_real - az_imag * phase_imag
    focused_imag = az_real * phase_imag + az_imag * phase_real
    focused = jnp.stack([focused_real, focused_imag])

    axes = ("pulse", "rng")
    up = [(i, (i + 1) % device_count) for i in range(device_count)]
    down = [(j, i) for i, j in up]
    left_rim = lax.ppermute(focused[:, :, block_len - RIM:], axes, up)
    right_rim = lax.ppermute(focused[:, :, :RIM], axes, down)
    left_rim = jnp.where(position == 0, jnp.roll(left_rim, 1, axis=1), left_rim)
    right_rim = jnp.where(
        position == device_count - 1, jnp.roll(right_rim, -1, axis=1), right_rim
    )

    tap_count = stolt_coef.shape[0]
    piece_index = jnp.arange(block_len, dtype=jnp.int32)
    q_global = position * block_len + piece_index
    bin_index = jnp.arange(lane_count, dtype=jnp.int32)[:, None] * span_len + q_global[None, :]
    relative = stolt_offset - bin_index + RIM
    tap_index = jnp.arange(tap_count, dtype=jnp.int32)
    source = stolt_offset[None, :, :] + tap_index[:, None, None]
    inside = (source >= 0) & (source < range_len)
    weights = jnp.where(inside, stolt_coef, 0.0)
    columns = jnp.arange(block_len + 2 * RIM, dtype=jnp.int32)
    target = piece_index[:, None] + relative[:, :, None]
    band = jnp.zeros((lane_count, block_len, block_len + 2 * RIM), jnp.float32)
    for t in range(tap_count):
        band = band + jnp.where(columns[None, None, :] == target + t, weights[t][:, :, None], 0.0)

    image = jnp.einsum(
        "sij,csja->csia", band[:, :, RIM:RIM + block_len], focused, precision=highest
    )
    left_part = jnp.einsum("sij,csja->csia", band[:, :RIM, :RIM], left_rim, precision=highest)
    right_part = jnp.einsum(
        "sij,csja->csia", band[:, block_len - RIM:, block_len + RIM:], right_rim, precision=highest
    )
    image = lax.dynamic_update_slice_in_dim(image, image[:, :, :RIM] + left_part, 0, axis=2)
    image = lax.dynamic_update_slice_in_dim(
        image, image[:, :, block_len - RIM:] + right_part, block_len - RIM, axis=2
    )
    return image


def solution(mesh):
    in_specs = (
        P(None, "pulse", "rng"),
        P(),
        P(None, ("pulse", "rng")),
        P(),
        P(None, ("pulse", "rng")),
        P(None, None, ("pulse", "rng")),
    )
    out_specs = P(None, None, ("pulse", "rng"), None)
    return jax.shard_map(
        on_device, mesh=mesh, in_specs=in_specs, out_specs=out_specs, check_vma=False
    )
```

```python
import math

import jax
import jax.numpy as jnp
from jax import lax
from jax.sharding import PartitionSpec as P

phase_scale = 24.0
highest = lax.Precision.HIGHEST
RIM = 8


def split_factor(length):
    outer_len = 1
    while length % (outer_len * 2) == 0 and outer_len * 2 * (outer_len * 2) <= length:
        outer_len = outer_len * 2
    return outer_len


def dft_table(length, factor):
    index_range = jnp.arange(length, dtype=jnp.int32)
    product = index_range[:, None] * index_range[None, :] % length
    twist_angle = product.astype(jnp.float32) * (-2.0 * math.pi / length)
    return (jnp.cos(twist_angle) * factor, jnp.sin(twist_angle) * factor)


def complex_einsum(pattern, real_part, imag_part, table_real, table_imag):

    def contract(operand, matrix):
        return jnp.einsum(pattern, operand, matrix, precision=lax.Precision.HIGH)

    return (
        contract(real_part, table_real) - contract(imag_part, table_imag),
        contract(real_part, table_imag) + contract(imag_part, table_real),
    )


def last_axis_dft(real_part, imag_part, length, factor):
    inner_len = split_factor(length)
    outer_len = length // inner_len
    leading = real_part.shape[:-1]
    real_part = real_part.reshape(leading + (outer_len, inner_len))
    imag_part = imag_part.reshape(leading + (outer_len, inner_len))
    outer_real, outer_imag = dft_table(outer_len, 1.0)
    real_part, imag_part = complex_einsum(
        "...ba,ub->...ua", real_part, imag_part, outer_real, outer_imag
    )
    col_index = jnp.arange(outer_len, dtype=jnp.int32)[:, None]
    row_index = jnp.arange(inner_len, dtype=jnp.int32)[None, :]
    twist_angle = (col_index * row_index % length).astype(jnp.float32) * (-2.0 * math.pi / length)
    twist_real = jnp.cos(twist_angle)
    twist_imag = jnp.sin(twist_angle)
    real_part, imag_part = (
        real_part * twist_real - imag_part * twist_imag,
        real_part * twist_imag + imag_part * twist_real,
    )
    inner_real, inner_imag = dft_table(inner_len, factor)
    real_part, imag_part = complex_einsum(
        "...ua,va->...vu", real_part, imag_part, inner_real, inner_imag
    )
    return (real_part.reshape(leading + (length,)), imag_part.reshape(leading + (length,)))


def azimuth_matrix(row_list, scale):
    total_rows = row_list.shape[0]
    pulse_index = jnp.arange(total_rows, dtype=jnp.int32)
    select = (row_list[:, None] == pulse_index[None, :]).astype(jnp.float32)
    dft_real, dft_imag = dft_table(total_rows, scale)
    fold_real = jnp.einsum("ji,ja->ai", select, dft_real, precision=highest)
    fold_imag = jnp.einsum("ji,ja->ai", select, dft_imag, precision=highest)
    top = jnp.concatenate([fold_real, -fold_imag], axis=1)
    bottom = jnp.concatenate([fold_imag, fold_real], axis=1)
    return jnp.concatenate([top, bottom], axis=0)


def on_device(echoes, row_list, wavenumber, az_wavenumber, stolt_offset, stolt_coef):
    rows_here = echoes.shape[1]
    span_len = echoes.shape[2]
    lane_count = lax.axis_size("rng")
    pulse_count = lax.axis_size("pulse")
    device_count = pulse_count * lane_count
    total_rows = row_list.shape[0]
    range_len = span_len * lane_count
    block_len = span_len // device_count
    position = lax.axis_index(("pulse", "rng"))
    lane_pos = lax.axis_index("rng")

    real_part, imag_part = last_axis_dft(echoes[0], echoes[1], span_len, 1.0)
    q_index = jnp.arange(span_len, dtype=jnp.int32)
    twist_angle = ((lane_pos * q_index) % range_len).astype(jnp.float32) * (
        -2.0 * math.pi / range_len
    )
    twist_real = jnp.cos(twist_angle)[None, :]
    twist_imag = jnp.sin(twist_angle)[None, :]
    spectrum = jnp.stack(
        [
            real_part * twist_real - imag_part * twist_imag,
            real_part * twist_imag + imag_part * twist_real,
        ]
    )
    spectrum = spectrum.reshape(2, rows_here, device_count, block_len)
    spectrum = jnp.transpose(spectrum, (2, 0, 1, 3))
    spectrum = lax.all_to_all(
        spectrum, ("pulse", "rng"), split_axis=0, concat_axis=0, tiled=True
    )
    spectrum = spectrum.reshape(pulse_count, lane_count, 2, rows_here, block_len)

    lane_real = spectrum[:, :, 0]
    lane_imag = spectrum[:, :, 1]
    combined_real = []
    combined_imag = []
    for s in range(lane_count):
        acc_real = 0.0
        acc_imag = 0.0
        for r in range(lane_count):
            turn = -2.0 * math.pi * ((r * s) % lane_count) / lane_count
            wr = round(math.cos(turn), 12)
            wi = round(math.sin(turn), 12)
            if wr != 0.0:
                acc_real = acc_real + wr * lane_real[:, r]
                acc_imag = acc_imag + wr * lane_imag[:, r]
            if wi != 0.0:
                acc_real = acc_real - wi * lane_imag[:, r]
                acc_imag = acc_imag + wi * lane_real[:, r]
        combined_real.append(acc_real)
        combined_imag.append(acc_imag)
    combined = jnp.stack([jnp.stack(combined_real), jnp.stack(combined_imag)], axis=1)
    combined = combined.reshape(lane_count, 2 * total_rows, block_len)

    fold = azimuth_matrix(row_list, 1.0 / math.sqrt(range_len * total_rows))
    az_real = jnp.einsum("ay,syq->sqa", fold[:total_rows], combined, precision=highest)
    az_imag = jnp.einsum("ay,syq->sqa", fold[total_rows:], combined, precision=highest)

    phase_angle = phase_scale * jnp.sqrt(
        wavenumber[:, :, None] ** 2 - az_wavenumber[None, None, :] ** 2
    )
    phase_real, phase_imag = lax.optimization_barrier(
        (jnp.cos(phase_angle), jnp.sin(phase_angle))
    )
    focused_real = az_real * phase_real - az_imag * phase_imag
    focused_imag = az_real * phase_imag + az_imag * phase_real
    focused = jnp.stack([focused_real, focused_imag])

    axes = ("pulse", "rng")
    up = [(i, (i + 1) % device_count) for i in range(device_count)]
    down = [(j, i) for i, j in up]
    left_rim = lax.ppermute(focused[:, :, block_len - RIM:], axes, up)
    right_rim = lax.ppermute(focused[:, :, :RIM], axes, down)
    left_rim = jnp.where(position == 0, jnp.roll(left_rim, 1, axis=1), left_rim)
    right_rim = jnp.where(
        position == device_count - 1, jnp.roll(right_rim, -1, axis=1), right_rim
    )
    widened = jnp.concatenate([left_rim, focused, right_rim], axis=2)

    tap_count = stolt_coef.shape[0]
    piece_index = jnp.arange(block_len, dtype=jnp.int32)
    q_global = position * block_len + piece_index
    bin_index = jnp.arange(lane_count, dtype=jnp.int32)[:, None] * span_len + q_global[None, :]
    relative = stolt_offset - bin_index + RIM
    tap_index = jnp.arange(tap_count, dtype=jnp.int32)
    source = stolt_offset[None, :, :] + tap_index[:, None, None]
    inside = (source >= 0) & (source < range_len)
    weights = jnp.where(inside, stolt_coef, 0.0)
    columns = jnp.arange(block_len + 2 * RIM, dtype=jnp.int32)
    target = piece_index[:, None] + relative[:, :, None]
    band = jnp.zeros((lane_count, block_len, block_len + 2 * RIM), jnp.float32)
    for t in range(tap_count):
        band = band + jnp.where(columns[None, None, :] == target + t, weights[t][:, :, None], 0.0)

    return jnp.einsum("sij,csja->csia", band, widened, precision=highest)


def solution(mesh):
    in_specs = (
        P(None, "pulse", "rng"),
        P(),
        P(None, ("pulse", "rng")),
        P(),
        P(None, ("pulse", "rng")),
        P(None, None, ("pulse", "rng")),
    )
    out_specs = P(None, None, ("pulse", "rng"), None)
    return jax.shard_map(
        on_device, mesh=mesh, in_specs=in_specs, out_specs=out_specs, check_vma=False
    )
```

```python
import math

import jax
import jax.numpy as jnp
from jax import lax
from jax.sharding import PartitionSpec as P

phase_scale = 24.0
highest = lax.Precision.HIGHEST
fast = lax.Precision.HIGH
RIM = 8


def split_factor(length):
    outer_len = 1
    while length % (outer_len * 2) == 0 and outer_len * 2 * (outer_len * 2) <= length:
        outer_len = outer_len * 2
    return outer_len


def dft_table(length, factor):
    index_range = jnp.arange(length, dtype=jnp.int32)
    product = index_range[:, None] * index_range[None, :] % length
    twist_angle = product.astype(jnp.float32) * (-2.0 * math.pi / length)
    return (jnp.cos(twist_angle) * factor, jnp.sin(twist_angle) * factor)


def complex_einsum(pattern, real_part, imag_part, table_real, table_imag):

    def contract(operand, matrix):
        return jnp.einsum(pattern, operand, matrix, precision=fast)

    return (
        contract(real_part, table_real) - contract(imag_part, table_imag),
        contract(real_part, table_imag) + contract(imag_part, table_real),
    )


def last_axis_dft(real_part, imag_part, length, factor):
    inner_len = split_factor(length)
    outer_len = length // inner_len
    leading = real_part.shape[:-1]
    real_part = real_part.reshape(leading + (outer_len, inner_len))
    imag_part = imag_part.reshape(leading + (outer_len, inner_len))
    outer_real, outer_imag = dft_table(outer_len, 1.0)
    real_part, imag_part = complex_einsum(
        "...ba,ub->...ua", real_part, imag_part, outer_real, outer_imag
    )
    col_index = jnp.arange(outer_len, dtype=jnp.int32)[:, None]
    row_index = jnp.arange(inner_len, dtype=jnp.int32)[None, :]
    twist_angle = (col_index * row_index % length).astype(jnp.float32) * (-2.0 * math.pi / length)
    twist_real = jnp.cos(twist_angle)
    twist_imag = jnp.sin(twist_angle)
    real_part, imag_part = (
        real_part * twist_real - imag_part * twist_imag,
        real_part * twist_imag + imag_part * twist_real,
    )
    inner_real, inner_imag = dft_table(inner_len, factor)
    real_part, imag_part = complex_einsum(
        "...ua,va->...vu", real_part, imag_part, inner_real, inner_imag
    )
    return (real_part.reshape(leading + (length,)), imag_part.reshape(leading + (length,)))


def azimuth_matrix(row_list, scale):
    total_rows = row_list.shape[0]
    pulse_index = jnp.arange(total_rows, dtype=jnp.int32)
    select = (row_list[:, None] == pulse_index[None, :]).astype(jnp.float32)
    dft_real, dft_imag = dft_table(total_rows, scale)
    fold_real = jnp.einsum("ji,ja->ai", select, dft_real, precision=highest)
    fold_imag = jnp.einsum("ji,ja->ai", select, dft_imag, precision=highest)
    top = jnp.concatenate([fold_real, -fold_imag], axis=1)
    bottom = jnp.concatenate([fold_imag, fold_real], axis=1)
    return jnp.concatenate([top, bottom], axis=0)


def on_device(echoes, row_list, wavenumber, az_wavenumber, stolt_offset, stolt_coef):
    rows_here = echoes.shape[1]
    span_len = echoes.shape[2]
    lane_count = lax.axis_size("rng")
    pulse_count = lax.axis_size("pulse")
    device_count = pulse_count * lane_count
    total_rows = row_list.shape[0]
    range_len = span_len * lane_count
    block_len = span_len // device_count
    position = lax.axis_index(("pulse", "rng"))
    lane_pos = lax.axis_index("rng")

    real_part, imag_part = last_axis_dft(echoes[0], echoes[1], span_len, 1.0)
    q_index = jnp.arange(span_len, dtype=jnp.int32)
    twist_angle = ((lane_pos * q_index) % range_len).astype(jnp.float32) * (
        -2.0 * math.pi / range_len
    )
    twist_real = jnp.cos(twist_angle)[None, :]
    twist_imag = jnp.sin(twist_angle)[None, :]
    spectrum = jnp.stack(
        [
            real_part * twist_real - imag_part * twist_imag,
            real_part * twist_imag + imag_part * twist_real,
        ]
    )
    spectrum = spectrum.reshape(2, rows_here, device_count, block_len)
    spectrum = jnp.transpose(spectrum, (2, 0, 1, 3))
    spectrum = lax.all_to_all(
        spectrum, ("pulse", "rng"), split_axis=0, concat_axis=0, tiled=True
    )
    spectrum = spectrum.reshape(pulse_count, lane_count, 2, rows_here, block_len)

    lane_real = spectrum[:, :, 0]
    lane_imag = spectrum[:, :, 1]
    combined_real = []
    combined_imag = []
    for s in range(lane_count):
        acc_real = 0.0
        acc_imag = 0.0
        for r in range(lane_count):
            turn = -2.0 * math.pi * ((r * s) % lane_count) / lane_count
            wr = round(math.cos(turn), 12)
            wi = round(math.sin(turn), 12)
            if wr != 0.0:
                acc_real = acc_real + wr * lane_real[:, r]
                acc_imag = acc_imag + wr * lane_imag[:, r]
            if wi != 0.0:
                acc_real = acc_real - wi * lane_imag[:, r]
                acc_imag = acc_imag + wi * lane_real[:, r]
        combined_real.append(acc_real)
        combined_imag.append(acc_imag)
    combined = jnp.stack([jnp.stack(combined_real), jnp.stack(combined_imag)], axis=1)
    combined = combined.reshape(lane_count, 2 * total_rows, block_len)

    fold = azimuth_matrix(row_list, 1.0 / math.sqrt(range_len * total_rows))
    az_real = jnp.einsum("ay,syq->sqa", fold[:total_rows], combined, precision=fast)
    az_imag = jnp.einsum("ay,syq->sqa", fold[total_rows:], combined, precision=fast)

    phase_angle = phase_scale * jnp.sqrt(
        wavenumber[:, :, None] ** 2 - az_wavenumber[None, None, :] ** 2
    )
    phase_real, phase_imag = lax.optimization_barrier(
        (jnp.cos(phase_angle), jnp.sin(phase_angle))
    )
    focused_real = az_real * phase_real - az_imag * phase_imag
    focused_imag = az_real * phase_imag + az_imag * phase_real
    focused = jnp.stack([focused_real, focused_imag])

    axes = ("pulse", "rng")
    up = [(i, (i + 1) % device_count) for i in range(device_count)]
    down = [(j, i) for i, j in up]
    left_rim = lax.ppermute(focused[:, :, block_len - RIM:], axes, up)
    right_rim = lax.ppermute(focused[:, :, :RIM], axes, down)
    left_rim = jnp.where(position == 0, jnp.roll(left_rim, 1, axis=1), left_rim)
    right_rim = jnp.where(
        position == device_count - 1, jnp.roll(right_rim, -1, axis=1), right_rim
    )
    widened = jnp.concatenate([left_rim, focused, right_rim], axis=2)

    tap_count = stolt_coef.shape[0]
    piece_index = jnp.arange(block_len, dtype=jnp.int32)
    q_global = position * block_len + piece_index
    bin_index = jnp.arange(lane_count, dtype=jnp.int32)[:, None] * span_len + q_global[None, :]
    relative = stolt_offset - bin_index + RIM
    tap_index = jnp.arange(tap_count, dtype=jnp.int32)
    source = stolt_offset[None, :, :] + tap_index[:, None, None]
    inside = (source >= 0) & (source < range_len)
    weights = jnp.where(inside, stolt_coef, 0.0)
    columns = jnp.arange(block_len + 2 * RIM, dtype=jnp.int32)
    target = piece_index[:, None] + relative[:, :, None]
    band = jnp.zeros((lane_count, block_len, block_len + 2 * RIM), jnp.float32)
    for t in range(tap_count):
        band = band + jnp.where(columns[None, None, :] == target + t, weights[t][:, :, None], 0.0)

    return jnp.einsum("sij,csja->csia", band, widened, precision=fast)


def solution(mesh):
    in_specs = (
        P(None, "pulse", "rng"),
        P(),
        P(None, ("pulse", "rng")),
        P(),
        P(None, ("pulse", "rng")),
        P(None, None, ("pulse", "rng")),
    )
    out_specs = P(None, None, ("pulse", "rng"), None)
    return jax.shard_map(
        on_device, mesh=mesh, in_specs=in_specs, out_specs=out_specs, check_vma=False
    )
```

```python
import math

import jax
import jax.numpy as jnp
from jax import lax
from jax.sharding import PartitionSpec as P

phase_scale = 24.0
highest = lax.Precision.HIGHEST
fast = lax.Precision.HIGH
RIM = 8


def split_factor(length):
    outer_len = 1
    while length % (outer_len * 2) == 0 and outer_len * 2 * (outer_len * 2) <= length:
        outer_len = outer_len * 2
    return outer_len


def dft_table(length, factor):
    index_range = jnp.arange(length, dtype=jnp.int32)
    product = index_range[:, None] * index_range[None, :] % length
    twist_angle = product.astype(jnp.float32) * (-2.0 * math.pi / length)
    return (jnp.cos(twist_angle) * factor, jnp.sin(twist_angle) * factor)


def complex_einsum(pattern, real_part, imag_part, table_real, table_imag):

    def contract(operand, matrix):
        return jnp.einsum(pattern, operand, matrix, precision=fast)

    return (
        contract(real_part, table_real) - contract(imag_part, table_imag),
        contract(real_part, table_imag) + contract(imag_part, table_real),
    )


def last_axis_dft(real_part, imag_part, length, factor):
    inner_len = split_factor(length)
    outer_len = length // inner_len
    leading = real_part.shape[:-1]
    real_part = real_part.reshape(leading + (outer_len, inner_len))
    imag_part = imag_part.reshape(leading + (outer_len, inner_len))
    outer_real, outer_imag = dft_table(outer_len, 1.0)
    real_part, imag_part = complex_einsum(
        "...ba,ub->...ua", real_part, imag_part, outer_real, outer_imag
    )
    col_index = jnp.arange(outer_len, dtype=jnp.int32)[:, None]
    row_index = jnp.arange(inner_len, dtype=jnp.int32)[None, :]
    twist_angle = (col_index * row_index % length).astype(jnp.float32) * (-2.0 * math.pi / length)
    twist_real = jnp.cos(twist_angle)
    twist_imag = jnp.sin(twist_angle)
    real_part, imag_part = (
        real_part * twist_real - imag_part * twist_imag,
        real_part * twist_imag + imag_part * twist_real,
    )
    inner_real, inner_imag = dft_table(inner_len, factor)
    real_part, imag_part = complex_einsum(
        "...ua,va->...vu", real_part, imag_part, inner_real, inner_imag
    )
    return (real_part.reshape(leading + (length,)), imag_part.reshape(leading + (length,)))


def stacked_table(length, factor):
    table_real, table_imag = dft_table(length, factor)
    top = jnp.stack([table_real, -table_imag], axis=1)
    bottom = jnp.stack([table_imag, table_real], axis=1)
    return jnp.stack([top, bottom])


def range_dft_blocks(pair, device_count, block_len, lane_pos, range_len):
    rows = pair.shape[1]
    length = pair.shape[2]
    inner_len = split_factor(length)
    outer_len = length // inner_len
    signal = pair.reshape(2, rows, outer_len, inner_len)
    first = jnp.einsum("ducb,crba->drua", stacked_table(outer_len, 1.0), signal, precision=fast)
    col_index = jnp.arange(outer_len, dtype=jnp.int32)[:, None]
    row_index = jnp.arange(inner_len, dtype=jnp.int32)[None, :]
    twist_angle = (col_index * row_index % length).astype(jnp.float32) * (-2.0 * math.pi / length)
    twist_real = jnp.cos(twist_angle)
    twist_imag = jnp.sin(twist_angle)
    first = jnp.stack(
        [
            first[0] * twist_real - first[1] * twist_imag,
            first[0] * twist_imag + first[1] * twist_real,
        ]
    )
    second = jnp.einsum("dvca,crua->vdru", stacked_table(inner_len, 1.0), first, precision=fast)
    q_index = jnp.arange(inner_len, dtype=jnp.int32)[:, None] * outer_len + jnp.arange(
        outer_len, dtype=jnp.int32
    )[None, :]
    turn_angle = ((lane_pos * q_index) % range_len).astype(jnp.float32) * (
        -2.0 * math.pi / range_len
    )
    turn_real = jnp.cos(turn_angle)[:, None, :]
    turn_imag = jnp.sin(turn_angle)[:, None, :]
    second = jnp.stack(
        [
            second[:, 0] * turn_real - second[:, 1] * turn_imag,
            second[:, 0] * turn_imag + second[:, 1] * turn_real,
        ],
        axis=1,
    )
    if block_len % outer_len == 0:
        per_block = block_len // outer_len
        second = second.reshape(device_count, per_block, 2, rows, outer_len)
        second = jnp.transpose(second, (0, 2, 3, 1, 4))
        return second.reshape(device_count, 2, rows, block_len)
    second = jnp.transpose(second, (1, 2, 0, 3)).reshape(2, rows, device_count, block_len)
    return jnp.transpose(second, (2, 0, 1, 3))


def azimuth_matrix(row_list, scale):
    total_rows = row_list.shape[0]
    pulse_index = jnp.arange(total_rows, dtype=jnp.int32)
    select = (row_list[:, None] == pulse_index[None, :]).astype(jnp.float32)
    dft_real, dft_imag = dft_table(total_rows, scale)
    fold_real = jnp.einsum("ji,ja->ai", select, dft_real, precision=highest)
    fold_imag = jnp.einsum("ji,ja->ai", select, dft_imag, precision=highest)
    top = jnp.concatenate([fold_real, -fold_imag], axis=1)
    bottom = jnp.concatenate([fold_imag, fold_real], axis=1)
    return jnp.concatenate([top, bottom], axis=0)


def on_device(echoes, row_list, wavenumber, az_wavenumber, stolt_offset, stolt_coef):
    rows_here = echoes.shape[1]
    span_len = echoes.shape[2]
    lane_count = lax.axis_size("rng")
    pulse_count = lax.axis_size("pulse")
    device_count = pulse_count * lane_count
    total_rows = row_list.shape[0]
    range_len = span_len * lane_count
    block_len = span_len // device_count
    position = lax.axis_index(("pulse", "rng"))
    lane_pos = lax.axis_index("rng")

    spectrum = range_dft_blocks(echoes, device_count, block_len, lane_pos, range_len)
    spectrum = lax.all_to_all(
        spectrum, ("pulse", "rng"), split_axis=0, concat_axis=0, tiled=True
    )
    spectrum = spectrum.reshape(pulse_count, lane_count, 2, rows_here, block_len)

    lane_real = spectrum[:, :, 0]
    lane_imag = spectrum[:, :, 1]
    combined_real = []
    combined_imag = []
    for s in range(lane_count):
        acc_real = 0.0
        acc_imag = 0.0
        for r in range(lane_count):
            turn = -2.0 * math.pi * ((r * s) % lane_count) / lane_count
            wr = round(math.cos(turn), 12)
            wi = round(math.sin(turn), 12)
            if wr != 0.0:
                acc_real = acc_real + wr * lane_real[:, r]
                acc_imag = acc_imag + wr * lane_imag[:, r]
            if wi != 0.0:
                acc_real = acc_real - wi * lane_imag[:, r]
                acc_imag = acc_imag + wi * lane_real[:, r]
        combined_real.append(acc_real)
        combined_imag.append(acc_imag)
    combined = jnp.stack([jnp.stack(combined_real), jnp.stack(combined_imag)], axis=1)
    combined = combined.reshape(lane_count, 2 * total_rows, block_len)

    fold = azimuth_matrix(row_list, 1.0 / math.sqrt(range_len * total_rows))
    az_real = jnp.einsum("ay,syq->sqa", fold[:total_rows], combined, precision=fast)
    az_imag = jnp.einsum("ay,syq->sqa", fold[total_rows:], combined, precision=fast)

    phase_angle = phase_scale * jnp.sqrt(
        wavenumber[:, :, None] ** 2 - az_wavenumber[None, None, :] ** 2
    )
    phase_real, phase_imag = lax.optimization_barrier(
        (jnp.cos(phase_angle), jnp.sin(phase_angle))
    )
    focused_real = az_real * phase_real - az_imag * phase_imag
    focused_imag = az_real * phase_imag + az_imag * phase_real
    focused = jnp.stack([focused_real, focused_imag])

    axes = ("pulse", "rng")
    up = [(i, (i + 1) % device_count) for i in range(device_count)]
    down = [(j, i) for i, j in up]
    left_rim = lax.ppermute(focused[:, :, block_len - RIM:], axes, up)
    right_rim = lax.ppermute(focused[:, :, :RIM], axes, down)
    left_rim = jnp.where(position == 0, jnp.roll(left_rim, 1, axis=1), left_rim)
    right_rim = jnp.where(
        position == device_count - 1, jnp.roll(right_rim, -1, axis=1), right_rim
    )
    widened = jnp.concatenate([left_rim, focused, right_rim], axis=2)

    tap_count = stolt_coef.shape[0]
    piece_index = jnp.arange(block_len, dtype=jnp.int32)
    q_global = position * block_len + piece_index
    bin_index = jnp.arange(lane_count, dtype=jnp.int32)[:, None] * span_len + q_global[None, :]
    relative = stolt_offset - bin_index + RIM
    tap_index = jnp.arange(tap_count, dtype=jnp.int32)
    source = stolt_offset[None, :, :] + tap_index[:, None, None]
    inside = (source >= 0) & (source < range_len)
    weights = jnp.where(inside, stolt_coef, 0.0)
    columns = jnp.arange(block_len + 2 * RIM, dtype=jnp.int32)
    target = piece_index[:, None] + relative[:, :, None]
    band = jnp.zeros((lane_count, block_len, block_len + 2 * RIM), jnp.float32)
    for t in range(tap_count):
        band = band + jnp.where(columns[None, None, :] == target + t, weights[t][:, :, None], 0.0)

    return jnp.einsum("sij,csja->csia", band, widened, precision=highest)


def solution(mesh):
    in_specs = (
        P(None, "pulse", "rng"),
        P(),
        P(None, ("pulse", "rng")),
        P(),
        P(None, ("pulse", "rng")),
        P(None, None, ("pulse", "rng")),
    )
    out_specs = P(None, None, ("pulse", "rng"), None)
    return jax.shard_map(
        on_device, mesh=mesh, in_specs=in_specs, out_specs=out_specs, check_vma=False
    )
```

```python
import math

import jax
import jax.numpy as jnp
from jax import lax
from jax.sharding import PartitionSpec as P

phase_scale = 24.0
highest = lax.Precision.HIGHEST
fast = lax.Precision.HIGH
RIM = 8


def split_factor(length):
    outer_len = 1
    while length % (outer_len * 2) == 0 and outer_len * 2 * (outer_len * 2) <= length:
        outer_len = outer_len * 2
    return outer_len


def dft_table(length, factor):
    index_range = jnp.arange(length, dtype=jnp.int32)
    product = index_range[:, None] * index_range[None, :] % length
    twist_angle = product.astype(jnp.float32) * (-2.0 * math.pi / length)
    return (jnp.cos(twist_angle) * factor, jnp.sin(twist_angle) * factor)


def complex_einsum(pattern, real_part, imag_part, table_real, table_imag):

    def contract(operand, matrix):
        return jnp.einsum(pattern, operand, matrix, precision=fast)

    return (
        contract(real_part, table_real) - contract(imag_part, table_imag),
        contract(real_part, table_imag) + contract(imag_part, table_real),
    )


def last_axis_dft(real_part, imag_part, length, factor):
    inner_len = split_factor(length)
    outer_len = length // inner_len
    leading = real_part.shape[:-1]
    real_part = real_part.reshape(leading + (outer_len, inner_len))
    imag_part = imag_part.reshape(leading + (outer_len, inner_len))
    outer_real, outer_imag = dft_table(outer_len, 1.0)
    real_part, imag_part = complex_einsum(
        "...ba,ub->...ua", real_part, imag_part, outer_real, outer_imag
    )
    col_index = jnp.arange(outer_len, dtype=jnp.int32)[:, None]
    row_index = jnp.arange(inner_len, dtype=jnp.int32)[None, :]
    twist_angle = (col_index * row_index % length).astype(jnp.float32) * (-2.0 * math.pi / length)
    twist_real = jnp.cos(twist_angle)
    twist_imag = jnp.sin(twist_angle)
    real_part, imag_part = (
        real_part * twist_real - imag_part * twist_imag,
        real_part * twist_imag + imag_part * twist_real,
    )
    inner_real, inner_imag = dft_table(inner_len, factor)
    real_part, imag_part = complex_einsum(
        "...ua,va->...vu", real_part, imag_part, inner_real, inner_imag
    )
    return (real_part.reshape(leading + (length,)), imag_part.reshape(leading + (length,)))


def stacked_table(length, factor):
    table_real, table_imag = dft_table(length, factor)
    top = jnp.stack([table_real, -table_imag], axis=1)
    bottom = jnp.stack([table_imag, table_real], axis=1)
    return jnp.stack([top, bottom])


def range_dft_blocks(pair, device_count, block_len, lane_pos, range_len):
    rows = pair.shape[1]
    length = pair.shape[2]
    outer_len = split_factor(length)
    inner_len = length // outer_len
    signal = pair.reshape(2, rows, outer_len, inner_len)
    first = jnp.einsum("ducb,crba->drua", stacked_table(outer_len, 1.0), signal, precision=fast)
    col_index = jnp.arange(outer_len, dtype=jnp.int32)[:, None]
    row_index = jnp.arange(inner_len, dtype=jnp.int32)[None, :]
    twist_angle = (col_index * row_index % length).astype(jnp.float32) * (-2.0 * math.pi / length)
    twist_real = jnp.cos(twist_angle)
    twist_imag = jnp.sin(twist_angle)
    first = jnp.stack(
        [
            first[0] * twist_real - first[1] * twist_imag,
            first[0] * twist_imag + first[1] * twist_real,
        ]
    )
    second = jnp.einsum("dvca,crua->vdru", stacked_table(inner_len, 1.0), first, precision=fast)
    q_index = jnp.arange(inner_len, dtype=jnp.int32)[:, None] * outer_len + jnp.arange(
        outer_len, dtype=jnp.int32
    )[None, :]
    turn_angle = ((lane_pos * q_index) % range_len).astype(jnp.float32) * (
        -2.0 * math.pi / range_len
    )
    turn_real = jnp.cos(turn_angle)[:, None, :]
    turn_imag = jnp.sin(turn_angle)[:, None, :]
    second = jnp.stack(
        [
            second[:, 0] * turn_real - second[:, 1] * turn_imag,
            second[:, 0] * turn_imag + second[:, 1] * turn_real,
        ],
        axis=1,
    )
    if block_len % outer_len == 0:
        per_block = block_len // outer_len
        second = second.reshape(device_count, per_block, 2, rows, outer_len)
        second = jnp.transpose(second, (0, 2, 3, 1, 4))
        return second.reshape(device_count, 2, rows, block_len)
    second = jnp.transpose(second, (1, 2, 0, 3)).reshape(2, rows, device_count, block_len)
    return jnp.transpose(second, (2, 0, 1, 3))


def azimuth_matrix(row_list, scale):
    total_rows = row_list.shape[0]
    pulse_index = jnp.arange(total_rows, dtype=jnp.int32)
    select = (row_list[:, None] == pulse_index[None, :]).astype(jnp.float32)
    dft_real, dft_imag = dft_table(total_rows, scale)
    fold_real = jnp.einsum("ji,ja->ai", select, dft_real, precision=highest)
    fold_imag = jnp.einsum("ji,ja->ai", select, dft_imag, precision=highest)
    top = jnp.concatenate([fold_real, -fold_imag], axis=1)
    bottom = jnp.concatenate([fold_imag, fold_real], axis=1)
    return jnp.concatenate([top, bottom], axis=0)


def on_device(echoes, row_list, wavenumber, az_wavenumber, stolt_offset, stolt_coef):
    rows_here = echoes.shape[1]
    span_len = echoes.shape[2]
    lane_count = lax.axis_size("rng")
    pulse_count = lax.axis_size("pulse")
    device_count = pulse_count * lane_count
    total_rows = row_list.shape[0]
    range_len = span_len * lane_count
    block_len = span_len // device_count
    position = lax.axis_index(("pulse", "rng"))
    lane_pos = lax.axis_index("rng")

    spectrum = range_dft_blocks(echoes, device_count, block_len, lane_pos, range_len)
    spectrum = lax.all_to_all(
        spectrum, ("pulse", "rng"), split_axis=0, concat_axis=0, tiled=True
    )
    spectrum = spectrum.reshape(pulse_count, lane_count, 2, rows_here, block_len)

    lane_real = spectrum[:, :, 0]
    lane_imag = spectrum[:, :, 1]
    combined_real = []
    combined_imag = []
    for s in range(lane_count):
        acc_real = 0.0
        acc_imag = 0.0
        for r in range(lane_count):
            turn = -2.0 * math.pi * ((r * s) % lane_count) / lane_count
            wr = round(math.cos(turn), 12)
            wi = round(math.sin(turn), 12)
            if wr != 0.0:
                acc_real = acc_real + wr * lane_real[:, r]
                acc_imag = acc_imag + wr * lane_imag[:, r]
            if wi != 0.0:
                acc_real = acc_real - wi * lane_imag[:, r]
                acc_imag = acc_imag + wi * lane_real[:, r]
        combined_real.append(acc_real)
        combined_imag.append(acc_imag)
    combined = jnp.stack([jnp.stack(combined_real), jnp.stack(combined_imag)], axis=1)
    combined = combined.reshape(lane_count, 2 * total_rows, block_len)

    fold = azimuth_matrix(row_list, 1.0 / math.sqrt(range_len * total_rows))
    az_real = jnp.einsum("ay,syq->sqa", fold[:total_rows], combined, precision=fast)
    az_imag = jnp.einsum("ay,syq->sqa", fold[total_rows:], combined, precision=fast)

    phase_angle = phase_scale * jnp.sqrt(
        wavenumber[:, :, None] ** 2 - az_wavenumber[None, None, :] ** 2
    )
    phase_real, phase_imag = lax.optimization_barrier(
        (jnp.cos(phase_angle), jnp.sin(phase_angle))
    )
    focused_real = az_real * phase_real - az_imag * phase_imag
    focused_imag = az_real * phase_imag + az_imag * phase_real
    focused = jnp.stack([focused_real, focused_imag])

    axes = ("pulse", "rng")
    up = [(i, (i + 1) % device_count) for i in range(device_count)]
    down = [(j, i) for i, j in up]
    left_rim = lax.ppermute(focused[:, :, block_len - RIM:], axes, up)
    right_rim = lax.ppermute(focused[:, :, :RIM], axes, down)
    left_rim = jnp.where(position == 0, jnp.roll(left_rim, 1, axis=1), left_rim)
    right_rim = jnp.where(
        position == device_count - 1, jnp.roll(right_rim, -1, axis=1), right_rim
    )
    widened = jnp.concatenate([left_rim, focused, right_rim], axis=2)

    tap_count = stolt_coef.shape[0]
    piece_index = jnp.arange(block_len, dtype=jnp.int32)
    q_global = position * block_len + piece_index
    bin_index = jnp.arange(lane_count, dtype=jnp.int32)[:, None] * span_len + q_global[None, :]
    relative = stolt_offset - bin_index + RIM
    tap_index = jnp.arange(tap_count, dtype=jnp.int32)
    source = stolt_offset[None, :, :] + tap_index[:, None, None]
    inside = (source >= 0) & (source < range_len)
    weights = jnp.where(inside, stolt_coef, 0.0)
    columns = jnp.arange(block_len + 2 * RIM, dtype=jnp.int32)
    target = piece_index[:, None] + relative[:, :, None]
    band = jnp.zeros((lane_count, block_len, block_len + 2 * RIM), jnp.float32)
    for t in range(tap_count):
        band = band + jnp.where(columns[None, None, :] == target + t, weights[t][:, :, None], 0.0)

    return jnp.einsum("sij,csja->csia", band, widened, precision=highest)


def solution(mesh):
    in_specs = (
        P(None, "pulse", "rng"),
        P(),
        P(None, ("pulse", "rng")),
        P(),
        P(None, ("pulse", "rng")),
        P(None, None, ("pulse", "rng")),
    )
    out_specs = P(None, None, ("pulse", "rng"), None)
    return jax.shard_map(
        on_device, mesh=mesh, in_specs=in_specs, out_specs=out_specs, check_vma=False
    )
```

```python
import math

import jax
import jax.numpy as jnp
from jax import lax
from jax.sharding import PartitionSpec as P

phase_scale = 24.0
highest = lax.Precision.HIGHEST
fast = lax.Precision.HIGH
RIM = 8


def split_factor(length):
    outer_len = 1
    while length % (outer_len * 2) == 0 and outer_len * 2 * (outer_len * 2) <= length:
        outer_len = outer_len * 2
    return outer_len


def dft_table(length, factor):
    index_range = jnp.arange(length, dtype=jnp.int32)
    product = index_range[:, None] * index_range[None, :] % length
    twist_angle = product.astype(jnp.float32) * (-2.0 * math.pi / length)
    return (jnp.cos(twist_angle) * factor, jnp.sin(twist_angle) * factor)


def complex_einsum(pattern, real_part, imag_part, table_real, table_imag):

    def contract(operand, matrix):
        return jnp.einsum(pattern, operand, matrix, precision=fast)

    return (
        contract(real_part, table_real) - contract(imag_part, table_imag),
        contract(real_part, table_imag) + contract(imag_part, table_real),
    )


def last_axis_dft(real_part, imag_part, length, factor):
    inner_len = split_factor(length)
    outer_len = length // inner_len
    leading = real_part.shape[:-1]
    real_part = real_part.reshape(leading + (outer_len, inner_len))
    imag_part = imag_part.reshape(leading + (outer_len, inner_len))
    outer_real, outer_imag = dft_table(outer_len, 1.0)
    real_part, imag_part = complex_einsum(
        "...ba,ub->...ua", real_part, imag_part, outer_real, outer_imag
    )
    col_index = jnp.arange(outer_len, dtype=jnp.int32)[:, None]
    row_index = jnp.arange(inner_len, dtype=jnp.int32)[None, :]
    twist_angle = (col_index * row_index % length).astype(jnp.float32) * (-2.0 * math.pi / length)
    twist_real = jnp.cos(twist_angle)
    twist_imag = jnp.sin(twist_angle)
    real_part, imag_part = (
        real_part * twist_real - imag_part * twist_imag,
        real_part * twist_imag + imag_part * twist_real,
    )
    inner_real, inner_imag = dft_table(inner_len, factor)
    real_part, imag_part = complex_einsum(
        "...ua,va->...vu", real_part, imag_part, inner_real, inner_imag
    )
    return (real_part.reshape(leading + (length,)), imag_part.reshape(leading + (length,)))


def stacked_table(length, factor):
    table_real, table_imag = dft_table(length, factor)
    top = jnp.stack([table_real, -table_imag], axis=1)
    bottom = jnp.stack([table_imag, table_real], axis=1)
    return jnp.stack([top, bottom])


def range_dft_blocks(pair, device_count, block_len, lane_pos, range_len):
    rows = pair.shape[1]
    length = pair.shape[2]
    inner_len = split_factor(length)
    outer_len = length // inner_len
    signal = pair.reshape(2, rows, outer_len, inner_len)
    first = jnp.einsum("ducb,crba->drua", stacked_table(outer_len, 1.0), signal, precision=fast)
    col_index = jnp.arange(outer_len, dtype=jnp.int32)[:, None]
    row_index = jnp.arange(inner_len, dtype=jnp.int32)[None, :]
    twist_angle = (col_index * row_index % length).astype(jnp.float32) * (-2.0 * math.pi / length)
    twist_real = jnp.cos(twist_angle)
    twist_imag = jnp.sin(twist_angle)
    first = jnp.stack(
        [
            first[0] * twist_real - first[1] * twist_imag,
            first[0] * twist_imag + first[1] * twist_real,
        ]
    )
    second = jnp.einsum("dvca,crua->vdru", stacked_table(inner_len, 1.0), first, precision=fast)
    q_index = jnp.arange(inner_len, dtype=jnp.int32)[:, None] * outer_len + jnp.arange(
        outer_len, dtype=jnp.int32
    )[None, :]
    turn_angle = ((lane_pos * q_index) % range_len).astype(jnp.float32) * (
        -2.0 * math.pi / range_len
    )
    turn_real = jnp.cos(turn_angle)[:, None, :]
    turn_imag = jnp.sin(turn_angle)[:, None, :]
    second = jnp.stack(
        [
            second[:, 0] * turn_real - second[:, 1] * turn_imag,
            second[:, 0] * turn_imag + second[:, 1] * turn_real,
        ],
        axis=1,
    )
    if block_len % outer_len == 0:
        per_block = block_len // outer_len
        second = second.reshape(device_count, per_block, 2, rows, outer_len)
        second = jnp.transpose(second, (0, 2, 3, 1, 4))
        return second.reshape(device_count, 2, rows, block_len)
    second = jnp.transpose(second, (1, 2, 0, 3)).reshape(2, rows, device_count, block_len)
    return jnp.transpose(second, (2, 0, 1, 3))


def azimuth_matrix(row_list, scale):
    total_rows = row_list.shape[0]
    pulse_index = jnp.arange(total_rows, dtype=jnp.int32)
    select = (row_list[:, None] == pulse_index[None, :]).astype(jnp.float32)
    dft_real, dft_imag = dft_table(total_rows, scale)
    fold_real = jnp.einsum("ji,ja->ai", select, dft_real, precision=highest)
    fold_imag = jnp.einsum("ji,ja->ai", select, dft_imag, precision=highest)
    top = jnp.concatenate([fold_real, -fold_imag], axis=1)
    bottom = jnp.concatenate([fold_imag, fold_real], axis=1)
    return jnp.concatenate([top, bottom], axis=0)


def on_device(echoes, row_list, wavenumber, az_wavenumber, stolt_offset, stolt_coef):
    rows_here = echoes.shape[1]
    span_len = echoes.shape[2]
    lane_count = lax.axis_size("rng")
    pulse_count = lax.axis_size("pulse")
    device_count = pulse_count * lane_count
    total_rows = row_list.shape[0]
    range_len = span_len * lane_count
    block_len = span_len // device_count
    position = lax.axis_index(("pulse", "rng"))
    lane_pos = lax.axis_index("rng")

    spectrum = range_dft_blocks(echoes, device_count, block_len, lane_pos, range_len)
    if device_count <= 32:
        axes = ("pulse", "rng")
        received = [spectrum[position]]
        for shift in range(1, device_count):
            outgoing = lax.dynamic_index_in_dim(
                spectrum, (position + shift) % device_count, axis=0, keepdims=False
            )
            pairs = [(i, (i + shift) % device_count) for i in range(device_count)]
            received.append(lax.ppermute(outgoing, axes, pairs))
        received = jnp.stack(received)
        source_order = (position - jnp.arange(device_count, dtype=jnp.int32)) % device_count
        spectrum = jnp.take(received, source_order, axis=0)
    else:
        spectrum = lax.all_to_all(
            spectrum, ("pulse", "rng"), split_axis=0, concat_axis=0, tiled=True
        )
    spectrum = spectrum.reshape(pulse_count, lane_count, 2, rows_here, block_len)

    lane_real = spectrum[:, :, 0]
    lane_imag = spectrum[:, :, 1]
    combined_real = []
    combined_imag = []
    for s in range(lane_count):
        acc_real = 0.0
        acc_imag = 0.0
        for r in range(lane_count):
            turn = -2.0 * math.pi * ((r * s) % lane_count) / lane_count
            wr = round(math.cos(turn), 12)
            wi = round(math.sin(turn), 12)
            if wr != 0.0:
                acc_real = acc_real + wr * lane_real[:, r]
                acc_imag = acc_imag + wr * lane_imag[:, r]
            if wi != 0.0:
                acc_real = acc_real - wi * lane_imag[:, r]
                acc_imag = acc_imag + wi * lane_real[:, r]
        combined_real.append(acc_real)
        combined_imag.append(acc_imag)
    combined = jnp.stack([jnp.stack(combined_real), jnp.stack(combined_imag)], axis=1)
    combined = combined.reshape(lane_count, 2 * total_rows, block_len)

    fold = azimuth_matrix(row_list, 1.0 / math.sqrt(range_len * total_rows))
    az_real = jnp.einsum("ay,syq->sqa", fold[:total_rows], combined, precision=fast)
    az_imag = jnp.einsum("ay,syq->sqa", fold[total_rows:], combined, precision=fast)

    phase_angle = phase_scale * jnp.sqrt(
        wavenumber[:, :, None] ** 2 - az_wavenumber[None, None, :] ** 2
    )
    phase_real, phase_imag = lax.optimization_barrier(
        (jnp.cos(phase_angle), jnp.sin(phase_angle))
    )
    focused_real = az_real * phase_real - az_imag * phase_imag
    focused_imag = az_real * phase_imag + az_imag * phase_real
    focused = jnp.stack([focused_real, focused_imag])

    axes = ("pulse", "rng")
    up = [(i, (i + 1) % device_count) for i in range(device_count)]
    down = [(j, i) for i, j in up]
    left_rim = lax.ppermute(focused[:, :, block_len - RIM:], axes, up)
    right_rim = lax.ppermute(focused[:, :, :RIM], axes, down)
    left_rim = jnp.where(position == 0, jnp.roll(left_rim, 1, axis=1), left_rim)
    right_rim = jnp.where(
        position == device_count - 1, jnp.roll(right_rim, -1, axis=1), right_rim
    )
    widened = jnp.concatenate([left_rim, focused, right_rim], axis=2)

    tap_count = stolt_coef.shape[0]
    piece_index = jnp.arange(block_len, dtype=jnp.int32)
    q_global = position * block_len + piece_index
    bin_index = jnp.arange(lane_count, dtype=jnp.int32)[:, None] * span_len + q_global[None, :]
    relative = stolt_offset - bin_index + RIM
    tap_index = jnp.arange(tap_count, dtype=jnp.int32)
    source = stolt_offset[None, :, :] + tap_index[:, None, None]
    inside = (source >= 0) & (source < range_len)
    weights = jnp.where(inside, stolt_coef, 0.0)
    columns = jnp.arange(block_len + 2 * RIM, dtype=jnp.int32)
    target = piece_index[:, None] + relative[:, :, None]
    band = jnp.zeros((lane_count, block_len, block_len + 2 * RIM), jnp.float32)
    for t in range(tap_count):
        band = band + jnp.where(columns[None, None, :] == target + t, weights[t][:, :, None], 0.0)

    return jnp.einsum("sij,csja->csia", band, widened, precision=highest)


def solution(mesh):
    in_specs = (
        P(None, "pulse", "rng"),
        P(),
        P(None, ("pulse", "rng")),
        P(),
        P(None, ("pulse", "rng")),
        P(None, None, ("pulse", "rng")),
    )
    out_specs = P(None, None, ("pulse", "rng"), None)
    return jax.shard_map(
        on_device, mesh=mesh, in_specs=in_specs, out_specs=out_specs, check_vma=False
    )
```

```python
import math

import jax
import jax.numpy as jnp
from jax import lax
from jax.sharding import PartitionSpec as P

phase_scale = 24.0
highest = lax.Precision.HIGHEST
fast = lax.Precision.HIGH
RIM = 8


def split_factor(length):
    outer_len = 1
    while length % (outer_len * 2) == 0 and outer_len * 2 * (outer_len * 2) <= length:
        outer_len = outer_len * 2
    return outer_len


def dft_table(length, factor):
    index_range = jnp.arange(length, dtype=jnp.int32)
    product = index_range[:, None] * index_range[None, :] % length
    twist_angle = product.astype(jnp.float32) * (-2.0 * math.pi / length)
    return (jnp.cos(twist_angle) * factor, jnp.sin(twist_angle) * factor)


def complex_einsum(pattern, real_part, imag_part, table_real, table_imag):

    def contract(operand, matrix):
        return jnp.einsum(pattern, operand, matrix, precision=fast)

    return (
        contract(real_part, table_real) - contract(imag_part, table_imag),
        contract(real_part, table_imag) + contract(imag_part, table_real),
    )


def last_axis_dft(real_part, imag_part, length, factor):
    inner_len = split_factor(length)
    outer_len = length // inner_len
    leading = real_part.shape[:-1]
    real_part = real_part.reshape(leading + (outer_len, inner_len))
    imag_part = imag_part.reshape(leading + (outer_len, inner_len))
    outer_real, outer_imag = dft_table(outer_len, 1.0)
    real_part, imag_part = complex_einsum(
        "...ba,ub->...ua", real_part, imag_part, outer_real, outer_imag
    )
    col_index = jnp.arange(outer_len, dtype=jnp.int32)[:, None]
    row_index = jnp.arange(inner_len, dtype=jnp.int32)[None, :]
    twist_angle = (col_index * row_index % length).astype(jnp.float32) * (-2.0 * math.pi / length)
    twist_real = jnp.cos(twist_angle)
    twist_imag = jnp.sin(twist_angle)
    real_part, imag_part = (
        real_part * twist_real - imag_part * twist_imag,
        real_part * twist_imag + imag_part * twist_real,
    )
    inner_real, inner_imag = dft_table(inner_len, factor)
    real_part, imag_part = complex_einsum(
        "...ua,va->...vu", real_part, imag_part, inner_real, inner_imag
    )
    return (real_part.reshape(leading + (length,)), imag_part.reshape(leading + (length,)))


def stacked_table(length, factor):
    table_real, table_imag = dft_table(length, factor)
    top = jnp.stack([table_real, -table_imag], axis=1)
    bottom = jnp.stack([table_imag, table_real], axis=1)
    return jnp.stack([top, bottom])


def range_dft_blocks(pair, device_count, block_len, lane_pos, range_len):
    rows = pair.shape[1]
    length = pair.shape[2]
    inner_len = split_factor(length)
    outer_len = length // inner_len
    signal = pair.reshape(2, rows, outer_len, inner_len)
    first = jnp.einsum("ducb,crba->drua", stacked_table(outer_len, 1.0), signal, precision=fast)
    col_index = jnp.arange(outer_len, dtype=jnp.int32)[:, None]
    row_index = jnp.arange(inner_len, dtype=jnp.int32)[None, :]
    twist_angle = (col_index * row_index % length).astype(jnp.float32) * (-2.0 * math.pi / length)
    twist_real = jnp.cos(twist_angle)
    twist_imag = jnp.sin(twist_angle)
    first = jnp.stack(
        [
            first[0] * twist_real - first[1] * twist_imag,
            first[0] * twist_imag + first[1] * twist_real,
        ]
    )
    second = jnp.einsum("dvca,crua->vdru", stacked_table(inner_len, 1.0), first, precision=fast)
    q_index = jnp.arange(inner_len, dtype=jnp.int32)[:, None] * outer_len + jnp.arange(
        outer_len, dtype=jnp.int32
    )[None, :]
    turn_angle = ((lane_pos * q_index) % range_len).astype(jnp.float32) * (
        -2.0 * math.pi / range_len
    )
    turn_real = jnp.cos(turn_angle)[:, None, :]
    turn_imag = jnp.sin(turn_angle)[:, None, :]
    second = jnp.stack(
        [
            second[:, 0] * turn_real - second[:, 1] * turn_imag,
            second[:, 0] * turn_imag + second[:, 1] * turn_real,
        ],
        axis=1,
    )
    if block_len % outer_len == 0:
        per_block = block_len // outer_len
        return second.reshape(device_count, per_block, 2, rows, outer_len)
    second = jnp.transpose(second, (1, 2, 0, 3)).reshape(2, rows, device_count, block_len)
    return jnp.transpose(second, (2, 0, 1, 3))[:, None]


def azimuth_matrix(row_list, scale):
    total_rows = row_list.shape[0]
    pulse_index = jnp.arange(total_rows, dtype=jnp.int32)
    select = (row_list[:, None] == pulse_index[None, :]).astype(jnp.float32)
    dft_real, dft_imag = dft_table(total_rows, scale)
    fold_real = jnp.einsum("ji,ja->ai", select, dft_real, precision=highest)
    fold_imag = jnp.einsum("ji,ja->ai", select, dft_imag, precision=highest)
    top = jnp.concatenate([fold_real, -fold_imag], axis=1)
    bottom = jnp.concatenate([fold_imag, fold_real], axis=1)
    return jnp.concatenate([top, bottom], axis=0)


def on_device(echoes, row_list, wavenumber, az_wavenumber, stolt_offset, stolt_coef):
    rows_here = echoes.shape[1]
    span_len = echoes.shape[2]
    lane_count = lax.axis_size("rng")
    pulse_count = lax.axis_size("pulse")
    device_count = pulse_count * lane_count
    total_rows = row_list.shape[0]
    range_len = span_len * lane_count
    block_len = span_len // device_count
    position = lax.axis_index(("pulse", "rng"))
    lane_pos = lax.axis_index("rng")

    spectrum = range_dft_blocks(echoes, device_count, block_len, lane_pos, range_len)
    spectrum = lax.all_to_all(
        spectrum, ("pulse", "rng"), split_axis=0, concat_axis=0, tiled=True
    )
    pieces = spectrum.shape[1]
    spectrum = spectrum.reshape(pulse_count, lane_count, pieces, 2, rows_here, block_len // pieces)
    spectrum = jnp.transpose(spectrum, (0, 1, 3, 4, 2, 5)).reshape(
        pulse_count, lane_count, 2, rows_here, block_len
    )

    lane_real = spectrum[:, :, 0]
    lane_imag = spectrum[:, :, 1]
    combined_real = []
    combined_imag = []
    for s in range(lane_count):
        acc_real = 0.0
        acc_imag = 0.0
        for r in range(lane_count):
            turn = -2.0 * math.pi * ((r * s) % lane_count) / lane_count
            wr = round(math.cos(turn), 12)
            wi = round(math.sin(turn), 12)
            if wr != 0.0:
                acc_real = acc_real + wr * lane_real[:, r]
                acc_imag = acc_imag + wr * lane_imag[:, r]
            if wi != 0.0:
                acc_real = acc_real - wi * lane_imag[:, r]
                acc_imag = acc_imag + wi * lane_real[:, r]
        combined_real.append(acc_real)
        combined_imag.append(acc_imag)
    combined = jnp.stack([jnp.stack(combined_real), jnp.stack(combined_imag)], axis=1)
    combined = combined.reshape(lane_count, 2 * total_rows, block_len)

    fold = azimuth_matrix(row_list, 1.0 / math.sqrt(range_len * total_rows))
    az_real = jnp.einsum("ay,syq->sqa", fold[:total_rows], combined, precision=fast)
    az_imag = jnp.einsum("ay,syq->sqa", fold[total_rows:], combined, precision=fast)

    phase_angle = phase_scale * jnp.sqrt(
        wavenumber[:, :, None] ** 2 - az_wavenumber[None, None, :] ** 2
    )
    phase_real, phase_imag = lax.optimization_barrier(
        (jnp.cos(phase_angle), jnp.sin(phase_angle))
    )
    focused_real = az_real * phase_real - az_imag * phase_imag
    focused_imag = az_real * phase_imag + az_imag * phase_real
    focused = jnp.stack([focused_real, focused_imag])

    axes = ("pulse", "rng")
    up = [(i, (i + 1) % device_count) for i in range(device_count)]
    down = [(j, i) for i, j in up]
    left_rim = lax.ppermute(focused[:, :, block_len - RIM:], axes, up)
    right_rim = lax.ppermute(focused[:, :, :RIM], axes, down)
    left_rim = jnp.where(position == 0, jnp.roll(left_rim, 1, axis=1), left_rim)
    right_rim = jnp.where(
        position == device_count - 1, jnp.roll(right_rim, -1, axis=1), right_rim
    )
    widened = jnp.concatenate([left_rim, focused, right_rim], axis=2)

    tap_count = stolt_coef.shape[0]
    piece_index = jnp.arange(block_len, dtype=jnp.int32)
    q_global = position * block_len + piece_index
    bin_index = jnp.arange(lane_count, dtype=jnp.int32)[:, None] * span_len + q_global[None, :]
    relative = stolt_offset - bin_index + RIM
    tap_index = jnp.arange(tap_count, dtype=jnp.int32)
    source = stolt_offset[None, :, :] + tap_index[:, None, None]
    inside = (source >= 0) & (source < range_len)
    weights = jnp.where(inside, stolt_coef, 0.0)
    columns = jnp.arange(block_len + 2 * RIM, dtype=jnp.int32)
    target = piece_index[:, None] + relative[:, :, None]
    band = jnp.zeros((lane_count, block_len, block_len + 2 * RIM), jnp.float32)
    for t in range(tap_count):
        band = band + jnp.where(columns[None, None, :] == target + t, weights[t][:, :, None], 0.0)

    return jnp.einsum("sij,csja->csia", band, widened, precision=highest)


def solution(mesh):
    in_specs = (
        P(None, "pulse", "rng"),
        P(),
        P(None, ("pulse", "rng")),
        P(),
        P(None, ("pulse", "rng")),
        P(None, None, ("pulse", "rng")),
    )
    out_specs = P(None, None, ("pulse", "rng"), None)
    return jax.shard_map(
        on_device, mesh=mesh, in_specs=in_specs, out_specs=out_specs, check_vma=False
    )
```

```python
import math

import jax
import jax.numpy as jnp
from jax import lax
from jax.sharding import PartitionSpec as P

phase_scale = 24.0
highest = lax.Precision.HIGHEST
fast = lax.Precision.HIGH
RIM = 8


def split_factor(length):
    outer_len = 1
    while length % (outer_len * 2) == 0 and outer_len * 2 * (outer_len * 2) <= length:
        outer_len = outer_len * 2
    return outer_len


def dft_table(length, factor):
    index_range = jnp.arange(length, dtype=jnp.int32)
    product = index_range[:, None] * index_range[None, :] % length
    twist_angle = product.astype(jnp.float32) * (-2.0 * math.pi / length)
    return (jnp.cos(twist_angle) * factor, jnp.sin(twist_angle) * factor)


def complex_einsum(pattern, real_part, imag_part, table_real, table_imag):

    def contract(operand, matrix):
        return jnp.einsum(pattern, operand, matrix, precision=fast)

    return (
        contract(real_part, table_real) - contract(imag_part, table_imag),
        contract(real_part, table_imag) + contract(imag_part, table_real),
    )


def last_axis_dft(real_part, imag_part, length, factor):
    inner_len = split_factor(length)
    outer_len = length // inner_len
    leading = real_part.shape[:-1]
    real_part = real_part.reshape(leading + (outer_len, inner_len))
    imag_part = imag_part.reshape(leading + (outer_len, inner_len))
    outer_real, outer_imag = dft_table(outer_len, 1.0)
    real_part, imag_part = complex_einsum(
        "...ba,ub->...ua", real_part, imag_part, outer_real, outer_imag
    )
    col_index = jnp.arange(outer_len, dtype=jnp.int32)[:, None]
    row_index = jnp.arange(inner_len, dtype=jnp.int32)[None, :]
    twist_angle = (col_index * row_index % length).astype(jnp.float32) * (-2.0 * math.pi / length)
    twist_real = jnp.cos(twist_angle)
    twist_imag = jnp.sin(twist_angle)
    real_part, imag_part = (
        real_part * twist_real - imag_part * twist_imag,
        real_part * twist_imag + imag_part * twist_real,
    )
    inner_real, inner_imag = dft_table(inner_len, factor)
    real_part, imag_part = complex_einsum(
        "...ua,va->...vu", real_part, imag_part, inner_real, inner_imag
    )
    return (real_part.reshape(leading + (length,)), imag_part.reshape(leading + (length,)))


def stacked_table(length, factor):
    table_real, table_imag = dft_table(length, factor)
    top = jnp.stack([table_real, -table_imag], axis=1)
    bottom = jnp.stack([table_imag, table_real], axis=1)
    return jnp.stack([top, bottom])


def range_dft_blocks(pair, device_count, block_len, lane_pos, range_len):
    rows = pair.shape[1]
    length = pair.shape[2]
    inner_len = split_factor(length)
    outer_len = length // inner_len
    signal = pair.reshape(2, rows, outer_len, inner_len)
    first = jnp.einsum("ducb,crba->drua", stacked_table(outer_len, 1.0), signal, precision=fast)
    col_index = jnp.arange(outer_len, dtype=jnp.int32)[:, None]
    row_index = jnp.arange(inner_len, dtype=jnp.int32)[None, :]
    twist_angle = (col_index * row_index % length).astype(jnp.float32) * (-2.0 * math.pi / length)
    twist_real = jnp.cos(twist_angle)
    twist_imag = jnp.sin(twist_angle)
    first = jnp.stack(
        [
            first[0] * twist_real - first[1] * twist_imag,
            first[0] * twist_imag + first[1] * twist_real,
        ]
    )
    second = jnp.einsum("dvca,crua->vdru", stacked_table(inner_len, 1.0), first, precision=fast)
    q_index = jnp.arange(inner_len, dtype=jnp.int32)[:, None] * outer_len + jnp.arange(
        outer_len, dtype=jnp.int32
    )[None, :]
    turn_angle = ((lane_pos * q_index) % range_len).astype(jnp.float32) * (
        -2.0 * math.pi / range_len
    )
    turn_real = jnp.cos(turn_angle)[:, None, :]
    turn_imag = jnp.sin(turn_angle)[:, None, :]
    second = jnp.stack(
        [
            second[:, 0] * turn_real - second[:, 1] * turn_imag,
            second[:, 0] * turn_imag + second[:, 1] * turn_real,
        ],
        axis=1,
    )
    if block_len % outer_len == 0:
        per_block = block_len // outer_len
        return second.reshape(device_count, per_block, 2, rows, outer_len)
    second = jnp.transpose(second, (1, 2, 0, 3)).reshape(2, rows, device_count, block_len)
    return jnp.transpose(second, (2, 0, 1, 3))[:, None]


def azimuth_matrix(row_list, scale):
    total_rows = row_list.shape[0]
    pulse_index = jnp.arange(total_rows, dtype=jnp.int32)
    select = (row_list[:, None] == pulse_index[None, :]).astype(jnp.float32)
    dft_real, dft_imag = dft_table(total_rows, scale)
    fold_real = jnp.einsum("ji,ja->ai", select, dft_real, precision=highest)
    fold_imag = jnp.einsum("ji,ja->ai", select, dft_imag, precision=highest)
    top = jnp.concatenate([fold_real, -fold_imag], axis=1)
    bottom = jnp.concatenate([fold_imag, fold_real], axis=1)
    return jnp.concatenate([top, bottom], axis=0)


def on_device(echoes, row_list, wavenumber, az_wavenumber, stolt_offset, stolt_coef):
    rows_here = echoes.shape[1]
    span_len = echoes.shape[2]
    lane_count = lax.axis_size("rng")
    pulse_count = lax.axis_size("pulse")
    device_count = pulse_count * lane_count
    total_rows = row_list.shape[0]
    range_len = span_len * lane_count
    block_len = span_len // device_count
    position = lax.axis_index(("pulse", "rng"))
    lane_pos = lax.axis_index("rng")

    spectrum = range_dft_blocks(echoes, device_count, block_len, lane_pos, range_len)
    spectrum = lax.all_to_all(
        spectrum, ("pulse", "rng"), split_axis=0, concat_axis=0, tiled=True
    )
    pieces = spectrum.shape[1]
    spectrum = spectrum.reshape(pulse_count, lane_count, pieces, 2, rows_here, block_len // pieces)
    spectrum = jnp.transpose(spectrum, (0, 1, 3, 4, 2, 5)).reshape(
        pulse_count, lane_count, 2, rows_here, block_len
    )

    lane_real = spectrum[:, :, 0]
    lane_imag = spectrum[:, :, 1]
    combined_real = []
    combined_imag = []
    for s in range(lane_count):
        acc_real = 0.0
        acc_imag = 0.0
        for r in range(lane_count):
            turn = -2.0 * math.pi * ((r * s) % lane_count) / lane_count
            wr = round(math.cos(turn), 12)
            wi = round(math.sin(turn), 12)
            if wr != 0.0:
                acc_real = acc_real + wr * lane_real[:, r]
                acc_imag = acc_imag + wr * lane_imag[:, r]
            if wi != 0.0:
                acc_real = acc_real - wi * lane_imag[:, r]
                acc_imag = acc_imag + wi * lane_real[:, r]
        combined_real.append(acc_real)
        combined_imag.append(acc_imag)
    combined = jnp.stack([jnp.stack(combined_real), jnp.stack(combined_imag)], axis=1)
    combined = combined.reshape(lane_count, 2 * total_rows, block_len)

    fold = azimuth_matrix(row_list, 1.0 / math.sqrt(range_len * total_rows))
    az_real = jnp.einsum("ay,syq->sqa", fold[:total_rows], combined, precision=fast)
    az_imag = jnp.einsum("ay,syq->sqa", fold[total_rows:], combined, precision=fast)

    phase_angle = phase_scale * jnp.sqrt(
        wavenumber[:, :, None] ** 2 - az_wavenumber[None, None, :] ** 2
    )
    phase_real, phase_imag = lax.optimization_barrier(
        (jnp.cos(phase_angle), jnp.sin(phase_angle))
    )
    focused_real = az_real * phase_real - az_imag * phase_imag
    focused_imag = az_real * phase_imag + az_imag * phase_real
    focused = jnp.stack([focused_real, focused_imag])

    axes = ("pulse", "rng")
    up = [(i, (i + 1) % device_count) for i in range(device_count)]
    down = [(j, i) for i, j in up]
    left_rim = lax.ppermute(focused[:, :, block_len - RIM:], axes, up)
    right_rim = lax.ppermute(focused[:, :, :RIM], axes, down)
    left_rim = jnp.where(position == 0, jnp.roll(left_rim, 1, axis=1), left_rim)
    right_rim = jnp.where(
        position == device_count - 1, jnp.roll(right_rim, -1, axis=1), right_rim
    )


    tap_count = stolt_coef.shape[0]
    piece_index = jnp.arange(block_len, dtype=jnp.int32)
    q_global = position * block_len + piece_index
    bin_index = jnp.arange(lane_count, dtype=jnp.int32)[:, None] * span_len + q_global[None, :]
    relative = stolt_offset - bin_index + RIM
    tap_index = jnp.arange(tap_count, dtype=jnp.int32)
    source = stolt_offset[None, :, :] + tap_index[:, None, None]
    inside = (source >= 0) & (source < range_len)
    weights = jnp.where(inside, stolt_coef, 0.0)
    columns = jnp.arange(block_len + 2 * RIM, dtype=jnp.int32)
    target = piece_index[:, None] + relative[:, :, None]
    band = jnp.zeros((lane_count, block_len, block_len + 2 * RIM), jnp.float32)
    for t in range(tap_count):
        band = band + jnp.where(columns[None, None, :] == target + t, weights[t][:, :, None], 0.0)

    image = jnp.einsum(
        "sij,csja->csia", band[:, :, RIM:RIM + block_len], focused, precision=highest
    )
    band_left = band[:, :RIM, :RIM]
    band_right = band[:, block_len - RIM:, block_len + RIM:]
    left_part = jnp.sum(band_left[None, :, :, :, None] * left_rim[:, :, None, :, :], axis=3)
    right_part = jnp.sum(band_right[None, :, :, :, None] * right_rim[:, :, None, :, :], axis=3)
    rest = block_len - RIM
    edges = jnp.concatenate(
        [left_part, jnp.zeros_like(image[:, :, RIM:rest]), right_part], axis=2
    ) if rest > RIM else None
    if edges is None:
        edges = jnp.pad(left_part, ((0, 0), (0, 0), (0, rest), (0, 0))) + jnp.pad(
            right_part, ((0, 0), (0, 0), (rest, 0), (0, 0))
        )
    return image + edges


def solution(mesh):
    in_specs = (
        P(None, "pulse", "rng"),
        P(),
        P(None, ("pulse", "rng")),
        P(),
        P(None, ("pulse", "rng")),
        P(None, None, ("pulse", "rng")),
    )
    out_specs = P(None, None, ("pulse", "rng"), None)
    return jax.shard_map(
        on_device, mesh=mesh, in_specs=in_specs, out_specs=out_specs, check_vma=False
    )
```

```python
import math

import jax
import jax.numpy as jnp
from jax import lax
from jax.experimental.layout import Layout, with_layout_constraint
from jax.sharding import PartitionSpec as P

phase_scale = 24.0
highest = lax.Precision.HIGHEST
fast = lax.Precision.HIGH
RIM = 8


def split_factor(length):
    outer_len = 1
    while length % (outer_len * 2) == 0 and outer_len * 2 * (outer_len * 2) <= length:
        outer_len = outer_len * 2
    return outer_len


def dft_table(length, factor):
    index_range = jnp.arange(length, dtype=jnp.int32)
    product = index_range[:, None] * index_range[None, :] % length
    twist_angle = product.astype(jnp.float32) * (-2.0 * math.pi / length)
    return (jnp.cos(twist_angle) * factor, jnp.sin(twist_angle) * factor)


def complex_einsum(pattern, real_part, imag_part, table_real, table_imag):

    def contract(operand, matrix):
        return jnp.einsum(pattern, operand, matrix, precision=fast)

    return (
        contract(real_part, table_real) - contract(imag_part, table_imag),
        contract(real_part, table_imag) + contract(imag_part, table_real),
    )


def last_axis_dft(real_part, imag_part, length, factor):
    inner_len = split_factor(length)
    outer_len = length // inner_len
    leading = real_part.shape[:-1]
    real_part = real_part.reshape(leading + (outer_len, inner_len))
    imag_part = imag_part.reshape(leading + (outer_len, inner_len))
    outer_real, outer_imag = dft_table(outer_len, 1.0)
    real_part, imag_part = complex_einsum(
        "...ba,ub->...ua", real_part, imag_part, outer_real, outer_imag
    )
    col_index = jnp.arange(outer_len, dtype=jnp.int32)[:, None]
    row_index = jnp.arange(inner_len, dtype=jnp.int32)[None, :]
    twist_angle = (col_index * row_index % length).astype(jnp.float32) * (-2.0 * math.pi / length)
    twist_real = jnp.cos(twist_angle)
    twist_imag = jnp.sin(twist_angle)
    real_part, imag_part = (
        real_part * twist_real - imag_part * twist_imag,
        real_part * twist_imag + imag_part * twist_real,
    )
    inner_real, inner_imag = dft_table(inner_len, factor)
    real_part, imag_part = complex_einsum(
        "...ua,va->...vu", real_part, imag_part, inner_real, inner_imag
    )
    return (real_part.reshape(leading + (length,)), imag_part.reshape(leading + (length,)))


def stacked_table(length, factor):
    table_real, table_imag = dft_table(length, factor)
    top = jnp.stack([table_real, -table_imag], axis=1)
    bottom = jnp.stack([table_imag, table_real], axis=1)
    return jnp.stack([top, bottom])


def range_dft_blocks(pair, device_count, block_len, lane_pos, range_len):
    rows = pair.shape[1]
    length = pair.shape[2]
    inner_len = split_factor(length)
    outer_len = length // inner_len
    signal = pair.reshape(2, rows, outer_len, inner_len)
    first = jnp.einsum("ducb,crba->drua", stacked_table(outer_len, 1.0), signal, precision=fast)
    col_index = jnp.arange(outer_len, dtype=jnp.int32)[:, None]
    row_index = jnp.arange(inner_len, dtype=jnp.int32)[None, :]
    twist_angle = (col_index * row_index % length).astype(jnp.float32) * (-2.0 * math.pi / length)
    twist_real = jnp.cos(twist_angle)
    twist_imag = jnp.sin(twist_angle)
    first = jnp.stack(
        [
            first[0] * twist_real - first[1] * twist_imag,
            first[0] * twist_imag + first[1] * twist_real,
        ]
    )
    second = jnp.einsum("dvca,crua->vdru", stacked_table(inner_len, 1.0), first, precision=fast)
    q_index = jnp.arange(inner_len, dtype=jnp.int32)[:, None] * outer_len + jnp.arange(
        outer_len, dtype=jnp.int32
    )[None, :]
    turn_angle = ((lane_pos * q_index) % range_len).astype(jnp.float32) * (
        -2.0 * math.pi / range_len
    )
    turn_real = jnp.cos(turn_angle)[:, None, :]
    turn_imag = jnp.sin(turn_angle)[:, None, :]
    second = jnp.stack(
        [
            second[:, 0] * turn_real - second[:, 1] * turn_imag,
            second[:, 0] * turn_imag + second[:, 1] * turn_real,
        ],
        axis=1,
    )
    if block_len % outer_len == 0:
        per_block = block_len // outer_len
        return second.reshape(device_count, per_block, 2, rows, outer_len)
    second = jnp.transpose(second, (1, 2, 0, 3)).reshape(2, rows, device_count, block_len)
    return jnp.transpose(second, (2, 0, 1, 3))[:, None]


def azimuth_matrix(row_list, scale):
    total_rows = row_list.shape[0]
    pulse_index = jnp.arange(total_rows, dtype=jnp.int32)
    select = (row_list[:, None] == pulse_index[None, :]).astype(jnp.float32)
    dft_real, dft_imag = dft_table(total_rows, scale)
    fold_real = jnp.einsum("ji,ja->ai", select, dft_real, precision=highest)
    fold_imag = jnp.einsum("ji,ja->ai", select, dft_imag, precision=highest)
    top = jnp.concatenate([fold_real, -fold_imag], axis=1)
    bottom = jnp.concatenate([fold_imag, fold_real], axis=1)
    return jnp.concatenate([top, bottom], axis=0)


def on_device(echoes, row_list, wavenumber, az_wavenumber, stolt_offset, stolt_coef):
    rows_here = echoes.shape[1]
    span_len = echoes.shape[2]
    lane_count = lax.axis_size("rng")
    pulse_count = lax.axis_size("pulse")
    device_count = pulse_count * lane_count
    total_rows = row_list.shape[0]
    range_len = span_len * lane_count
    block_len = span_len // device_count
    position = lax.axis_index(("pulse", "rng"))
    lane_pos = lax.axis_index("rng")

    spectrum = range_dft_blocks(echoes, device_count, block_len, lane_pos, range_len)
    spectrum = lax.all_to_all(
        spectrum, ("pulse", "rng"), split_axis=0, concat_axis=0, tiled=True
    )
    pieces = spectrum.shape[1]
    spectrum = spectrum.reshape(pulse_count, lane_count, pieces, 2, rows_here, block_len // pieces)
    spectrum = jnp.transpose(spectrum, (0, 1, 3, 4, 2, 5)).reshape(
        pulse_count, lane_count, 2, rows_here, block_len
    )

    lane_real = spectrum[:, :, 0]
    lane_imag = spectrum[:, :, 1]
    combined_real = []
    combined_imag = []
    for s in range(lane_count):
        acc_real = 0.0
        acc_imag = 0.0
        for r in range(lane_count):
            turn = -2.0 * math.pi * ((r * s) % lane_count) / lane_count
            wr = round(math.cos(turn), 12)
            wi = round(math.sin(turn), 12)
            if wr != 0.0:
                acc_real = acc_real + wr * lane_real[:, r]
                acc_imag = acc_imag + wr * lane_imag[:, r]
            if wi != 0.0:
                acc_real = acc_real - wi * lane_imag[:, r]
                acc_imag = acc_imag + wi * lane_real[:, r]
        combined_real.append(acc_real)
        combined_imag.append(acc_imag)
    combined = jnp.stack([jnp.stack(combined_real), jnp.stack(combined_imag)], axis=1)
    combined = combined.reshape(lane_count, 2 * total_rows, block_len)

    fold = azimuth_matrix(row_list, 1.0 / math.sqrt(range_len * total_rows))
    az_real = jnp.einsum("ay,syq->sqa", fold[:total_rows], combined, precision=fast)
    az_imag = jnp.einsum("ay,syq->sqa", fold[total_rows:], combined, precision=fast)
    az_real = with_layout_constraint(az_real, Layout(major_to_minor=(0, 1, 2)))
    az_imag = with_layout_constraint(az_imag, Layout(major_to_minor=(0, 1, 2)))

    phase_angle = phase_scale * jnp.sqrt(
        wavenumber[:, :, None] ** 2 - az_wavenumber[None, None, :] ** 2
    )
    phase_real, phase_imag = lax.optimization_barrier(
        (jnp.cos(phase_angle), jnp.sin(phase_angle))
    )
    focused_real = az_real * phase_real - az_imag * phase_imag
    focused_imag = az_real * phase_imag + az_imag * phase_real
    focused = jnp.stack([focused_real, focused_imag])

    axes = ("pulse", "rng")
    up = [(i, (i + 1) % device_count) for i in range(device_count)]
    down = [(j, i) for i, j in up]
    left_rim = lax.ppermute(focused[:, :, block_len - RIM:], axes, up)
    right_rim = lax.ppermute(focused[:, :, :RIM], axes, down)
    left_rim = jnp.where(position == 0, jnp.roll(left_rim, 1, axis=1), left_rim)
    right_rim = jnp.where(
        position == device_count - 1, jnp.roll(right_rim, -1, axis=1), right_rim
    )


    tap_count = stolt_coef.shape[0]
    piece_index = jnp.arange(block_len, dtype=jnp.int32)
    q_global = position * block_len + piece_index
    bin_index = jnp.arange(lane_count, dtype=jnp.int32)[:, None] * span_len + q_global[None, :]
    relative = stolt_offset - bin_index + RIM
    tap_index = jnp.arange(tap_count, dtype=jnp.int32)
    source = stolt_offset[None, :, :] + tap_index[:, None, None]
    inside = (source >= 0) & (source < range_len)
    weights = jnp.where(inside, stolt_coef, 0.0)
    columns = jnp.arange(block_len + 2 * RIM, dtype=jnp.int32)
    target = piece_index[:, None] + relative[:, :, None]
    band = jnp.zeros((lane_count, block_len, block_len + 2 * RIM), jnp.float32)
    for t in range(tap_count):
        band = band + jnp.where(columns[None, None, :] == target + t, weights[t][:, :, None], 0.0)

    image = jnp.einsum(
        "sij,csja->csia", band[:, :, RIM:RIM + block_len], focused, precision=highest
    )
    band_left = band[:, :RIM, :RIM]
    band_right = band[:, block_len - RIM:, block_len + RIM:]
    left_part = jnp.sum(band_left[None, :, :, :, None] * left_rim[:, :, None, :, :], axis=3)
    right_part = jnp.sum(band_right[None, :, :, :, None] * right_rim[:, :, None, :, :], axis=3)
    rest = block_len - RIM
    edges = jnp.concatenate(
        [left_part, jnp.zeros_like(image[:, :, RIM:rest]), right_part], axis=2
    ) if rest > RIM else None
    if edges is None:
        edges = jnp.pad(left_part, ((0, 0), (0, 0), (0, rest), (0, 0))) + jnp.pad(
            right_part, ((0, 0), (0, 0), (rest, 0), (0, 0))
        )
    return image + edges


def solution(mesh):
    in_specs = (
        P(None, "pulse", "rng"),
        P(),
        P(None, ("pulse", "rng")),
        P(),
        P(None, ("pulse", "rng")),
        P(None, None, ("pulse", "rng")),
    )
    out_specs = P(None, None, ("pulse", "rng"), None)
    return jax.shard_map(
        on_device, mesh=mesh, in_specs=in_specs, out_specs=out_specs, check_vma=False
    )
```

```python
import math

import jax
import jax.numpy as jnp
from jax import lax
from jax.sharding import PartitionSpec as P

phase_scale = 24.0
highest = lax.Precision.HIGHEST
fast = lax.Precision.HIGH
RIM = 8


def split_factor(length):
    outer_len = 1
    while length % (outer_len * 2) == 0 and outer_len * 2 * (outer_len * 2) <= length:
        outer_len = outer_len * 2
    return outer_len


def dft_table(length, factor):
    index_range = jnp.arange(length, dtype=jnp.int32)
    product = index_range[:, None] * index_range[None, :] % length
    twist_angle = product.astype(jnp.float32) * (-2.0 * math.pi / length)
    return (jnp.cos(twist_angle) * factor, jnp.sin(twist_angle) * factor)


def complex_einsum(pattern, real_part, imag_part, table_real, table_imag):

    def contract(operand, matrix):
        return jnp.einsum(pattern, operand, matrix, precision=fast)

    return (
        contract(real_part, table_real) - contract(imag_part, table_imag),
        contract(real_part, table_imag) + contract(imag_part, table_real),
    )


def last_axis_dft(real_part, imag_part, length, factor):
    inner_len = split_factor(length)
    outer_len = length // inner_len
    leading = real_part.shape[:-1]
    real_part = real_part.reshape(leading + (outer_len, inner_len))
    imag_part = imag_part.reshape(leading + (outer_len, inner_len))
    outer_real, outer_imag = dft_table(outer_len, 1.0)
    real_part, imag_part = complex_einsum(
        "...ba,ub->...ua", real_part, imag_part, outer_real, outer_imag
    )
    col_index = jnp.arange(outer_len, dtype=jnp.int32)[:, None]
    row_index = jnp.arange(inner_len, dtype=jnp.int32)[None, :]
    twist_angle = (col_index * row_index % length).astype(jnp.float32) * (-2.0 * math.pi / length)
    twist_real = jnp.cos(twist_angle)
    twist_imag = jnp.sin(twist_angle)
    real_part, imag_part = (
        real_part * twist_real - imag_part * twist_imag,
        real_part * twist_imag + imag_part * twist_real,
    )
    inner_real, inner_imag = dft_table(inner_len, factor)
    real_part, imag_part = complex_einsum(
        "...ua,va->...vu", real_part, imag_part, inner_real, inner_imag
    )
    return (real_part.reshape(leading + (length,)), imag_part.reshape(leading + (length,)))


def stacked_table(length, factor):
    table_real, table_imag = dft_table(length, factor)
    top = jnp.stack([table_real, -table_imag], axis=1)
    bottom = jnp.stack([table_imag, table_real], axis=1)
    return jnp.stack([top, bottom])


def range_dft_blocks(pair, device_count, block_len, lane_pos, range_len):
    rows = pair.shape[1]
    length = pair.shape[2]
    inner_len = split_factor(length)
    outer_len = length // inner_len
    signal = pair.reshape(2, rows, outer_len, inner_len)
    first = jnp.einsum("ducb,crba->drua", stacked_table(outer_len, 1.0), signal, precision=fast)
    col_index = jnp.arange(outer_len, dtype=jnp.int32)[:, None]
    row_index = jnp.arange(inner_len, dtype=jnp.int32)[None, :]
    twist_angle = (col_index * row_index % length).astype(jnp.float32) * (-2.0 * math.pi / length)
    twist_real = jnp.cos(twist_angle)
    twist_imag = jnp.sin(twist_angle)
    first = jnp.stack(
        [
            first[0] * twist_real - first[1] * twist_imag,
            first[0] * twist_imag + first[1] * twist_real,
        ]
    )
    second = jnp.einsum("dvca,crua->vdru", stacked_table(inner_len, 1.0), first, precision=fast)
    q_index = jnp.arange(inner_len, dtype=jnp.int32)[:, None] * outer_len + jnp.arange(
        outer_len, dtype=jnp.int32
    )[None, :]
    turn_angle = ((lane_pos * q_index) % range_len).astype(jnp.float32) * (
        -2.0 * math.pi / range_len
    )
    turn_real = jnp.cos(turn_angle)[:, None, :]
    turn_imag = jnp.sin(turn_angle)[:, None, :]
    second = jnp.stack(
        [
            second[:, 0] * turn_real - second[:, 1] * turn_imag,
            second[:, 0] * turn_imag + second[:, 1] * turn_real,
        ],
        axis=1,
    )
    if block_len % outer_len == 0:
        per_block = block_len // outer_len
        return second.reshape(device_count, per_block, 2, rows, outer_len)
    second = jnp.transpose(second, (1, 2, 0, 3)).reshape(2, rows, device_count, block_len)
    return jnp.transpose(second, (2, 0, 1, 3))[:, None]


def azimuth_matrix(row_list, scale):
    total_rows = row_list.shape[0]
    pulse_index = jnp.arange(total_rows, dtype=jnp.int32)
    select = (row_list[:, None] == pulse_index[None, :]).astype(jnp.float32)
    dft_real, dft_imag = dft_table(total_rows, scale)
    fold_real = jnp.einsum("ji,ja->ai", select, dft_real, precision=highest)
    fold_imag = jnp.einsum("ji,ja->ai", select, dft_imag, precision=highest)
    top = jnp.concatenate([fold_real, -fold_imag], axis=1)
    bottom = jnp.concatenate([fold_imag, fold_real], axis=1)
    return jnp.concatenate([top, bottom], axis=0)


def on_device(echoes, row_list, wavenumber, az_wavenumber, stolt_offset, stolt_coef):
    rows_here = echoes.shape[1]
    span_len = echoes.shape[2]
    lane_count = lax.axis_size("rng")
    pulse_count = lax.axis_size("pulse")
    device_count = pulse_count * lane_count
    total_rows = row_list.shape[0]
    range_len = span_len * lane_count
    block_len = span_len // device_count
    position = lax.axis_index(("pulse", "rng"))
    lane_pos = lax.axis_index("rng")

    spectrum = range_dft_blocks(echoes, device_count, block_len, lane_pos, range_len)
    spectrum = lax.all_to_all(
        spectrum, ("pulse", "rng"), split_axis=0, concat_axis=0, tiled=True
    )
    pieces = spectrum.shape[1]
    spectrum = spectrum.reshape(pulse_count, lane_count, pieces, 2, rows_here, block_len // pieces)
    spectrum = jnp.transpose(spectrum, (0, 1, 3, 4, 2, 5)).reshape(
        pulse_count, lane_count, 2, rows_here, block_len
    )

    lane_real = spectrum[:, :, 0]
    lane_imag = spectrum[:, :, 1]
    combined_real = []
    combined_imag = []
    for s in range(lane_count):
        acc_real = 0.0
        acc_imag = 0.0
        for r in range(lane_count):
            turn = -2.0 * math.pi * ((r * s) % lane_count) / lane_count
            wr = round(math.cos(turn), 12)
            wi = round(math.sin(turn), 12)
            if wr != 0.0:
                acc_real = acc_real + wr * lane_real[:, r]
                acc_imag = acc_imag + wr * lane_imag[:, r]
            if wi != 0.0:
                acc_real = acc_real - wi * lane_imag[:, r]
                acc_imag = acc_imag + wi * lane_real[:, r]
        combined_real.append(acc_real)
        combined_imag.append(acc_imag)
    combined = jnp.stack([jnp.stack(combined_real), jnp.stack(combined_imag)], axis=1)
    combined = combined.reshape(lane_count, 2 * total_rows, block_len)

    fold = azimuth_matrix(row_list, 1.0 / math.sqrt(range_len * total_rows))
    az_real = jnp.einsum("ay,syq->sqa", fold[:total_rows], combined, precision=fast)
    az_imag = jnp.einsum("ay,syq->sqa", fold[total_rows:], combined, precision=fast)

    phase_angle = phase_scale * jnp.sqrt(
        wavenumber[:, :, None] ** 2 - az_wavenumber[None, None, :] ** 2
    )
    phase_real, phase_imag = lax.optimization_barrier(
        (jnp.cos(phase_angle), jnp.sin(phase_angle))
    )
    focused_real = az_real * phase_real - az_imag * phase_imag
    focused_imag = az_real * phase_imag + az_imag * phase_real
    focused = jnp.stack([focused_real, focused_imag])

    axes = ("pulse", "rng")
    even = position % 2 == 0
    right_edge = focused[:, :, block_len - RIM:]
    left_edge = focused[:, :, :RIM]
    on_chip = [(i, i ^ 1) for i in range(device_count)]
    across = [(i, (i + 1) % device_count if i % 2 else (i - 1) % device_count) for i in range(device_count)]
    from_partner = lax.ppermute(jnp.where(even, right_edge, left_edge), axes, on_chip)
    from_far = lax.ppermute(jnp.where(even, left_edge, right_edge), axes, across)
    left_rim = jnp.where(even, from_far, from_partner)
    right_rim = jnp.where(even, from_partner, from_far)
    left_rim = jnp.where(position == 0, jnp.roll(left_rim, 1, axis=1), left_rim)
    right_rim = jnp.where(
        position == device_count - 1, jnp.roll(right_rim, -1, axis=1), right_rim
    )
    widened = jnp.concatenate([left_rim, focused, right_rim], axis=2)

    tap_count = stolt_coef.shape[0]
    piece_index = jnp.arange(block_len, dtype=jnp.int32)
    q_global = position * block_len + piece_index
    bin_index = jnp.arange(lane_count, dtype=jnp.int32)[:, None] * span_len + q_global[None, :]
    relative = stolt_offset - bin_index + RIM
    tap_index = jnp.arange(tap_count, dtype=jnp.int32)
    source = stolt_offset[None, :, :] + tap_index[:, None, None]
    inside = (source >= 0) & (source < range_len)
    weights = jnp.where(inside, stolt_coef, 0.0)
    columns = jnp.arange(block_len + 2 * RIM, dtype=jnp.int32)
    target = piece_index[:, None] + relative[:, :, None]
    band = jnp.zeros((lane_count, block_len, block_len + 2 * RIM), jnp.float32)
    for t in range(tap_count):
        band = band + jnp.where(columns[None, None, :] == target + t, weights[t][:, :, None], 0.0)

    return jnp.einsum("sij,csja->csia", band, widened, precision=highest)


def solution(mesh):
    in_specs = (
        P(None, "pulse", "rng"),
        P(),
        P(None, ("pulse", "rng")),
        P(),
        P(None, ("pulse", "rng")),
        P(None, None, ("pulse", "rng")),
    )
    out_specs = P(None, None, ("pulse", "rng"), None)
    return jax.shard_map(
        on_device, mesh=mesh, in_specs=in_specs, out_specs=out_specs, check_vma=False
    )
```

```python
import math

import jax
import jax.numpy as jnp
from jax import lax
from jax.sharding import PartitionSpec as P

phase_scale = 24.0
highest = lax.Precision.HIGHEST
fast = lax.Precision.HIGH
RIM = 8


def split_factor(length):
    outer_len = 1
    while length % (outer_len * 2) == 0 and outer_len * 2 * (outer_len * 2) <= length:
        outer_len = outer_len * 2
    return outer_len


def dft_table(length, factor):
    index_range = jnp.arange(length, dtype=jnp.int32)
    product = index_range[:, None] * index_range[None, :] % length
    twist_angle = product.astype(jnp.float32) * (-2.0 * math.pi / length)
    return (jnp.cos(twist_angle) * factor, jnp.sin(twist_angle) * factor)


def complex_einsum(pattern, real_part, imag_part, table_real, table_imag):

    def contract(operand, matrix):
        return jnp.einsum(pattern, operand, matrix, precision=fast)

    return (
        contract(real_part, table_real) - contract(imag_part, table_imag),
        contract(real_part, table_imag) + contract(imag_part, table_real),
    )


def last_axis_dft(real_part, imag_part, length, factor):
    inner_len = split_factor(length)
    outer_len = length // inner_len
    leading = real_part.shape[:-1]
    real_part = real_part.reshape(leading + (outer_len, inner_len))
    imag_part = imag_part.reshape(leading + (outer_len, inner_len))
    outer_real, outer_imag = dft_table(outer_len, 1.0)
    real_part, imag_part = complex_einsum(
        "...ba,ub->...ua", real_part, imag_part, outer_real, outer_imag
    )
    col_index = jnp.arange(outer_len, dtype=jnp.int32)[:, None]
    row_index = jnp.arange(inner_len, dtype=jnp.int32)[None, :]
    twist_angle = (col_index * row_index % length).astype(jnp.float32) * (-2.0 * math.pi / length)
    twist_real = jnp.cos(twist_angle)
    twist_imag = jnp.sin(twist_angle)
    real_part, imag_part = (
        real_part * twist_real - imag_part * twist_imag,
        real_part * twist_imag + imag_part * twist_real,
    )
    inner_real, inner_imag = dft_table(inner_len, factor)
    real_part, imag_part = complex_einsum(
        "...ua,va->...vu", real_part, imag_part, inner_real, inner_imag
    )
    return (real_part.reshape(leading + (length,)), imag_part.reshape(leading + (length,)))


def stacked_table(length, factor):
    table_real, table_imag = dft_table(length, factor)
    top = jnp.stack([table_real, -table_imag], axis=1)
    bottom = jnp.stack([table_imag, table_real], axis=1)
    return jnp.stack([top, bottom])


def range_dft_blocks(pair, device_count, block_len, lane_pos, range_len):
    rows = pair.shape[1]
    length = pair.shape[2]
    inner_len = split_factor(length)
    outer_len = length // inner_len
    signal = pair.reshape(2, rows, outer_len, inner_len)
    first = jnp.einsum("ducb,crba->drua", stacked_table(outer_len, 1.0), signal, precision=fast)
    col_index = jnp.arange(outer_len, dtype=jnp.int32)[:, None]
    row_index = jnp.arange(inner_len, dtype=jnp.int32)[None, :]
    twist_angle = (col_index * row_index % length).astype(jnp.float32) * (-2.0 * math.pi / length)
    twist_real = jnp.cos(twist_angle)
    twist_imag = jnp.sin(twist_angle)
    first = jnp.stack(
        [
            first[0] * twist_real - first[1] * twist_imag,
            first[0] * twist_imag + first[1] * twist_real,
        ]
    )
    second = jnp.einsum("dvca,crua->vdru", stacked_table(inner_len, 1.0), first, precision=fast)
    q_index = jnp.arange(inner_len, dtype=jnp.int32)[:, None] * outer_len + jnp.arange(
        outer_len, dtype=jnp.int32
    )[None, :]
    turn_angle = ((lane_pos * q_index) % range_len).astype(jnp.float32) * (
        -2.0 * math.pi / range_len
    )
    turn_real = jnp.cos(turn_angle)[:, None, :]
    turn_imag = jnp.sin(turn_angle)[:, None, :]
    second = jnp.stack(
        [
            second[:, 0] * turn_real - second[:, 1] * turn_imag,
            second[:, 0] * turn_imag + second[:, 1] * turn_real,
        ],
        axis=1,
    )
    if block_len % outer_len == 0:
        per_block = block_len // outer_len
        return second.reshape(device_count, per_block, 2, rows, outer_len)
    second = jnp.transpose(second, (1, 2, 0, 3)).reshape(2, rows, device_count, block_len)
    return jnp.transpose(second, (2, 0, 1, 3))[:, None]


def azimuth_matrix(row_list, scale):
    total_rows = row_list.shape[0]
    pulse_index = jnp.arange(total_rows, dtype=jnp.int32)
    select = (row_list[:, None] == pulse_index[None, :]).astype(jnp.float32)
    dft_real, dft_imag = dft_table(total_rows, scale)
    fold_real = jnp.einsum("ji,ja->ai", select, dft_real, precision=highest)
    fold_imag = jnp.einsum("ji,ja->ai", select, dft_imag, precision=highest)
    top = jnp.concatenate([fold_real, -fold_imag], axis=1)
    bottom = jnp.concatenate([fold_imag, fold_real], axis=1)
    return jnp.concatenate([top, bottom], axis=0)


def on_device(echoes, row_list, wavenumber, az_wavenumber, stolt_offset, stolt_coef):
    rows_here = echoes.shape[1]
    span_len = echoes.shape[2]
    lane_count = lax.axis_size("rng")
    pulse_count = lax.axis_size("pulse")
    device_count = pulse_count * lane_count
    total_rows = row_list.shape[0]
    range_len = span_len * lane_count
    block_len = span_len // device_count
    position = lax.axis_index(("pulse", "rng"))
    lane_pos = lax.axis_index("rng")

    spectrum = range_dft_blocks(echoes, device_count, block_len, lane_pos, range_len)
    spectrum = lax.all_to_all(
        spectrum, ("pulse", "rng"), split_axis=0, concat_axis=0, tiled=True
    )
    pieces = spectrum.shape[1]
    spectrum = spectrum.reshape(pulse_count, lane_count, pieces, 2, rows_here, block_len // pieces)
    spectrum = jnp.transpose(spectrum, (0, 1, 3, 4, 2, 5)).reshape(
        pulse_count, lane_count, 2, rows_here, block_len
    )

    lane_real = spectrum[:, :, 0]
    lane_imag = spectrum[:, :, 1]
    combined_real = []
    combined_imag = []
    for s in range(lane_count):
        acc_real = 0.0
        acc_imag = 0.0
        for r in range(lane_count):
            turn = -2.0 * math.pi * ((r * s) % lane_count) / lane_count
            wr = round(math.cos(turn), 12)
            wi = round(math.sin(turn), 12)
            if wr != 0.0:
                acc_real = acc_real + wr * lane_real[:, r]
                acc_imag = acc_imag + wr * lane_imag[:, r]
            if wi != 0.0:
                acc_real = acc_real - wi * lane_imag[:, r]
                acc_imag = acc_imag + wi * lane_real[:, r]
        combined_real.append(acc_real)
        combined_imag.append(acc_imag)
    combined = jnp.stack([jnp.stack(combined_real), jnp.stack(combined_imag)], axis=1)
    combined = combined.reshape(lane_count, 2 * total_rows, block_len)

    fold = azimuth_matrix(row_list, 1.0 / math.sqrt(range_len * total_rows))
    az_real = jnp.einsum("ay,syq->sqa", fold[:total_rows], combined, precision=fast)
    az_imag = jnp.einsum("ay,syq->sqa", fold[total_rows:], combined, precision=fast)

    phase_angle = phase_scale * jnp.sqrt(
        wavenumber[:, :, None] ** 2 - az_wavenumber[None, None, :] ** 2
    )
    phase_real, phase_imag = lax.optimization_barrier(
        (jnp.cos(phase_angle), jnp.sin(phase_angle))
    )
    focused_real = az_real * phase_real - az_imag * phase_imag
    focused_imag = az_real * phase_imag + az_imag * phase_real
    focused = jnp.stack([focused_real, focused_imag])

    axes = ("pulse", "rng")
    up = [(i, (i + 1) % device_count) for i in range(device_count)]
    down = [(j, i) for i, j in up]
    left_rim = lax.ppermute(focused[:, :, block_len - RIM:], axes, up)
    right_rim = lax.ppermute(focused[:, :, :RIM], axes, down)
    left_rim = jnp.where(position == 0, jnp.roll(left_rim, 1, axis=1), left_rim)
    right_rim = jnp.where(
        position == device_count - 1, jnp.roll(right_rim, -1, axis=1), right_rim
    )
    widened = jnp.concatenate([left_rim, focused, right_rim], axis=2)

    tap_count = stolt_coef.shape[0]
    piece_index = jnp.arange(block_len, dtype=jnp.int32)
    q_global = position * block_len + piece_index
    bin_index = jnp.arange(lane_count, dtype=jnp.int32)[:, None] * span_len + q_global[None, :]
    relative = stolt_offset - bin_index + RIM
    tap_index = jnp.arange(tap_count, dtype=jnp.int32)
    source = stolt_offset[None, :, :] + tap_index[:, None, None]
    inside = (source >= 0) & (source < range_len)
    weights = jnp.where(inside, stolt_coef, 0.0)
    columns = jnp.arange(block_len + 2 * RIM, dtype=jnp.int32)
    target = piece_index[:, None] + relative[:, :, None]
    band = jnp.zeros((lane_count, block_len, block_len + 2 * RIM), jnp.float32)
    for t in range(tap_count):
        band = band + jnp.where(columns[None, None, :] == target + t, weights[t][:, :, None], 0.0)

    return jnp.einsum("sij,csja->csia", band, widened, precision=fast)


def solution(mesh):
    in_specs = (
        P(None, "pulse", "rng"),
        P(),
        P(None, ("pulse", "rng")),
        P(),
        P(None, ("pulse", "rng")),
        P(None, None, ("pulse", "rng")),
    )
    out_specs = P(None, None, ("pulse", "rng"), None)
    return jax.shard_map(
        on_device, mesh=mesh, in_specs=in_specs, out_specs=out_specs, check_vma=False
    )
```

```python
import math

import jax
import jax.numpy as jnp
from jax import lax
from jax.sharding import PartitionSpec as P

phase_scale = 24.0
highest = lax.Precision.HIGHEST
fast = lax.Precision.HIGH
RIM = 8


def split_factor(length):
    outer_len = 1
    while length % (outer_len * 2) == 0 and outer_len * 2 * (outer_len * 2) <= length:
        outer_len = outer_len * 2
    return outer_len


def dft_table(length, factor):
    index_range = jnp.arange(length, dtype=jnp.int32)
    product = index_range[:, None] * index_range[None, :] % length
    twist_angle = product.astype(jnp.float32) * (-2.0 * math.pi / length)
    return (jnp.cos(twist_angle) * factor, jnp.sin(twist_angle) * factor)


def complex_einsum(pattern, real_part, imag_part, table_real, table_imag):

    def contract(operand, matrix):
        return jnp.einsum(pattern, operand, matrix, precision=fast)

    return (
        contract(real_part, table_real) - contract(imag_part, table_imag),
        contract(real_part, table_imag) + contract(imag_part, table_real),
    )


def last_axis_dft(real_part, imag_part, length, factor):
    inner_len = split_factor(length)
    outer_len = length // inner_len
    leading = real_part.shape[:-1]
    real_part = real_part.reshape(leading + (outer_len, inner_len))
    imag_part = imag_part.reshape(leading + (outer_len, inner_len))
    outer_real, outer_imag = dft_table(outer_len, 1.0)
    real_part, imag_part = complex_einsum(
        "...ba,ub->...ua", real_part, imag_part, outer_real, outer_imag
    )
    col_index = jnp.arange(outer_len, dtype=jnp.int32)[:, None]
    row_index = jnp.arange(inner_len, dtype=jnp.int32)[None, :]
    twist_angle = (col_index * row_index % length).astype(jnp.float32) * (-2.0 * math.pi / length)
    twist_real = jnp.cos(twist_angle)
    twist_imag = jnp.sin(twist_angle)
    real_part, imag_part = (
        real_part * twist_real - imag_part * twist_imag,
        real_part * twist_imag + imag_part * twist_real,
    )
    inner_real, inner_imag = dft_table(inner_len, factor)
    real_part, imag_part = complex_einsum(
        "...ua,va->...vu", real_part, imag_part, inner_real, inner_imag
    )
    return (real_part.reshape(leading + (length,)), imag_part.reshape(leading + (length,)))


def stacked_table(length, factor):
    table_real, table_imag = dft_table(length, factor)
    top = jnp.stack([table_real, -table_imag], axis=1)
    bottom = jnp.stack([table_imag, table_real], axis=1)
    return jnp.stack([top, bottom])


def range_dft_blocks(pair, device_count, block_len, lane_pos, range_len):
    rows = pair.shape[1]
    length = pair.shape[2]
    inner_len = split_factor(length)
    outer_len = length // inner_len
    signal = pair.reshape(2, rows, outer_len, inner_len)
    first = jnp.einsum("ducb,crba->drua", stacked_table(outer_len, 1.0), signal, precision=fast)
    col_index = jnp.arange(outer_len, dtype=jnp.int32)[:, None]
    row_index = jnp.arange(inner_len, dtype=jnp.int32)[None, :]
    twist_angle = (col_index * row_index % length).astype(jnp.float32) * (-2.0 * math.pi / length)
    twist_real = jnp.cos(twist_angle)
    twist_imag = jnp.sin(twist_angle)
    first = jnp.stack(
        [
            first[0] * twist_real - first[1] * twist_imag,
            first[0] * twist_imag + first[1] * twist_real,
        ]
    )
    second = jnp.einsum("dvca,crua->vdru", stacked_table(inner_len, 1.0), first, precision=fast)
    q_index = jnp.arange(inner_len, dtype=jnp.int32)[:, None] * outer_len + jnp.arange(
        outer_len, dtype=jnp.int32
    )[None, :]
    turn_angle = ((lane_pos * q_index) % range_len).astype(jnp.float32) * (
        -2.0 * math.pi / range_len
    )
    turn_real = jnp.cos(turn_angle)[:, None, :]
    turn_imag = jnp.sin(turn_angle)[:, None, :]
    second = jnp.stack(
        [
            second[:, 0] * turn_real - second[:, 1] * turn_imag,
            second[:, 0] * turn_imag + second[:, 1] * turn_real,
        ],
        axis=1,
    )
    if block_len % outer_len == 0:
        per_block = block_len // outer_len
        return second.reshape(device_count, per_block, 2, rows, outer_len)
    second = jnp.transpose(second, (1, 2, 0, 3)).reshape(2, rows, device_count, block_len)
    return jnp.transpose(second, (2, 0, 1, 3))[:, None]


def azimuth_matrix(row_list, scale):
    total_rows = row_list.shape[0]
    pulse_index = jnp.arange(total_rows, dtype=jnp.int32)
    select = (row_list[:, None] == pulse_index[None, :]).astype(jnp.float32)
    dft_real, dft_imag = dft_table(total_rows, scale)
    fold_real = jnp.einsum("ji,ja->ai", select, dft_real, precision=highest)
    fold_imag = jnp.einsum("ji,ja->ai", select, dft_imag, precision=highest)
    top = jnp.concatenate([fold_real, -fold_imag], axis=1)
    bottom = jnp.concatenate([fold_imag, fold_real], axis=1)
    return jnp.concatenate([top, bottom], axis=0)


def on_device(echoes, row_list, wavenumber, az_wavenumber, stolt_offset, stolt_coef):
    rows_here = echoes.shape[1]
    span_len = echoes.shape[2]
    lane_count = lax.axis_size("rng")
    pulse_count = lax.axis_size("pulse")
    device_count = pulse_count * lane_count
    total_rows = row_list.shape[0]
    range_len = span_len * lane_count
    block_len = span_len // device_count
    position = lax.axis_index(("pulse", "rng"))
    lane_pos = lax.axis_index("rng")

    spectrum = range_dft_blocks(echoes, device_count, block_len, lane_pos, range_len)
    pieces = spectrum.shape[1]
    spectrum = spectrum.reshape(device_count, pieces * 2 * rows_here, block_len // pieces)
    spectrum = lax.all_to_all(
        spectrum, ("pulse", "rng"), split_axis=0, concat_axis=0, tiled=True
    )
    spectrum = spectrum.reshape(pulse_count, lane_count, pieces, 2, rows_here, block_len // pieces)
    spectrum = jnp.transpose(spectrum, (0, 1, 3, 4, 2, 5)).reshape(
        pulse_count, lane_count, 2, rows_here, block_len
    )

    lane_real = spectrum[:, :, 0]
    lane_imag = spectrum[:, :, 1]
    combined_real = []
    combined_imag = []
    for s in range(lane_count):
        acc_real = 0.0
        acc_imag = 0.0
        for r in range(lane_count):
            turn = -2.0 * math.pi * ((r * s) % lane_count) / lane_count
            wr = round(math.cos(turn), 12)
            wi = round(math.sin(turn), 12)
            if wr != 0.0:
                acc_real = acc_real + wr * lane_real[:, r]
                acc_imag = acc_imag + wr * lane_imag[:, r]
            if wi != 0.0:
                acc_real = acc_real - wi * lane_imag[:, r]
                acc_imag = acc_imag + wi * lane_real[:, r]
        combined_real.append(acc_real)
        combined_imag.append(acc_imag)
    combined = jnp.stack([jnp.stack(combined_real), jnp.stack(combined_imag)], axis=1)
    combined = combined.reshape(lane_count, 2 * total_rows, block_len)

    fold = azimuth_matrix(row_list, 1.0 / math.sqrt(range_len * total_rows))
    az_real = jnp.einsum("ay,syq->sqa", fold[:total_rows], combined, precision=fast)
    az_imag = jnp.einsum("ay,syq->sqa", fold[total_rows:], combined, precision=fast)

    phase_angle = phase_scale * jnp.sqrt(
        wavenumber[:, :, None] ** 2 - az_wavenumber[None, None, :] ** 2
    )
    phase_real, phase_imag = lax.optimization_barrier(
        (jnp.cos(phase_angle), jnp.sin(phase_angle))
    )
    focused_real = az_real * phase_real - az_imag * phase_imag
    focused_imag = az_real * phase_imag + az_imag * phase_real
    focused = jnp.stack([focused_real, focused_imag])

    axes = ("pulse", "rng")
    up = [(i, (i + 1) % device_count) for i in range(device_count)]
    down = [(j, i) for i, j in up]
    left_rim = lax.ppermute(focused[:, :, block_len - RIM:], axes, up)
    right_rim = lax.ppermute(focused[:, :, :RIM], axes, down)
    left_rim = jnp.where(position == 0, jnp.roll(left_rim, 1, axis=1), left_rim)
    right_rim = jnp.where(
        position == device_count - 1, jnp.roll(right_rim, -1, axis=1), right_rim
    )
    widened = jnp.concatenate([left_rim, focused, right_rim], axis=2)

    tap_count = stolt_coef.shape[0]
    piece_index = jnp.arange(block_len, dtype=jnp.int32)
    q_global = position * block_len + piece_index
    bin_index = jnp.arange(lane_count, dtype=jnp.int32)[:, None] * span_len + q_global[None, :]
    relative = stolt_offset - bin_index + RIM
    tap_index = jnp.arange(tap_count, dtype=jnp.int32)
    source = stolt_offset[None, :, :] + tap_index[:, None, None]
    inside = (source >= 0) & (source < range_len)
    weights = jnp.where(inside, stolt_coef, 0.0)
    columns = jnp.arange(block_len + 2 * RIM, dtype=jnp.int32)
    target = piece_index[:, None] + relative[:, :, None]
    band = jnp.zeros((lane_count, block_len, block_len + 2 * RIM), jnp.float32)
    for t in range(tap_count):
        band = band + jnp.where(columns[None, None, :] == target + t, weights[t][:, :, None], 0.0)

    return jnp.einsum("sij,csja->csia", band, widened, precision=fast)


def solution(mesh):
    in_specs = (
        P(None, "pulse", "rng"),
        P(),
        P(None, ("pulse", "rng")),
        P(),
        P(None, ("pulse", "rng")),
        P(None, None, ("pulse", "rng")),
    )
    out_specs = P(None, None, ("pulse", "rng"), None)
    return jax.shard_map(
        on_device, mesh=mesh, in_specs=in_specs, out_specs=out_specs, check_vma=False
    )
```

```python
import math

import jax
import jax.numpy as jnp
from jax import lax
from jax.sharding import PartitionSpec as P

phase_scale = 24.0
highest = lax.Precision.HIGHEST
fast = lax.Precision.HIGH
RIM = 8


def split_factor(length):
    outer_len = 1
    while length % (outer_len * 2) == 0 and outer_len * 2 * (outer_len * 2) <= length:
        outer_len = outer_len * 2
    return outer_len


def dft_table(length, factor):
    index_range = jnp.arange(length, dtype=jnp.int32)
    product = index_range[:, None] * index_range[None, :] % length
    twist_angle = product.astype(jnp.float32) * (-2.0 * math.pi / length)
    return (jnp.cos(twist_angle) * factor, jnp.sin(twist_angle) * factor)


def complex_einsum(pattern, real_part, imag_part, table_real, table_imag):

    def contract(operand, matrix):
        return jnp.einsum(pattern, operand, matrix, precision=fast)

    return (
        contract(real_part, table_real) - contract(imag_part, table_imag),
        contract(real_part, table_imag) + contract(imag_part, table_real),
    )


def last_axis_dft(real_part, imag_part, length, factor):
    inner_len = split_factor(length)
    outer_len = length // inner_len
    leading = real_part.shape[:-1]
    real_part = real_part.reshape(leading + (outer_len, inner_len))
    imag_part = imag_part.reshape(leading + (outer_len, inner_len))
    outer_real, outer_imag = dft_table(outer_len, 1.0)
    real_part, imag_part = complex_einsum(
        "...ba,ub->...ua", real_part, imag_part, outer_real, outer_imag
    )
    col_index = jnp.arange(outer_len, dtype=jnp.int32)[:, None]
    row_index = jnp.arange(inner_len, dtype=jnp.int32)[None, :]
    twist_angle = (col_index * row_index % length).astype(jnp.float32) * (-2.0 * math.pi / length)
    twist_real = jnp.cos(twist_angle)
    twist_imag = jnp.sin(twist_angle)
    real_part, imag_part = (
        real_part * twist_real - imag_part * twist_imag,
        real_part * twist_imag + imag_part * twist_real,
    )
    inner_real, inner_imag = dft_table(inner_len, factor)
    real_part, imag_part = complex_einsum(
        "...ua,va->...vu", real_part, imag_part, inner_real, inner_imag
    )
    return (real_part.reshape(leading + (length,)), imag_part.reshape(leading + (length,)))


def stacked_table(length, factor):
    table_real, table_imag = dft_table(length, factor)
    top = jnp.stack([table_real, -table_imag], axis=1)
    bottom = jnp.stack([table_imag, table_real], axis=1)
    return jnp.stack([top, bottom])


def range_dft_blocks(pair, device_count, block_len, lane_pos, range_len):
    rows = pair.shape[1]
    length = pair.shape[2]
    inner_len = split_factor(length)
    outer_len = length // inner_len
    signal = pair.reshape(2, rows, outer_len, inner_len)
    first = jnp.einsum("ducb,crba->drua", stacked_table(outer_len, 1.0), signal, precision=fast)
    col_index = jnp.arange(outer_len, dtype=jnp.int32)[:, None]
    row_index = jnp.arange(inner_len, dtype=jnp.int32)[None, :]
    twist_angle = (col_index * row_index % length).astype(jnp.float32) * (-2.0 * math.pi / length)
    twist_real = jnp.cos(twist_angle)
    twist_imag = jnp.sin(twist_angle)
    first = jnp.stack(
        [
            first[0] * twist_real - first[1] * twist_imag,
            first[0] * twist_imag + first[1] * twist_real,
        ]
    )
    second = jnp.einsum("dvca,crua->vdru", stacked_table(inner_len, 1.0), first, precision=fast)
    q_index = jnp.arange(inner_len, dtype=jnp.int32)[:, None] * outer_len + jnp.arange(
        outer_len, dtype=jnp.int32
    )[None, :]
    turn_angle = ((lane_pos * q_index) % range_len).astype(jnp.float32) * (
        -2.0 * math.pi / range_len
    )
    turn_real = jnp.cos(turn_angle)[:, None, :]
    turn_imag = jnp.sin(turn_angle)[:, None, :]
    second = jnp.stack(
        [
            second[:, 0] * turn_real - second[:, 1] * turn_imag,
            second[:, 0] * turn_imag + second[:, 1] * turn_real,
        ],
        axis=1,
    )
    if block_len % outer_len == 0:
        per_block = block_len // outer_len
        return second.reshape(device_count, per_block, 2, rows, outer_len)
    second = jnp.transpose(second, (1, 2, 0, 3)).reshape(2, rows, device_count, block_len)
    return jnp.transpose(second, (2, 0, 1, 3))[:, None]


def azimuth_matrix(row_list, scale):
    total_rows = row_list.shape[0]
    pulse_index = jnp.arange(total_rows, dtype=jnp.int32)
    select = (row_list[:, None] == pulse_index[None, :]).astype(jnp.float32)
    dft_real, dft_imag = dft_table(total_rows, scale)
    fold_real = jnp.einsum("ji,ja->ai", select, dft_real, precision=highest)
    fold_imag = jnp.einsum("ji,ja->ai", select, dft_imag, precision=highest)
    top = jnp.concatenate([fold_real, -fold_imag], axis=1)
    bottom = jnp.concatenate([fold_imag, fold_real], axis=1)
    return jnp.concatenate([top, bottom], axis=0)


def on_device(echoes, row_list, wavenumber, az_wavenumber, stolt_offset, stolt_coef):
    rows_here = echoes.shape[1]
    span_len = echoes.shape[2]
    lane_count = lax.axis_size("rng")
    pulse_count = lax.axis_size("pulse")
    device_count = pulse_count * lane_count
    total_rows = row_list.shape[0]
    range_len = span_len * lane_count
    block_len = span_len // device_count
    position = lax.axis_index(("pulse", "rng"))
    lane_pos = lax.axis_index("rng")

    spectrum = range_dft_blocks(echoes, device_count, block_len, lane_pos, range_len)
    pieces = spectrum.shape[1]
    spectrum = spectrum.reshape(device_count, pieces * 2 * rows_here, block_len // pieces)
    spectrum = lax.all_to_all(
        spectrum, ("pulse", "rng"), split_axis=0, concat_axis=0, tiled=True
    )
    spectrum = spectrum.reshape(pulse_count, lane_count, pieces, 2, rows_here, block_len // pieces)
    spectrum = jnp.transpose(spectrum, (0, 1, 3, 4, 2, 5)).reshape(
        pulse_count, lane_count, 2, rows_here, block_len
    )

    lane_real = spectrum[:, :, 0]
    lane_imag = spectrum[:, :, 1]
    combined_real = []
    combined_imag = []
    for s in range(lane_count):
        acc_real = 0.0
        acc_imag = 0.0
        for r in range(lane_count):
            turn = -2.0 * math.pi * ((r * s) % lane_count) / lane_count
            wr = round(math.cos(turn), 12)
            wi = round(math.sin(turn), 12)
            if wr != 0.0:
                acc_real = acc_real + wr * lane_real[:, r]
                acc_imag = acc_imag + wr * lane_imag[:, r]
            if wi != 0.0:
                acc_real = acc_real - wi * lane_imag[:, r]
                acc_imag = acc_imag + wi * lane_real[:, r]
        combined_real.append(acc_real)
        combined_imag.append(acc_imag)
    combined = jnp.stack([jnp.stack(combined_real), jnp.stack(combined_imag)], axis=1)
    combined = combined.reshape(lane_count, 2 * total_rows, block_len)

    axes = ("pulse", "rng")
    up = [(i, (i + 1) % device_count) for i in range(device_count)]
    down = [(j, i) for i, j in up]

    def beside(left_piece, right_piece, axis):
        left = lax.ppermute(left_piece, axes, up)
        right = lax.ppermute(right_piece, axes, down)
        left = jnp.where(position == 0, jnp.roll(left, 1, axis=axis), left)
        right = jnp.where(position == device_count - 1, jnp.roll(right, -1, axis=axis), right)
        return left, right

    wave_left, wave_right = beside(wavenumber[:, block_len - RIM:], wavenumber[:, :RIM], 0)
    rim_left, rim_right = beside(
        jnp.swapaxes(combined[:, :, block_len - RIM:], 1, 2),
        jnp.swapaxes(combined[:, :, :RIM], 1, 2),
        0,
    )

    fold = azimuth_matrix(row_list, 1.0 / math.sqrt(range_len * total_rows))

    def focus(az_real, az_imag, wave):
        phase_angle = phase_scale * jnp.sqrt(
            wave[:, :, None] ** 2 - az_wavenumber[None, None, :] ** 2
        )
        phase_real = jnp.cos(phase_angle)
        phase_imag = jnp.sin(phase_angle)
        return jnp.stack(
            [
                az_real * phase_real - az_imag * phase_imag,
                az_real * phase_imag + az_imag * phase_real,
            ]
        )

    az_real = jnp.einsum("ay,syq->sqa", fold[:total_rows], combined, precision=fast)
    az_imag = jnp.einsum("ay,syq->sqa", fold[total_rows:], combined, precision=fast)
    phase_angle = phase_scale * jnp.sqrt(
        wavenumber[:, :, None] ** 2 - az_wavenumber[None, None, :] ** 2
    )
    phase_real, phase_imag = lax.optimization_barrier(
        (jnp.cos(phase_angle), jnp.sin(phase_angle))
    )
    focused = jnp.stack(
        [
            az_real * phase_real - az_imag * phase_imag,
            az_real * phase_imag + az_imag * phase_real,
        ]
    )

    def rim_focus(rim, wave):
        rim_real = jnp.einsum("ay,sjy->sja", fold[:total_rows], rim, precision=fast)
        rim_imag = jnp.einsum("ay,sjy->sja", fold[total_rows:], rim, precision=fast)
        return focus(rim_real, rim_imag, wave)

    left_rim = rim_focus(rim_left, wave_left)
    right_rim = rim_focus(rim_right, wave_right)
    widened = jnp.concatenate([left_rim, focused, right_rim], axis=2)

    tap_count = stolt_coef.shape[0]
    piece_index = jnp.arange(block_len, dtype=jnp.int32)
    q_global = position * block_len + piece_index
    bin_index = jnp.arange(lane_count, dtype=jnp.int32)[:, None] * span_len + q_global[None, :]
    relative = stolt_offset - bin_index + RIM
    tap_index = jnp.arange(tap_count, dtype=jnp.int32)
    source = stolt_offset[None, :, :] + tap_index[:, None, None]
    inside = (source >= 0) & (source < range_len)
    weights = jnp.where(inside, stolt_coef, 0.0)
    columns = jnp.arange(block_len + 2 * RIM, dtype=jnp.int32)
    target = piece_index[:, None] + relative[:, :, None]
    band = jnp.zeros((lane_count, block_len, block_len + 2 * RIM), jnp.float32)
    for t in range(tap_count):
        band = band + jnp.where(columns[None, None, :] == target + t, weights[t][:, :, None], 0.0)

    return jnp.einsum("sij,csja->csia", band, widened, precision=fast)


def solution(mesh):
    in_specs = (
        P(None, "pulse", "rng"),
        P(),
        P(None, ("pulse", "rng")),
        P(),
        P(None, ("pulse", "rng")),
        P(None, None, ("pulse", "rng")),
    )
    out_specs = P(None, None, ("pulse", "rng"), None)
    return jax.shard_map(
        on_device, mesh=mesh, in_specs=in_specs, out_specs=out_specs, check_vma=False
    )
```

```python
import math

import jax
import jax.numpy as jnp
from jax import lax
from jax.sharding import PartitionSpec as P

phase_scale = 24.0
highest = lax.Precision.HIGHEST
fast = lax.Precision.HIGH
RIM = 8


def split_factor(length):
    outer_len = 1
    while length % (outer_len * 2) == 0 and outer_len * 2 * (outer_len * 2) <= length:
        outer_len = outer_len * 2
    return outer_len


def dft_table(length, factor):
    index_range = jnp.arange(length, dtype=jnp.int32)
    product = index_range[:, None] * index_range[None, :] % length
    twist_angle = product.astype(jnp.float32) * (-2.0 * math.pi / length)
    return (jnp.cos(twist_angle) * factor, jnp.sin(twist_angle) * factor)


def complex_einsum(pattern, real_part, imag_part, table_real, table_imag):

    def contract(operand, matrix):
        return jnp.einsum(pattern, operand, matrix, precision=fast)

    return (
        contract(real_part, table_real) - contract(imag_part, table_imag),
        contract(real_part, table_imag) + contract(imag_part, table_real),
    )


def last_axis_dft(real_part, imag_part, length, factor):
    inner_len = split_factor(length)
    outer_len = length // inner_len
    leading = real_part.shape[:-1]
    real_part = real_part.reshape(leading + (outer_len, inner_len))
    imag_part = imag_part.reshape(leading + (outer_len, inner_len))
    outer_real, outer_imag = dft_table(outer_len, 1.0)
    real_part, imag_part = complex_einsum(
        "...ba,ub->...ua", real_part, imag_part, outer_real, outer_imag
    )
    col_index = jnp.arange(outer_len, dtype=jnp.int32)[:, None]
    row_index = jnp.arange(inner_len, dtype=jnp.int32)[None, :]
    twist_angle = (col_index * row_index % length).astype(jnp.float32) * (-2.0 * math.pi / length)
    twist_real = jnp.cos(twist_angle)
    twist_imag = jnp.sin(twist_angle)
    real_part, imag_part = (
        real_part * twist_real - imag_part * twist_imag,
        real_part * twist_imag + imag_part * twist_real,
    )
    inner_real, inner_imag = dft_table(inner_len, factor)
    real_part, imag_part = complex_einsum(
        "...ua,va->...vu", real_part, imag_part, inner_real, inner_imag
    )
    return (real_part.reshape(leading + (length,)), imag_part.reshape(leading + (length,)))


def stacked_table(length, factor):
    table_real, table_imag = dft_table(length, factor)
    top = jnp.stack([table_real, -table_imag], axis=1)
    bottom = jnp.stack([table_imag, table_real], axis=1)
    return jnp.stack([top, bottom])


def range_dft_blocks(pair, device_count, block_len, lane_pos, range_len):
    rows = pair.shape[1]
    length = pair.shape[2]
    inner_len = split_factor(length)
    outer_len = length // inner_len
    signal = pair.reshape(2, rows, outer_len, inner_len)
    first = jnp.einsum("ducb,crba->drua", stacked_table(outer_len, 1.0), signal, precision=fast)
    col_index = jnp.arange(outer_len, dtype=jnp.int32)[:, None]
    row_index = jnp.arange(inner_len, dtype=jnp.int32)[None, :]
    twist_angle = (col_index * row_index % length).astype(jnp.float32) * (-2.0 * math.pi / length)
    twist_real = jnp.cos(twist_angle)
    twist_imag = jnp.sin(twist_angle)
    first = jnp.stack(
        [
            first[0] * twist_real - first[1] * twist_imag,
            first[0] * twist_imag + first[1] * twist_real,
        ]
    )
    second = jnp.einsum("dvca,crua->vdru", stacked_table(inner_len, 1.0), first, precision=fast)
    q_index = jnp.arange(inner_len, dtype=jnp.int32)[:, None] * outer_len + jnp.arange(
        outer_len, dtype=jnp.int32
    )[None, :]
    turn_angle = ((lane_pos * q_index) % range_len).astype(jnp.float32) * (
        -2.0 * math.pi / range_len
    )
    turn_real = jnp.cos(turn_angle)[:, None, :]
    turn_imag = jnp.sin(turn_angle)[:, None, :]
    second = jnp.stack(
        [
            second[:, 0] * turn_real - second[:, 1] * turn_imag,
            second[:, 0] * turn_imag + second[:, 1] * turn_real,
        ],
        axis=1,
    )
    if block_len % outer_len == 0:
        per_block = block_len // outer_len
        return second.reshape(device_count, per_block, 2, rows, outer_len)
    second = jnp.transpose(second, (1, 2, 0, 3)).reshape(2, rows, device_count, block_len)
    return jnp.transpose(second, (2, 0, 1, 3))[:, None]


def azimuth_matrix(row_list, scale):
    total_rows = row_list.shape[0]
    pulse_index = jnp.arange(total_rows, dtype=jnp.int32)
    select = (row_list[:, None] == pulse_index[None, :]).astype(jnp.float32)
    dft_real, dft_imag = dft_table(total_rows, scale)
    fold_real = jnp.einsum("ji,ja->ai", select, dft_real, precision=highest)
    fold_imag = jnp.einsum("ji,ja->ai", select, dft_imag, precision=highest)
    top = jnp.concatenate([fold_real, -fold_imag], axis=1)
    bottom = jnp.concatenate([fold_imag, fold_real], axis=1)
    return top, bottom


def on_device(echoes, row_list, wavenumber, az_wavenumber, stolt_offset, stolt_coef):
    rows_here = echoes.shape[1]
    span_len = echoes.shape[2]
    lane_count = lax.axis_size("rng")
    pulse_count = lax.axis_size("pulse")
    device_count = pulse_count * lane_count
    total_rows = row_list.shape[0]
    range_len = span_len * lane_count
    block_len = span_len // device_count
    position = lax.axis_index(("pulse", "rng"))
    lane_pos = lax.axis_index("rng")

    spectrum = range_dft_blocks(echoes, device_count, block_len, lane_pos, range_len)
    pieces = spectrum.shape[1]
    spectrum = spectrum.reshape(device_count, pieces * 2 * rows_here, block_len // pieces)
    spectrum = lax.all_to_all(
        spectrum, ("pulse", "rng"), split_axis=0, concat_axis=0, tiled=True
    )
    spectrum = spectrum.reshape(pulse_count, lane_count, pieces, 2, rows_here, block_len // pieces)
    spectrum = jnp.transpose(spectrum, (0, 1, 3, 4, 2, 5)).reshape(
        pulse_count, lane_count, 2, rows_here, block_len
    )

    lane_real = spectrum[:, :, 0]
    lane_imag = spectrum[:, :, 1]
    combined_real = []
    combined_imag = []
    for s in range(lane_count):
        acc_real = 0.0
        acc_imag = 0.0
        for r in range(lane_count):
            turn = -2.0 * math.pi * ((r * s) % lane_count) / lane_count
            wr = round(math.cos(turn), 12)
            wi = round(math.sin(turn), 12)
            if wr != 0.0:
                acc_real = acc_real + wr * lane_real[:, r]
                acc_imag = acc_imag + wr * lane_imag[:, r]
            if wi != 0.0:
                acc_real = acc_real - wi * lane_imag[:, r]
                acc_imag = acc_imag + wi * lane_real[:, r]
        combined_real.append(acc_real)
        combined_imag.append(acc_imag)
    combined = jnp.stack([jnp.stack(combined_real), jnp.stack(combined_imag)], axis=1)
    combined = combined.reshape(lane_count, 2 * total_rows, block_len)

    axes = ("pulse", "rng")
    up = [(i, (i + 1) % device_count) for i in range(device_count)]
    down = [(j, i) for i, j in up]

    def beside(left_piece, right_piece, axis):
        left = lax.ppermute(left_piece, axes, up)
        right = lax.ppermute(right_piece, axes, down)
        left = jnp.where(position == 0, jnp.roll(left, 1, axis=axis), left)
        right = jnp.where(position == device_count - 1, jnp.roll(right, -1, axis=axis), right)
        return left, right

    wave_left, wave_right = beside(wavenumber[:, block_len - RIM:], wavenumber[:, :RIM], 0)
    rim_left, rim_right = beside(
        jnp.swapaxes(combined[:, :, block_len - RIM:], 1, 2),
        jnp.swapaxes(combined[:, :, :RIM], 1, 2),
        0,
    )

    fold_top, fold_bottom = azimuth_matrix(row_list, 1.0 / math.sqrt(range_len * total_rows))

    def focus(az_real, az_imag, wave):
        phase_angle = phase_scale * jnp.sqrt(
            wave[:, :, None] ** 2 - az_wavenumber[None, None, :] ** 2
        )
        phase_real = jnp.cos(phase_angle)
        phase_imag = jnp.sin(phase_angle)
        return jnp.stack(
            [
                az_real * phase_real - az_imag * phase_imag,
                az_real * phase_imag + az_imag * phase_real,
            ]
        )

    az_real = jnp.einsum("ay,syq->sqa", fold_top, combined, precision=fast)
    az_imag = jnp.einsum("ay,syq->sqa", fold_bottom, combined, precision=fast)
    phase_angle = phase_scale * jnp.sqrt(
        wavenumber[:, :, None] ** 2 - az_wavenumber[None, None, :] ** 2
    )
    phase_real, phase_imag = lax.optimization_barrier(
        (jnp.cos(phase_angle), jnp.sin(phase_angle))
    )
    focused = jnp.stack(
        [
            az_real * phase_real - az_imag * phase_imag,
            az_real * phase_imag + az_imag * phase_real,
        ]
    )

    rims = jnp.concatenate([rim_left, rim_right], axis=1)
    rim_real = jnp.einsum("ay,sjy->sja", fold_top, rims, precision=fast)
    rim_imag = jnp.einsum("ay,sjy->sja", fold_bottom, rims, precision=fast)
    rims = focus(rim_real, rim_imag, jnp.concatenate([wave_left, wave_right], axis=1))
    left_rim = rims[:, :, :RIM]
    right_rim = rims[:, :, RIM:]
    widened = jnp.concatenate([left_rim, focused, right_rim], axis=2)

    tap_count = stolt_coef.shape[0]
    piece_index = jnp.arange(block_len, dtype=jnp.int32)
    q_global = position * block_len + piece_index
    bin_index = jnp.arange(lane_count, dtype=jnp.int32)[:, None] * span_len + q_global[None, :]
    relative = stolt_offset - bin_index + RIM
    tap_index = jnp.arange(tap_count, dtype=jnp.int32)
    source = stolt_offset[None, :, :] + tap_index[:, None, None]
    inside = (source >= 0) & (source < range_len)
    weights = jnp.where(inside, stolt_coef, 0.0)
    columns = jnp.arange(block_len + 2 * RIM, dtype=jnp.int32)
    target = piece_index[:, None] + relative[:, :, None]
    band = jnp.zeros((lane_count, block_len, block_len + 2 * RIM), jnp.float32)
    for t in range(tap_count):
        band = band + jnp.where(columns[None, None, :] == target + t, weights[t][:, :, None], 0.0)

    return jnp.einsum("sij,csja->csia", band, widened, precision=fast)


def solution(mesh):
    in_specs = (
        P(None, "pulse", "rng"),
        P(),
        P(None, ("pulse", "rng")),
        P(),
        P(None, ("pulse", "rng")),
        P(None, None, ("pulse", "rng")),
    )
    out_specs = P(None, None, ("pulse", "rng"), None)
    return jax.shard_map(
        on_device, mesh=mesh, in_specs=in_specs, out_specs=out_specs, check_vma=False
    )
```

```python
import math

import jax
import jax.numpy as jnp
from jax import lax
from jax.sharding import PartitionSpec as P

phase_scale = 24.0
highest = lax.Precision.HIGHEST
fast = lax.Precision.HIGH
RIM = 8


def split_factor(length):
    outer_len = 1
    while length % (outer_len * 2) == 0 and outer_len * 2 * (outer_len * 2) <= length:
        outer_len = outer_len * 2
    return outer_len


def dft_table(length, factor):
    index_range = jnp.arange(length, dtype=jnp.int32)
    product = index_range[:, None] * index_range[None, :] % length
    twist_angle = product.astype(jnp.float32) * (-2.0 * math.pi / length)
    return (jnp.cos(twist_angle) * factor, jnp.sin(twist_angle) * factor)


def complex_einsum(pattern, real_part, imag_part, table_real, table_imag):

    def contract(operand, matrix):
        return jnp.einsum(pattern, operand, matrix, precision=fast)

    return (
        contract(real_part, table_real) - contract(imag_part, table_imag),
        contract(real_part, table_imag) + contract(imag_part, table_real),
    )


def last_axis_dft(real_part, imag_part, length, factor):
    inner_len = split_factor(length)
    outer_len = length // inner_len
    leading = real_part.shape[:-1]
    real_part = real_part.reshape(leading + (outer_len, inner_len))
    imag_part = imag_part.reshape(leading + (outer_len, inner_len))
    outer_real, outer_imag = dft_table(outer_len, 1.0)
    real_part, imag_part = complex_einsum(
        "...ba,ub->...ua", real_part, imag_part, outer_real, outer_imag
    )
    col_index = jnp.arange(outer_len, dtype=jnp.int32)[:, None]
    row_index = jnp.arange(inner_len, dtype=jnp.int32)[None, :]
    twist_angle = (col_index * row_index % length).astype(jnp.float32) * (-2.0 * math.pi / length)
    twist_real = jnp.cos(twist_angle)
    twist_imag = jnp.sin(twist_angle)
    real_part, imag_part = (
        real_part * twist_real - imag_part * twist_imag,
        real_part * twist_imag + imag_part * twist_real,
    )
    inner_real, inner_imag = dft_table(inner_len, factor)
    real_part, imag_part = complex_einsum(
        "...ua,va->...vu", real_part, imag_part, inner_real, inner_imag
    )
    return (real_part.reshape(leading + (length,)), imag_part.reshape(leading + (length,)))


def stacked_table(length, factor):
    table_real, table_imag = dft_table(length, factor)
    top = jnp.stack([table_real, -table_imag], axis=1)
    bottom = jnp.stack([table_imag, table_real], axis=1)
    return jnp.stack([top, bottom])


def range_dft_blocks(pair, device_count, block_len, lane_pos, range_len):
    rows = pair.shape[1]
    length = pair.shape[2]
    inner_len = split_factor(length)
    outer_len = length // inner_len
    signal = pair.reshape(2, rows, outer_len, inner_len)
    first = jnp.einsum("ducb,crba->drua", stacked_table(outer_len, 1.0), signal, precision=fast)
    col_index = jnp.arange(outer_len, dtype=jnp.int32)[:, None]
    row_index = jnp.arange(inner_len, dtype=jnp.int32)[None, :]
    twist_angle = (col_index * row_index % length).astype(jnp.float32) * (-2.0 * math.pi / length)
    twist_real = jnp.cos(twist_angle)
    twist_imag = jnp.sin(twist_angle)
    first = jnp.stack(
        [
            first[0] * twist_real - first[1] * twist_imag,
            first[0] * twist_imag + first[1] * twist_real,
        ]
    )
    second = jnp.einsum("dvca,crua->vdru", stacked_table(inner_len, 1.0), first, precision=fast)
    q_index = jnp.arange(inner_len, dtype=jnp.int32)[:, None] * outer_len + jnp.arange(
        outer_len, dtype=jnp.int32
    )[None, :]
    turn_angle = ((lane_pos * q_index) % range_len).astype(jnp.float32) * (
        -2.0 * math.pi / range_len
    )
    turn_real = jnp.cos(turn_angle)[:, None, :]
    turn_imag = jnp.sin(turn_angle)[:, None, :]
    second = jnp.stack(
        [
            second[:, 0] * turn_real - second[:, 1] * turn_imag,
            second[:, 0] * turn_imag + second[:, 1] * turn_real,
        ],
        axis=1,
    )
    if block_len % outer_len == 0:
        per_block = block_len // outer_len
        return second.reshape(device_count, per_block, 2, rows, outer_len)
    second = jnp.transpose(second, (1, 2, 0, 3)).reshape(2, rows, device_count, block_len)
    return jnp.transpose(second, (2, 0, 1, 3))[:, None]


def azimuth_matrix(row_list, scale):
    total_rows = row_list.shape[0]
    pulse_index = jnp.arange(total_rows, dtype=jnp.int32)
    select = (row_list[:, None] == pulse_index[None, :]).astype(jnp.float32)
    dft_real, dft_imag = dft_table(total_rows, scale)
    fold_real = jnp.einsum("ji,ja->ai", select, dft_real, precision=highest)
    fold_imag = jnp.einsum("ji,ja->ai", select, dft_imag, precision=highest)
    top = jnp.concatenate([fold_real, -fold_imag], axis=1)
    bottom = jnp.concatenate([fold_imag, fold_real], axis=1)
    return top, bottom


def on_device(echoes, row_list, wavenumber, az_wavenumber, stolt_offset, stolt_coef):
    rows_here = echoes.shape[1]
    span_len = echoes.shape[2]
    lane_count = lax.axis_size("rng")
    pulse_count = lax.axis_size("pulse")
    device_count = pulse_count * lane_count
    total_rows = row_list.shape[0]
    range_len = span_len * lane_count
    block_len = span_len // device_count
    position = lax.axis_index(("pulse", "rng"))
    lane_pos = lax.axis_index("rng")

    spectrum = range_dft_blocks(echoes, device_count, block_len, lane_pos, range_len)
    pieces = spectrum.shape[1]
    spectrum = spectrum.reshape(device_count, pieces * 2 * rows_here, block_len // pieces)
    spectrum = lax.all_to_all(
        spectrum, ("pulse", "rng"), split_axis=0, concat_axis=0, tiled=True
    )
    spectrum = spectrum.reshape(pulse_count, lane_count, pieces, 2, rows_here, block_len // pieces)
    spectrum = jnp.transpose(spectrum, (0, 1, 3, 4, 2, 5)).reshape(
        pulse_count, lane_count, 2, rows_here, block_len
    )

    lane_real = spectrum[:, :, 0]
    lane_imag = spectrum[:, :, 1]
    combined_real = []
    combined_imag = []
    for s in range(lane_count):
        acc_real = 0.0
        acc_imag = 0.0
        for r in range(lane_count):
            turn = -2.0 * math.pi * ((r * s) % lane_count) / lane_count
            wr = round(math.cos(turn), 12)
            wi = round(math.sin(turn), 12)
            if wr != 0.0:
                acc_real = acc_real + wr * lane_real[:, r]
                acc_imag = acc_imag + wr * lane_imag[:, r]
            if wi != 0.0:
                acc_real = acc_real - wi * lane_imag[:, r]
                acc_imag = acc_imag + wi * lane_real[:, r]
        combined_real.append(acc_real)
        combined_imag.append(acc_imag)
    combined = jnp.stack([jnp.stack(combined_real), jnp.stack(combined_imag)], axis=1)
    combined = combined.reshape(lane_count, 2 * total_rows, block_len)

    axes = ("pulse", "rng")
    up = [(i, (i + 1) % device_count) for i in range(device_count)]
    down = [(j, i) for i, j in up]

    def beside(left_piece, right_piece, axis):
        left = lax.ppermute(left_piece, axes, up)
        right = lax.ppermute(right_piece, axes, down)
        left = jnp.where(position == 0, jnp.roll(left, 1, axis=axis), left)
        right = jnp.where(position == device_count - 1, jnp.roll(right, -1, axis=axis), right)
        return left, right

    wave_left, wave_right = beside(wavenumber[:, block_len - RIM:], wavenumber[:, :RIM], 0)
    rim_left, rim_right = beside(
        jnp.swapaxes(combined[:, :, block_len - RIM:], 1, 2),
        jnp.swapaxes(combined[:, :, :RIM], 1, 2),
        0,
    )

    fold_top, fold_bottom = azimuth_matrix(row_list, 1.0 / math.sqrt(range_len * total_rows))

    def focus(az_real, az_imag, wave):
        phase_angle = phase_scale * jnp.sqrt(
            wave[:, :, None] ** 2 - az_wavenumber[None, None, :] ** 2
        )
        phase_real = jnp.cos(phase_angle)
        phase_imag = jnp.sin(phase_angle)
        return jnp.stack(
            [
                az_real * phase_real - az_imag * phase_imag,
                az_real * phase_imag + az_imag * phase_real,
            ]
        )

    az_real = jnp.einsum("ay,syq->sqa", fold_top, combined, precision=fast)
    az_imag = jnp.einsum("ay,syq->sqa", fold_bottom, combined, precision=fast)
    phase_angle = phase_scale * jnp.sqrt(
        wavenumber[:, :, None] ** 2 - az_wavenumber[None, None, :] ** 2
    )
    phase_real, phase_imag = lax.optimization_barrier(
        (jnp.cos(phase_angle), jnp.sin(phase_angle))
    )
    focused = jnp.stack(
        [
            az_real * phase_real - az_imag * phase_imag,
            az_real * phase_imag + az_imag * phase_real,
        ]
    )

    rims = jnp.concatenate([rim_left, rim_right], axis=1)
    rim_real = jnp.einsum("ay,sjy->sja", fold_top, rims, precision=fast)
    rim_imag = jnp.einsum("ay,sjy->sja", fold_bottom, rims, precision=fast)
    rims = focus(rim_real, rim_imag, jnp.concatenate([wave_left, wave_right], axis=1))
    widened = jnp.concatenate([focused, rims], axis=2)

    tap_count = stolt_coef.shape[0]
    piece_index = jnp.arange(block_len, dtype=jnp.int32)
    q_global = position * block_len + piece_index
    bin_index = jnp.arange(lane_count, dtype=jnp.int32)[:, None] * span_len + q_global[None, :]
    relative = stolt_offset - bin_index + RIM
    tap_index = jnp.arange(tap_count, dtype=jnp.int32)
    source = stolt_offset[None, :, :] + tap_index[:, None, None]
    inside = (source >= 0) & (source < range_len)
    weights = jnp.where(inside, stolt_coef, 0.0)
    columns = jnp.arange(block_len + 2 * RIM, dtype=jnp.int32)
    target = piece_index[:, None] + relative[:, :, None]
    band = jnp.zeros((lane_count, block_len, block_len + 2 * RIM), jnp.float32)
    for t in range(tap_count):
        band = band + jnp.where(columns[None, None, :] == target + t, weights[t][:, :, None], 0.0)

    band = jnp.concatenate(
        [band[:, :, RIM:RIM + block_len], band[:, :, :RIM], band[:, :, RIM + block_len:]], axis=2
    )
    return jnp.einsum("sij,csja->csia", band, widened, precision=fast)


def solution(mesh):
    in_specs = (
        P(None, "pulse", "rng"),
        P(),
        P(None, ("pulse", "rng")),
        P(),
        P(None, ("pulse", "rng")),
        P(None, None, ("pulse", "rng")),
    )
    out_specs = P(None, None, ("pulse", "rng"), None)
    return jax.shard_map(
        on_device, mesh=mesh, in_specs=in_specs, out_specs=out_specs, check_vma=False
    )
```

```python
import math

import jax
import jax.numpy as jnp
from jax import lax
from jax.sharding import PartitionSpec as P

phase_scale = 24.0
highest = lax.Precision.HIGHEST
fast = lax.Precision.HIGH
RIM = 8


def split_factor(length):
    outer_len = 1
    while length % (outer_len * 2) == 0 and outer_len * 2 * (outer_len * 2) <= length:
        outer_len = outer_len * 2
    return outer_len


def dft_table(length, factor):
    index_range = jnp.arange(length, dtype=jnp.int32)
    product = index_range[:, None] * index_range[None, :] % length
    twist_angle = product.astype(jnp.float32) * (-2.0 * math.pi / length)
    return (jnp.cos(twist_angle) * factor, jnp.sin(twist_angle) * factor)


def complex_einsum(pattern, real_part, imag_part, table_real, table_imag):

    def contract(operand, matrix):
        return jnp.einsum(pattern, operand, matrix, precision=fast)

    return (
        contract(real_part, table_real) - contract(imag_part, table_imag),
        contract(real_part, table_imag) + contract(imag_part, table_real),
    )


def last_axis_dft(real_part, imag_part, length, factor):
    inner_len = split_factor(length)
    outer_len = length // inner_len
    leading = real_part.shape[:-1]
    real_part = real_part.reshape(leading + (outer_len, inner_len))
    imag_part = imag_part.reshape(leading + (outer_len, inner_len))
    outer_real, outer_imag = dft_table(outer_len, 1.0)
    real_part, imag_part = complex_einsum(
        "...ba,ub->...ua", real_part, imag_part, outer_real, outer_imag
    )
    col_index = jnp.arange(outer_len, dtype=jnp.int32)[:, None]
    row_index = jnp.arange(inner_len, dtype=jnp.int32)[None, :]
    twist_angle = (col_index * row_index % length).astype(jnp.float32) * (-2.0 * math.pi / length)
    twist_real = jnp.cos(twist_angle)
    twist_imag = jnp.sin(twist_angle)
    real_part, imag_part = (
        real_part * twist_real - imag_part * twist_imag,
        real_part * twist_imag + imag_part * twist_real,
    )
    inner_real, inner_imag = dft_table(inner_len, factor)
    real_part, imag_part = complex_einsum(
        "...ua,va->...vu", real_part, imag_part, inner_real, inner_imag
    )
    return (real_part.reshape(leading + (length,)), imag_part.reshape(leading + (length,)))


def stacked_table(length, factor):
    table_real, table_imag = dft_table(length, factor)
    top = jnp.stack([table_real, -table_imag], axis=1)
    bottom = jnp.stack([table_imag, table_real], axis=1)
    return jnp.stack([top, bottom])


def range_dft_blocks(pair, device_count, block_len, lane_pos, range_len):
    rows = pair.shape[1]
    length = pair.shape[2]
    inner_len = split_factor(length)
    outer_len = length // inner_len
    signal = pair.reshape(2, rows, outer_len, inner_len)
    first = jnp.einsum("ducb,crba->drua", stacked_table(outer_len, 1.0), signal, precision=fast)
    col_index = jnp.arange(outer_len, dtype=jnp.int32)[:, None]
    row_index = jnp.arange(inner_len, dtype=jnp.int32)[None, :]
    twist_angle = (col_index * row_index % length).astype(jnp.float32) * (-2.0 * math.pi / length)
    twist_real = jnp.cos(twist_angle)
    twist_imag = jnp.sin(twist_angle)
    first = jnp.stack(
        [
            first[0] * twist_real - first[1] * twist_imag,
            first[0] * twist_imag + first[1] * twist_real,
        ]
    )
    second = jnp.einsum("dvca,crua->vdru", stacked_table(inner_len, 1.0), first, precision=fast)
    if block_len % outer_len == 0:
        per_block = block_len // outer_len
        return second.reshape(device_count, per_block, 2, rows, outer_len)
    second = jnp.transpose(second, (1, 2, 0, 3)).reshape(2, rows, device_count, block_len)
    return jnp.transpose(second, (2, 0, 1, 3))[:, None]


def azimuth_matrix(row_list, scale):
    total_rows = row_list.shape[0]
    pulse_index = jnp.arange(total_rows, dtype=jnp.int32)
    select = (row_list[:, None] == pulse_index[None, :]).astype(jnp.float32)
    dft_real, dft_imag = dft_table(total_rows, scale)
    fold_real = jnp.einsum("ji,ja->ai", select, dft_real, precision=highest)
    fold_imag = jnp.einsum("ji,ja->ai", select, dft_imag, precision=highest)
    top = jnp.concatenate([fold_real, -fold_imag], axis=1)
    bottom = jnp.concatenate([fold_imag, fold_real], axis=1)
    return top, bottom


def on_device(echoes, row_list, wavenumber, az_wavenumber, stolt_offset, stolt_coef):
    rows_here = echoes.shape[1]
    span_len = echoes.shape[2]
    lane_count = lax.axis_size("rng")
    pulse_count = lax.axis_size("pulse")
    device_count = pulse_count * lane_count
    total_rows = row_list.shape[0]
    range_len = span_len * lane_count
    block_len = span_len // device_count
    position = lax.axis_index(("pulse", "rng"))
    lane_pos = lax.axis_index("rng")

    spectrum = range_dft_blocks(echoes, device_count, block_len, lane_pos, range_len)
    pieces = spectrum.shape[1]
    spectrum = spectrum.reshape(device_count, pieces * 2 * rows_here, block_len // pieces)
    spectrum = lax.all_to_all(
        spectrum, ("pulse", "rng"), split_axis=0, concat_axis=0, tiled=True
    )
    spectrum = spectrum.reshape(pulse_count, lane_count, pieces, 2, rows_here, block_len // pieces)
    spectrum = jnp.transpose(spectrum, (0, 1, 3, 4, 2, 5)).reshape(
        pulse_count, lane_count, 2, rows_here, block_len
    )

    q_global = position * block_len + jnp.arange(block_len, dtype=jnp.int32)
    lane_index = jnp.arange(lane_count, dtype=jnp.int32)[:, None]
    turn_angle = ((lane_index * q_global[None, :]) % range_len).astype(jnp.float32) * (
        -2.0 * math.pi / range_len
    )
    turn_real = jnp.cos(turn_angle)[None, :, None, :]
    turn_imag = jnp.sin(turn_angle)[None, :, None, :]
    lane_real = spectrum[:, :, 0] * turn_real - spectrum[:, :, 1] * turn_imag
    lane_imag = spectrum[:, :, 0] * turn_imag + spectrum[:, :, 1] * turn_real
    combined_real = []
    combined_imag = []
    for s in range(lane_count):
        acc_real = 0.0
        acc_imag = 0.0
        for r in range(lane_count):
            turn = -2.0 * math.pi * ((r * s) % lane_count) / lane_count
            wr = round(math.cos(turn), 12)
            wi = round(math.sin(turn), 12)
            if wr != 0.0:
                acc_real = acc_real + wr * lane_real[:, r]
                acc_imag = acc_imag + wr * lane_imag[:, r]
            if wi != 0.0:
                acc_real = acc_real - wi * lane_imag[:, r]
                acc_imag = acc_imag + wi * lane_real[:, r]
        combined_real.append(acc_real)
        combined_imag.append(acc_imag)
    combined = jnp.stack([jnp.stack(combined_real), jnp.stack(combined_imag)], axis=1)
    combined = combined.reshape(lane_count, 2 * total_rows, block_len)

    axes = ("pulse", "rng")
    up = [(i, (i + 1) % device_count) for i in range(device_count)]
    down = [(j, i) for i, j in up]

    def beside(left_piece, right_piece, axis):
        left = lax.ppermute(left_piece, axes, up)
        right = lax.ppermute(right_piece, axes, down)
        left = jnp.where(position == 0, jnp.roll(left, 1, axis=axis), left)
        right = jnp.where(position == device_count - 1, jnp.roll(right, -1, axis=axis), right)
        return left, right

    wave_left, wave_right = beside(wavenumber[:, block_len - RIM:], wavenumber[:, :RIM], 0)
    rim_left, rim_right = beside(
        jnp.swapaxes(combined[:, :, block_len - RIM:], 1, 2),
        jnp.swapaxes(combined[:, :, :RIM], 1, 2),
        0,
    )

    fold_top, fold_bottom = azimuth_matrix(row_list, 1.0 / math.sqrt(range_len * total_rows))

    def focus(az_real, az_imag, wave):
        phase_angle = phase_scale * jnp.sqrt(
            wave[:, :, None] ** 2 - az_wavenumber[None, None, :] ** 2
        )
        phase_real = jnp.cos(phase_angle)
        phase_imag = jnp.sin(phase_angle)
        return jnp.stack(
            [
                az_real * phase_real - az_imag * phase_imag,
                az_real * phase_imag + az_imag * phase_real,
            ]
        )

    az_real = jnp.einsum("ay,syq->sqa", fold_top, combined, precision=fast)
    az_imag = jnp.einsum("ay,syq->sqa", fold_bottom, combined, precision=fast)
    phase_angle = phase_scale * jnp.sqrt(
        wavenumber[:, :, None] ** 2 - az_wavenumber[None, None, :] ** 2
    )
    phase_real, phase_imag = lax.optimization_barrier(
        (jnp.cos(phase_angle), jnp.sin(phase_angle))
    )
    focused = jnp.stack(
        [
            az_real * phase_real - az_imag * phase_imag,
            az_real * phase_imag + az_imag * phase_real,
        ]
    )

    rims = jnp.concatenate([rim_left, rim_right], axis=1)
    rim_real = jnp.einsum("ay,sjy->sja", fold_top, rims, precision=fast)
    rim_imag = jnp.einsum("ay,sjy->sja", fold_bottom, rims, precision=fast)
    rims = focus(rim_real, rim_imag, jnp.concatenate([wave_left, wave_right], axis=1))
    widened = jnp.concatenate([focused, rims], axis=2)

    tap_count = stolt_coef.shape[0]
    piece_index = jnp.arange(block_len, dtype=jnp.int32)
    q_global = position * block_len + piece_index
    bin_index = jnp.arange(lane_count, dtype=jnp.int32)[:, None] * span_len + q_global[None, :]
    relative = stolt_offset - bin_index + RIM
    tap_index = jnp.arange(tap_count, dtype=jnp.int32)
    source = stolt_offset[None, :, :] + tap_index[:, None, None]
    inside = (source >= 0) & (source < range_len)
    weights = jnp.where(inside, stolt_coef, 0.0)
    columns = jnp.arange(block_len + 2 * RIM, dtype=jnp.int32)
    target = piece_index[:, None] + relative[:, :, None]
    band = jnp.zeros((lane_count, block_len, block_len + 2 * RIM), jnp.float32)
    for t in range(tap_count):
        band = band + jnp.where(columns[None, None, :] == target + t, weights[t][:, :, None], 0.0)

    band = jnp.concatenate(
        [band[:, :, RIM:RIM + block_len], band[:, :, :RIM], band[:, :, RIM + block_len:]], axis=2
    )
    return jnp.einsum("sij,csja->csia", band, widened, precision=fast)


def solution(mesh):
    in_specs = (
        P(None, "pulse", "rng"),
        P(),
        P(None, ("pulse", "rng")),
        P(),
        P(None, ("pulse", "rng")),
        P(None, None, ("pulse", "rng")),
    )
    out_specs = P(None, None, ("pulse", "rng"), None)
    return jax.shard_map(
        on_device, mesh=mesh, in_specs=in_specs, out_specs=out_specs, check_vma=False
    )
```

```python
import math

import jax
import jax.numpy as jnp
from jax import lax
from jax.sharding import PartitionSpec as P

phase_scale = 24.0
highest = lax.Precision.HIGHEST
fast = lax.Precision.HIGH
RIM = 8


def split_factor(length):
    outer_len = 1
    while length % (outer_len * 2) == 0 and outer_len * 2 * (outer_len * 2) <= length:
        outer_len = outer_len * 2
    return outer_len


def dft_table(length, factor):
    index_range = jnp.arange(length, dtype=jnp.int32)
    product = index_range[:, None] * index_range[None, :] % length
    twist_angle = product.astype(jnp.float32) * (-2.0 * math.pi / length)
    return (jnp.cos(twist_angle) * factor, jnp.sin(twist_angle) * factor)


def complex_einsum(pattern, real_part, imag_part, table_real, table_imag):

    def contract(operand, matrix):
        return jnp.einsum(pattern, operand, matrix, precision=fast)

    return (
        contract(real_part, table_real) - contract(imag_part, table_imag),
        contract(real_part, table_imag) + contract(imag_part, table_real),
    )


def last_axis_dft(real_part, imag_part, length, factor):
    inner_len = split_factor(length)
    outer_len = length // inner_len
    leading = real_part.shape[:-1]
    real_part = real_part.reshape(leading + (outer_len, inner_len))
    imag_part = imag_part.reshape(leading + (outer_len, inner_len))
    outer_real, outer_imag = dft_table(outer_len, 1.0)
    real_part, imag_part = complex_einsum(
        "...ba,ub->...ua", real_part, imag_part, outer_real, outer_imag
    )
    col_index = jnp.arange(outer_len, dtype=jnp.int32)[:, None]
    row_index = jnp.arange(inner_len, dtype=jnp.int32)[None, :]
    twist_angle = (col_index * row_index % length).astype(jnp.float32) * (-2.0 * math.pi / length)
    twist_real = jnp.cos(twist_angle)
    twist_imag = jnp.sin(twist_angle)
    real_part, imag_part = (
        real_part * twist_real - imag_part * twist_imag,
        real_part * twist_imag + imag_part * twist_real,
    )
    inner_real, inner_imag = dft_table(inner_len, factor)
    real_part, imag_part = complex_einsum(
        "...ua,va->...vu", real_part, imag_part, inner_real, inner_imag
    )
    return (real_part.reshape(leading + (length,)), imag_part.reshape(leading + (length,)))


def stacked_table(length, factor):
    table_real, table_imag = dft_table(length, factor)
    top = jnp.stack([table_real, -table_imag], axis=1)
    bottom = jnp.stack([table_imag, table_real], axis=1)
    return jnp.stack([top, bottom])


def range_dft_blocks(pair, device_count, block_len, lane_pos, range_len):
    rows = pair.shape[1]
    length = pair.shape[2]
    inner_len = split_factor(length)
    outer_len = length // inner_len
    signal = pair.reshape(2, rows, outer_len, inner_len)
    first = jnp.einsum("ducb,crba->drua", stacked_table(outer_len, 1.0), signal, precision=fast)
    col_index = jnp.arange(outer_len, dtype=jnp.int32)[:, None]
    row_index = jnp.arange(inner_len, dtype=jnp.int32)[None, :]
    twist_angle = (col_index * row_index % length).astype(jnp.float32) * (-2.0 * math.pi / length)
    twist_real = jnp.cos(twist_angle)
    twist_imag = jnp.sin(twist_angle)
    first = jnp.stack(
        [
            first[0] * twist_real - first[1] * twist_imag,
            first[0] * twist_imag + first[1] * twist_real,
        ]
    )
    second = jnp.einsum("dvca,crua->vdru", stacked_table(inner_len, 1.0), first, precision=fast)
    q_index = jnp.arange(inner_len, dtype=jnp.int32)[:, None] * outer_len + jnp.arange(
        outer_len, dtype=jnp.int32
    )[None, :]
    turn_angle = ((lane_pos * q_index) % range_len).astype(jnp.float32) * (
        -2.0 * math.pi / range_len
    )
    turn_real = jnp.cos(turn_angle)[:, None, :]
    turn_imag = jnp.sin(turn_angle)[:, None, :]
    second = jnp.stack(
        [
            second[:, 0] * turn_real - second[:, 1] * turn_imag,
            second[:, 0] * turn_imag + second[:, 1] * turn_real,
        ],
        axis=1,
    )
    if block_len % outer_len == 0:
        per_block = block_len // outer_len
        return second.reshape(device_count, per_block, 2, rows, outer_len)
    second = jnp.transpose(second, (1, 2, 0, 3)).reshape(2, rows, device_count, block_len)
    return jnp.transpose(second, (2, 0, 1, 3))[:, None]


def azimuth_matrix(row_list, scale):
    total_rows = row_list.shape[0]
    pulse_index = jnp.arange(total_rows, dtype=jnp.int32)
    select = (row_list[:, None] == pulse_index[None, :]).astype(jnp.float32)
    dft_real, dft_imag = dft_table(total_rows, scale)
    fold_real = jnp.einsum("ji,ja->ai", select, dft_real, precision=highest)
    fold_imag = jnp.einsum("ji,ja->ai", select, dft_imag, precision=highest)
    top = jnp.concatenate([fold_real, -fold_imag], axis=1)
    bottom = jnp.concatenate([fold_imag, fold_real], axis=1)
    return top, bottom


def on_device(echoes, row_list, wavenumber, az_wavenumber, stolt_offset, stolt_coef):
    rows_here = echoes.shape[1]
    span_len = echoes.shape[2]
    lane_count = lax.axis_size("rng")
    pulse_count = lax.axis_size("pulse")
    device_count = pulse_count * lane_count
    total_rows = row_list.shape[0]
    range_len = span_len * lane_count
    block_len = span_len // device_count
    position = lax.axis_index(("pulse", "rng"))
    lane_pos = lax.axis_index("rng")

    spectrum = range_dft_blocks(echoes, device_count, block_len, lane_pos, range_len)
    pieces = spectrum.shape[1]
    spectrum = spectrum.reshape(device_count, pieces * 2 * rows_here, block_len // pieces)
    spectrum = lax.all_to_all(
        spectrum, ("pulse", "rng"), split_axis=0, concat_axis=0, tiled=True
    )
    spectrum = spectrum.reshape(pulse_count, lane_count, pieces, 2, rows_here, block_len // pieces)
    spectrum = jnp.transpose(spectrum, (0, 1, 3, 4, 2, 5)).reshape(
        pulse_count, lane_count, 2, rows_here, block_len
    )

    lane_real = spectrum[:, :, 0]
    lane_imag = spectrum[:, :, 1]
    combined_real = []
    combined_imag = []
    for s in range(lane_count):
        acc_real = 0.0
        acc_imag = 0.0
        for r in range(lane_count):
            turn = -2.0 * math.pi * ((r * s) % lane_count) / lane_count
            wr = round(math.cos(turn), 12)
            wi = round(math.sin(turn), 12)
            if wr != 0.0:
                acc_real = acc_real + wr * lane_real[:, r]
                acc_imag = acc_imag + wr * lane_imag[:, r]
            if wi != 0.0:
                acc_real = acc_real - wi * lane_imag[:, r]
                acc_imag = acc_imag + wi * lane_real[:, r]
        combined_real.append(acc_real)
        combined_imag.append(acc_imag)
    combined = jnp.stack([jnp.stack(combined_real), jnp.stack(combined_imag)], axis=1)
    combined = combined.reshape(lane_count, 2 * total_rows, block_len)

    axes = ("pulse", "rng")
    up = [(i, (i + 1) % device_count) for i in range(device_count)]
    down = [(j, i) for i, j in up]

    def beside(left_piece, right_piece, axis):
        left = lax.ppermute(left_piece, axes, up)
        right = lax.ppermute(right_piece, axes, down)
        left = jnp.where(position == 0, jnp.roll(left, 1, axis=axis), left)
        right = jnp.where(position == device_count - 1, jnp.roll(right, -1, axis=axis), right)
        return left, right

    wave_left, wave_right = beside(wavenumber[:, block_len - RIM:], wavenumber[:, :RIM], 0)
    rim_left, rim_right = beside(
        jnp.swapaxes(combined[:, :, block_len - RIM:], 1, 2),
        jnp.swapaxes(combined[:, :, :RIM], 1, 2),
        0,
    )

    fold_top, fold_bottom = azimuth_matrix(row_list, 1.0 / math.sqrt(range_len * total_rows))

    def focus(az_real, az_imag, wave):
        phase_angle = phase_scale * jnp.sqrt(
            wave[:, :, None] ** 2 - az_wavenumber[None, None, :] ** 2
        )
        phase_real = jnp.cos(phase_angle)
        phase_imag = jnp.sin(phase_angle)
        return jnp.stack(
            [
                az_real * phase_real - az_imag * phase_imag,
                az_real * phase_imag + az_imag * phase_real,
            ]
        )

    fold_both = jnp.concatenate([fold_top, fold_bottom], axis=0)
    az_both = jnp.einsum("xy,syq->sqx", fold_both, combined, precision=fast)
    az_real = az_both[..., :total_rows]
    az_imag = az_both[..., total_rows:]
    phase_angle = phase_scale * jnp.sqrt(
        wavenumber[:, :, None] ** 2 - az_wavenumber[None, None, :] ** 2
    )
    phase_real, phase_imag = lax.optimization_barrier(
        (jnp.cos(phase_angle), jnp.sin(phase_angle))
    )
    focused = jnp.stack(
        [
            az_real * phase_real - az_imag * phase_imag,
            az_real * phase_imag + az_imag * phase_real,
        ]
    )

    rims = jnp.concatenate([rim_left, rim_right], axis=1)
    rim_real = jnp.einsum("ay,sjy->sja", fold_top, rims, precision=fast)
    rim_imag = jnp.einsum("ay,sjy->sja", fold_bottom, rims, precision=fast)
    rims = focus(rim_real, rim_imag, jnp.concatenate([wave_left, wave_right], axis=1))
    widened = jnp.concatenate([focused, rims], axis=2)

    tap_count = stolt_coef.shape[0]
    piece_index = jnp.arange(block_len, dtype=jnp.int32)
    q_global = position * block_len + piece_index
    bin_index = jnp.arange(lane_count, dtype=jnp.int32)[:, None] * span_len + q_global[None, :]
    relative = stolt_offset - bin_index + RIM
    tap_index = jnp.arange(tap_count, dtype=jnp.int32)
    source = stolt_offset[None, :, :] + tap_index[:, None, None]
    inside = (source >= 0) & (source < range_len)
    weights = jnp.where(inside, stolt_coef, 0.0)
    columns = jnp.arange(block_len + 2 * RIM, dtype=jnp.int32)
    target = piece_index[:, None] + relative[:, :, None]
    band = jnp.zeros((lane_count, block_len, block_len + 2 * RIM), jnp.float32)
    for t in range(tap_count):
        band = band + jnp.where(columns[None, None, :] == target + t, weights[t][:, :, None], 0.0)

    band = jnp.concatenate(
        [band[:, :, RIM:RIM + block_len], band[:, :, :RIM], band[:, :, RIM + block_len:]], axis=2
    )
    return jnp.einsum("sij,csja->csia", band, widened, precision=fast)


def solution(mesh):
    in_specs = (
        P(None, "pulse", "rng"),
        P(),
        P(None, ("pulse", "rng")),
        P(),
        P(None, ("pulse", "rng")),
        P(None, None, ("pulse", "rng")),
    )
    out_specs = P(None, None, ("pulse", "rng"), None)
    return jax.shard_map(
        on_device, mesh=mesh, in_specs=in_specs, out_specs=out_specs, check_vma=False
    )
```

```python
import math

import jax
import jax.numpy as jnp
from jax import lax
from jax.sharding import PartitionSpec as P

phase_scale = 24.0
highest = lax.Precision.HIGHEST
fast = lax.Precision.HIGH
RIM = 8


def split_factor(length):
    outer_len = 1
    while length % (outer_len * 2) == 0 and outer_len * 2 * (outer_len * 2) <= length:
        outer_len = outer_len * 2
    return outer_len


def dft_table(length, factor):
    index_range = jnp.arange(length, dtype=jnp.int32)
    product = index_range[:, None] * index_range[None, :] % length
    twist_angle = product.astype(jnp.float32) * (-2.0 * math.pi / length)
    return (jnp.cos(twist_angle) * factor, jnp.sin(twist_angle) * factor)


def complex_einsum(pattern, real_part, imag_part, table_real, table_imag):

    def contract(operand, matrix):
        return jnp.einsum(pattern, operand, matrix, precision=fast)

    return (
        contract(real_part, table_real) - contract(imag_part, table_imag),
        contract(real_part, table_imag) + contract(imag_part, table_real),
    )


def last_axis_dft(real_part, imag_part, length, factor):
    inner_len = split_factor(length)
    outer_len = length // inner_len
    leading = real_part.shape[:-1]
    real_part = real_part.reshape(leading + (outer_len, inner_len))
    imag_part = imag_part.reshape(leading + (outer_len, inner_len))
    outer_real, outer_imag = dft_table(outer_len, 1.0)
    real_part, imag_part = complex_einsum(
        "...ba,ub->...ua", real_part, imag_part, outer_real, outer_imag
    )
    col_index = jnp.arange(outer_len, dtype=jnp.int32)[:, None]
    row_index = jnp.arange(inner_len, dtype=jnp.int32)[None, :]
    twist_angle = (col_index * row_index % length).astype(jnp.float32) * (-2.0 * math.pi / length)
    twist_real = jnp.cos(twist_angle)
    twist_imag = jnp.sin(twist_angle)
    real_part, imag_part = (
        real_part * twist_real - imag_part * twist_imag,
        real_part * twist_imag + imag_part * twist_real,
    )
    inner_real, inner_imag = dft_table(inner_len, factor)
    real_part, imag_part = complex_einsum(
        "...ua,va->...vu", real_part, imag_part, inner_real, inner_imag
    )
    return (real_part.reshape(leading + (length,)), imag_part.reshape(leading + (length,)))


def stacked_table(length, factor):
    table_real, table_imag = dft_table(length, factor)
    top = jnp.stack([table_real, -table_imag], axis=1)
    bottom = jnp.stack([table_imag, table_real], axis=1)
    return jnp.stack([top, bottom])


def range_dft_blocks(pair, device_count, block_len, lane_pos, range_len):
    rows = pair.shape[1]
    length = pair.shape[2]
    inner_len = split_factor(length)
    outer_len = length // inner_len
    signal = pair.reshape(2, rows, outer_len, inner_len)
    first = jnp.einsum("ducb,crba->drua", stacked_table(outer_len, 1.0), signal, precision=fast)
    col_index = jnp.arange(outer_len, dtype=jnp.int32)[:, None]
    row_index = jnp.arange(inner_len, dtype=jnp.int32)[None, :]
    twist_angle = (col_index * row_index % length).astype(jnp.float32) * (-2.0 * math.pi / length)
    twist_real = jnp.cos(twist_angle)
    twist_imag = jnp.sin(twist_angle)
    first = jnp.stack(
        [
            first[0] * twist_real - first[1] * twist_imag,
            first[0] * twist_imag + first[1] * twist_real,
        ]
    )
    second = jnp.einsum("dvca,crua->vdru", stacked_table(inner_len, 1.0), first, precision=fast)
    q_index = jnp.arange(inner_len, dtype=jnp.int32)[:, None] * outer_len + jnp.arange(
        outer_len, dtype=jnp.int32
    )[None, :]
    turn_angle = ((lane_pos * q_index) % range_len).astype(jnp.float32) * (
        -2.0 * math.pi / range_len
    )
    turn_real = jnp.cos(turn_angle)[:, None, :]
    turn_imag = jnp.sin(turn_angle)[:, None, :]
    second = jnp.stack(
        [
            second[:, 0] * turn_real - second[:, 1] * turn_imag,
            second[:, 0] * turn_imag + second[:, 1] * turn_real,
        ],
        axis=1,
    )
    if block_len % outer_len == 0:
        per_block = block_len // outer_len
        return second.reshape(device_count, per_block, 2, rows, outer_len)
    second = jnp.transpose(second, (1, 2, 0, 3)).reshape(2, rows, device_count, block_len)
    return jnp.transpose(second, (2, 0, 1, 3))[:, None]


def azimuth_matrix(row_list, scale):
    total_rows = row_list.shape[0]
    pulse_index = jnp.arange(total_rows, dtype=jnp.int32)
    select = (row_list[:, None] == pulse_index[None, :]).astype(jnp.float32)
    dft_real, dft_imag = dft_table(total_rows, scale)
    fold_real = jnp.einsum("ji,ja->ai", select, dft_real, precision=highest)
    fold_imag = jnp.einsum("ji,ja->ai", select, dft_imag, precision=highest)
    top = jnp.concatenate([fold_real, -fold_imag], axis=1)
    bottom = jnp.concatenate([fold_imag, fold_real], axis=1)
    return top, bottom


def on_device(echoes, row_list, wavenumber, az_wavenumber, stolt_offset, stolt_coef):
    rows_here = echoes.shape[1]
    span_len = echoes.shape[2]
    lane_count = lax.axis_size("rng")
    pulse_count = lax.axis_size("pulse")
    device_count = pulse_count * lane_count
    total_rows = row_list.shape[0]
    range_len = span_len * lane_count
    block_len = span_len // device_count
    position = lax.axis_index(("pulse", "rng"))
    lane_pos = lax.axis_index("rng")

    spectrum = range_dft_blocks(echoes, device_count, block_len, lane_pos, range_len)
    pieces = spectrum.shape[1]
    spectrum = spectrum.reshape(device_count, pieces * 2 * rows_here, block_len // pieces)
    spectrum = lax.all_to_all(
        spectrum, ("pulse", "rng"), split_axis=0, concat_axis=0, tiled=True
    )
    spectrum = spectrum.reshape(pulse_count, lane_count, pieces, 2, rows_here, block_len // pieces)
    spectrum = jnp.transpose(spectrum, (0, 1, 3, 4, 2, 5)).reshape(
        pulse_count, lane_count, 2, rows_here, block_len
    )

    lane_real = spectrum[:, :, 0]
    lane_imag = spectrum[:, :, 1]
    combined_real = []
    combined_imag = []
    for s in range(lane_count):
        acc_real = 0.0
        acc_imag = 0.0
        for r in range(lane_count):
            turn = -2.0 * math.pi * ((r * s) % lane_count) / lane_count
            wr = round(math.cos(turn), 12)
            wi = round(math.sin(turn), 12)
            if wr != 0.0:
                acc_real = acc_real + wr * lane_real[:, r]
                acc_imag = acc_imag + wr * lane_imag[:, r]
            if wi != 0.0:
                acc_real = acc_real - wi * lane_imag[:, r]
                acc_imag = acc_imag + wi * lane_real[:, r]
        combined_real.append(acc_real)
        combined_imag.append(acc_imag)
    combined = jnp.stack([jnp.stack(combined_real), jnp.stack(combined_imag)], axis=1)
    combined = combined.reshape(lane_count, 2 * total_rows, block_len)

    axes = ("pulse", "rng")
    up = [(i, (i + 1) % device_count) for i in range(device_count)]
    down = [(j, i) for i, j in up]

    def beside(left_piece, right_piece, axis):
        left = lax.ppermute(left_piece, axes, up)
        right = lax.ppermute(right_piece, axes, down)
        left = jnp.where(position == 0, jnp.roll(left, 1, axis=axis), left)
        right = jnp.where(position == device_count - 1, jnp.roll(right, -1, axis=axis), right)
        return left, right

    wave_left, wave_right = beside(wavenumber[:, block_len - RIM:], wavenumber[:, :RIM], 0)
    rim_left, rim_right = beside(
        jnp.swapaxes(combined[:, :, block_len - RIM:], 1, 2),
        jnp.swapaxes(combined[:, :, :RIM], 1, 2),
        0,
    )

    fold_top, fold_bottom = azimuth_matrix(row_list, 1.0 / math.sqrt(range_len * total_rows))

    def focus(az_real, az_imag, wave):
        phase_angle = phase_scale * jnp.sqrt(
            wave[:, :, None] ** 2 - az_wavenumber[None, None, :] ** 2
        )
        phase_real = jnp.cos(phase_angle)
        phase_imag = jnp.sin(phase_angle)
        return jnp.stack(
            [
                az_real * phase_real - az_imag * phase_imag,
                az_real * phase_imag + az_imag * phase_real,
            ]
        )

    fold_both = jnp.concatenate([fold_top, fold_bottom], axis=0)
    az_both = jnp.einsum("xy,syq->sqx", fold_both, combined, precision=fast)
    az_real = az_both[..., :total_rows]
    az_imag = az_both[..., total_rows:]
    phase_angle = phase_scale * jnp.sqrt(
        wavenumber[:, :, None] ** 2 - az_wavenumber[None, None, :] ** 2
    )
    phase_real, phase_imag = lax.optimization_barrier(
        (jnp.cos(phase_angle), jnp.sin(phase_angle))
    )
    focused = jnp.stack(
        [
            az_real * phase_real - az_imag * phase_imag,
            az_real * phase_imag + az_imag * phase_real,
        ]
    )

    rims = jnp.concatenate([rim_left, rim_right], axis=1)
    rim_both = jnp.einsum("xy,sjy->sjx", fold_both, rims, precision=fast)
    rim_real = rim_both[..., :total_rows]
    rim_imag = rim_both[..., total_rows:]
    rims = focus(rim_real, rim_imag, jnp.concatenate([wave_left, wave_right], axis=1))
    widened = jnp.concatenate([focused, rims], axis=2)

    tap_count = stolt_coef.shape[0]
    piece_index = jnp.arange(block_len, dtype=jnp.int32)
    q_global = position * block_len + piece_index
    bin_index = jnp.arange(lane_count, dtype=jnp.int32)[:, None] * span_len + q_global[None, :]
    relative = stolt_offset - bin_index + RIM
    tap_index = jnp.arange(tap_count, dtype=jnp.int32)
    source = stolt_offset[None, :, :] + tap_index[:, None, None]
    inside = (source >= 0) & (source < range_len)
    weights = jnp.where(inside, stolt_coef, 0.0)
    columns = jnp.arange(block_len + 2 * RIM, dtype=jnp.int32)
    target = piece_index[:, None] + relative[:, :, None]
    band = jnp.zeros((lane_count, block_len, block_len + 2 * RIM), jnp.float32)
    for t in range(tap_count):
        band = band + jnp.where(columns[None, None, :] == target + t, weights[t][:, :, None], 0.0)

    band = jnp.concatenate(
        [band[:, :, RIM:RIM + block_len], band[:, :, :RIM], band[:, :, RIM + block_len:]], axis=2
    )
    return jnp.einsum("sij,csja->csia", band, widened, precision=fast)


def solution(mesh):
    in_specs = (
        P(None, "pulse", "rng"),
        P(),
        P(None, ("pulse", "rng")),
        P(),
        P(None, ("pulse", "rng")),
        P(None, None, ("pulse", "rng")),
    )
    out_specs = P(None, None, ("pulse", "rng"), None)
    return jax.shard_map(
        on_device, mesh=mesh, in_specs=in_specs, out_specs=out_specs, check_vma=False
    )
```
